32 devices in a mesh: groups: 2 (over y), dom: 4 (over z), cols: 4 (over x, core).
Axes of the slice: x: 2, y: 2, z: 4, core: 2. Of those that a mesh axis runs over, the one named last changes fastest.
Arguments:
- features: bfloat16 [32768, 768], P(('groups', 'dom'), 'cols'), parts along dimension 0, may hold values from -6 to 6
- edge_source: int32 [8, 4, 1024], P(('groups', 'dom')), parts along dimension 0, may hold values from 0 to 4095, as said below
- edge_target: int32 [8, 4, 1024], P(('groups', 'dom')), parts along dimension 0, may hold values from 0 to 1024, as said below
- neigh_weight: bfloat16 [768, 1024], P('cols'), may hold values from -0.21875 to 0.21875
- self_weight: bfloat16 [768, 1024], P('cols'), may hold values from -0.21875 to 0.21875
- bias_one: float32 [1024], replicated, may hold values from -3 to 3
- upper_weight: bfloat16 [1024, 1024], P('cols'), may hold values from -0.375 to 0.375
- bias_two: float32 [1024], replicated, may hold values from -3 to 3
- upper_neighbours: int32 [8192, 15], P(('groups', 'dom', 'cols')), parts along dimension 0, may hold values from 0 to 255
- out_cotangent: bfloat16 [8192, 1024], P(('groups', 'dom', 'cols')), parts along dimension 0, may hold values from -6 to 6
Outputs:
- hidden_two: bfloat16 [8192, 1024], P(('groups', 'dom', 'cols')), parts along dimension 0
- grad_neigh: float32 [1536, 1024], P(('groups', 'cols'), 'dom'), parts along dimension 0
- grad_self: float32 [1536, 1024], P(('groups', 'cols'), 'dom'), parts along dimension 0
- grad_upper: float32 [2048, 1024], P(('groups', 'cols')), parts along dimension 0
The draws below stay inside these ranges and needn't reach their ends.
There are 2 independent parts, one for each index of `groups`. The reference program is written for one: setup_inputs(seed, part) draws one part's arguments, and reference() takes and returns one part's arrays. A program takes and returns all parts, laid end to end along the dimension named above; an argument that names none is the same for every part. Nothing has to cross between parts.
Inputs may be any that keep to these rules, and one draw needn't show every extreme that they name: `edge_source`: for each pair (s, o) the live slots are the first ones, 1 to 1024 of them, and some pair has all 1024 live; busy owners receive more edges; dead slots hold 0. edge_target[o, s, k] belongs to the same edge as edge_source[s, o, k]; dead slots hold 1024.
All inputs are finite; a program needn't handle non-finite values.
Results may differ from the reference program's by a relative error of at most 0.015.
Values may be sent and summed in bfloat16 or wider, within the bound.
No kernel may reach another device: no remote copies, remote signals or barrier semaphores. Data moves between devices by JAX's collectives and lax.ppermute only.
A program may use at most 128 MiB of HBM per device.

```python
import jax
import jax.numpy as jnp
from jax import lax

FEAT = 768
HIDDEN_SIZE = 1024
FANOUT2 = 15
NODE_DEV = 4096
TGT_DEV = 1024
CAP = 1024
TGT_LOC = 256
NODES = 16384
TARGETS = 4096
N_DOM = 4
N_COLS = 4


def edge_plan(key):
    owner_load = jax.random.randint(jax.random.fold_in(key, 11), (N_DOM,), 1, 5)
    base_count = jax.random.randint(jax.random.fold_in(key, 12), (N_DOM, N_DOM), CAP // 8, CAP // 4 + 1)
    counts = jnp.minimum(base_count * owner_load[None, :], CAP)
    pick_row = jax.random.randint(jax.random.fold_in(key, 13), (), 0, N_DOM)
    pick_col = jax.random.randint(jax.random.fold_in(key, 14), (), 0, N_DOM)
    counts = counts.at[pick_row, pick_col].set(CAP)
    slots = jnp.arange(CAP, dtype=jnp.int32)
    live = slots[None, None, :] < counts[:, :, None]
    sources = jax.random.randint(jax.random.fold_in(key, 15), (N_DOM, N_DOM, CAP), 0, NODE_DEV)
    targets = jax.random.randint(jax.random.fold_in(key, 16), (N_DOM, N_DOM, CAP), 0, TGT_DEV)
    sources = jnp.where(live, sources, 0).astype(jnp.int32)
    targets = jnp.where(live, targets, TGT_DEV).astype(jnp.int32)
    return (sources, targets)


def draw_edge_source(key, part):
    sources, targets = edge_plan(key)
    return sources


def draw_edge_target(key, part):
    sources, targets = edge_plan(key)
    return jnp.transpose(targets, (1, 0, 2))


def touch_ends(entries, own_key, smallest, largest):
    longest = entries.shape.index(max(entries.shape))
    spots = []
    for shift in (0, 1):
        where = [jax.random.randint(jax.random.fold_in(own_key, axis), (), 0, length) for axis, length in enumerate(entries.shape)]
        where[longest] = (where[longest] + shift) % entries.shape[longest]
        spots.append(tuple(where))
    return entries.at[spots[0]].set(smallest).at[spots[1]].set(largest)


def steps_of(rng, shape, shards, least, high):
    gain, own = 1.0, jax.random.fold_in(rng, 6)
    for position, blocks in shards:
        heights = jnp.exp(jax.random.uniform(jax.random.fold_in(own, position), (blocks,), jnp.float32, least / len(shards), high / len(shards)))
        gain = gain * jnp.repeat(heights, shape[position] // blocks).reshape([-1 if axis == position else 1 for axis in range(len(shape))])
    return gain


def gaussian(own_key, extent, scale, bound, pieces=(), held_as=jnp.bfloat16):
    loudness = steps_of(own_key, extent, pieces, -0.22, 0.18) if pieces else 1.0
    array = jax.random.normal(own_key, extent, jnp.float32) * scale * loudness
    return jnp.minimum(jnp.maximum(array, -bound), bound).astype(held_as)


def setup_inputs(seed: int = 0, part: int = 0) -> dict:
    seeds = jax.random.split(jax.random.key(seed), 11)
    part_keys = jax.random.split(jax.random.fold_in(seeds[10], part), 11)
    return {
        "features": gaussian(part_keys[0], (NODES, FEAT), 1.0, 6.0, ((0, 4), (1, 4))),
        "edge_source": draw_edge_source(jax.random.fold_in(jax.random.fold_in(seeds[10], part), 71), part),
        "edge_target": draw_edge_target(jax.random.fold_in(jax.random.fold_in(seeds[10], part), 71), part),
        "neigh_weight": gaussian(seeds[3], (FEAT, HIDDEN_SIZE), FEAT ** -0.5, 0.21875, ((0, 4),)),
        "self_weight": gaussian(seeds[4], (FEAT, HIDDEN_SIZE), FEAT ** -0.5, 0.21875, ((0, 4),)),
        "bias_one": gaussian(seeds[5], (HIDDEN_SIZE,), 0.5, 3.0, (), jnp.float32),
        "upper_weight": gaussian(seeds[6], (HIDDEN_SIZE, HIDDEN_SIZE), (HIDDEN_SIZE // 4) ** -0.5, 0.375, ((0, 4),)),
        "bias_two": gaussian(seeds[7], (HIDDEN_SIZE,), 0.5, 3.0, (), jnp.float32),
        "upper_neighbours": touch_ends(jax.random.randint(part_keys[8], (TARGETS, FANOUT2), 0, TGT_LOC), jax.random.fold_in(part_keys[8], 1), 0, TGT_LOC - 1).astype(jnp.int32),
        "out_cotangent": gaussian(part_keys[9], (TARGETS, HIDDEN_SIZE), 1.0, 6.0, ((0, 16),)),
    }


def swish_slope(preact):
    gate_val = jax.nn.sigmoid(preact)
    return gate_val * (1.0 + preact * (1.0 - gate_val))


def reference(features, edge_source, edge_target, neigh_weight, self_weight, bias_one, upper_weight, bias_two, upper_neighbours, out_cotangent):
    slice_width = FEAT // N_COLS

    def owner_rows(owner):
        source_local = edge_source[:, owner, :]
        node_ids = (jnp.arange(N_DOM, dtype=jnp.int32)[:, None] * NODE_DEV + source_local).reshape(-1)
        edge_feats = features[node_ids].astype(jnp.float32)
        targets_of = edge_target[owner].reshape(-1)
        summed = jax.ops.segment_sum(edge_feats, targets_of, TGT_DEV + 1)[:TGT_DEV]
        counts = jax.ops.segment_sum(jnp.ones(targets_of.shape, jnp.float32), targets_of, TGT_DEV + 1)[:TGT_DEV]
        mean_feats = (summed / jnp.maximum(counts, 1.0)[:, None]).astype(jnp.bfloat16)
        own_feats = lax.dynamic_slice_in_dim(features, (owner * NODE_DEV).astype(jnp.int32), TGT_DEV, 0)
        total = jnp.zeros((TGT_DEV, HIDDEN_SIZE), jnp.float32)
        for column in range(N_COLS):
            lower = column * slice_width
            upper = lower + slice_width
            partial_value = jnp.dot(mean_feats[:, lower:upper], neigh_weight[lower:upper], preferred_element_type=jnp.float32)
            partial_value = partial_value + jnp.dot(own_feats[:, lower:upper], self_weight[lower:upper], preferred_element_type=jnp.float32)
            rounded = lax.optimization_barrier(partial_value.astype(jnp.bfloat16))
            total = total + rounded.astype(jnp.float32)
        return mean_feats, own_feats, total + bias_one

    mean_all, own_all, pre_one = lax.map(owner_rows, jnp.arange(N_DOM, dtype=jnp.int32))
    mean_all = mean_all.reshape(TARGETS, FEAT)
    own_all = own_all.reshape(TARGETS, FEAT)
    pre_one = pre_one.reshape(TARGETS, HIDDEN_SIZE)
    hidden_one = jax.nn.silu(pre_one).astype(jnp.bfloat16)
    blocks = N_DOM * N_COLS
    positions = jnp.arange(TGT_LOC, dtype=jnp.int32)

    def mixing(neighbours):
        neighbour_hits = jnp.sum((neighbours[:, :, None] == positions[None, None, :]).astype(jnp.float32), axis=1)
        return (jnp.eye(TGT_LOC, dtype=jnp.float32) + neighbour_hits) / (FANOUT2 + 1.0)

    mixers = jax.vmap(mixing)(upper_neighbours.reshape(blocks, TGT_LOC, FANOUT2))
    hidden_blocks = hidden_one.reshape(blocks, TGT_LOC, HIDDEN_SIZE).astype(jnp.float32)
    upper_input = jnp.einsum("bij,bjh->bih", mixers, hidden_blocks, precision=lax.Precision.HIGHEST)
    upper_input = upper_input.astype(jnp.bfloat16).reshape(TARGETS, HIDDEN_SIZE)
    pre_two = jnp.dot(upper_input, upper_weight, preferred_element_type=jnp.float32) + bias_two
    hidden_two = jax.nn.silu(pre_two).astype(jnp.bfloat16)
    slope_two = (out_cotangent.astype(jnp.float32) * swish_slope(pre_two)).astype(jnp.bfloat16)
    grad_upper = jnp.dot(upper_input.T, slope_two, preferred_element_type=jnp.float32)
    back_mixed = jnp.dot(slope_two, upper_weight.T, preferred_element_type=jnp.float32)
    back_one = jnp.einsum("bji,bjh->bih", mixers, back_mixed.reshape(blocks, TGT_LOC, HIDDEN_SIZE), precision=lax.Precision.HIGHEST)
    slope_one = (back_one.reshape(TARGETS, HIDDEN_SIZE) * swish_slope(pre_one)).astype(jnp.bfloat16)
    grad_neigh = jnp.dot(mean_all.T, slope_one, preferred_element_type=jnp.float32)
    grad_self = jnp.dot(own_all.T, slope_one, preferred_element_type=jnp.float32)
    return (hidden_two, grad_neigh, grad_self, grad_upper)
```

```python
import jax
import jax.numpy as jnp
from jax import lax
from jax.experimental import pallas as pl
from jax.experimental.pallas import tpu as pltpu
from jax.sharding import PartitionSpec as P


def swish_slope(preact):
    gate_val = jax.nn.sigmoid(preact)
    return gate_val * (1.0 + preact * (1.0 - gate_val))


def mixing(neighbours, block_len):
    positions = jnp.arange(block_len, dtype=jnp.int32)
    neighbour_hits = jnp.sum(
        (neighbours[:, :, None] == positions[None, None, :]).astype(jnp.float32), axis=1
    )
    return (jnp.eye(block_len, dtype=jnp.float32) + neighbour_hits) / (neighbours.shape[1] + 1.0)


def contract_rows(left_mat, right_mat):
    return lax.dot_general(
        left_mat, right_mat, (((0,), (0,)), ((), ())), preferred_element_type=jnp.float32
    )


def _aggregate_kernel(tgt_ref, rec_ref, sum_ref, cnt_ref):
    step = pl.program_id(0)

    @pl.when(step == 0)
    def _():
        sum_ref[...] = jnp.zeros_like(sum_ref)
        cnt_ref[...] = jnp.zeros_like(cnt_ref)

    targets = tgt_ref[0]
    n_tgt = sum_ref.shape[0]
    rows = lax.broadcasted_iota(jnp.int32, (n_tgt, targets.shape[1]), 0)
    hot = (rows == targets).astype(jnp.bfloat16)
    sum_ref[...] += jnp.dot(hot, rec_ref[0], preferred_element_type=jnp.float32)
    ones = jnp.ones((targets.shape[1], cnt_ref.shape[1]), jnp.bfloat16)
    cnt_ref[...] += jnp.dot(hot, ones, preferred_element_type=jnp.float32)


def aggregate(targets, received, n_tgt):
    n_src, cap = targets.shape
    width = received.shape[-1]
    targets = targets.reshape(n_src, 1, cap)
    received = received.reshape(n_src, cap, width)
    return pl.pallas_call(
        _aggregate_kernel,
        grid=(n_src,),
        in_specs=[
            pl.BlockSpec((1, 1, cap), lambda s: (s, 0, 0)),
            pl.BlockSpec((1, cap, width), lambda s: (s, 0, 0)),
        ],
        out_specs=[
            pl.BlockSpec((n_tgt, width), lambda s: (0, 0)),
            pl.BlockSpec((n_tgt, 128), lambda s: (0, 0)),
        ],
        out_shape=[
            jax.ShapeDtypeStruct((n_tgt, width), jnp.float32),
            jax.ShapeDtypeStruct((n_tgt, 128), jnp.float32),
        ],
        cost_estimate=pl.CostEstimate(
            flops=2 * n_src * n_tgt * cap * (width + 128),
            transcendentals=0,
            bytes_accessed=n_src * cap * (width * 2 + 4) + n_tgt * (width + 128) * 4,
        ),
    )(targets, received)


def local(
    features,
    edge_source,
    edge_target,
    neigh_weight,
    self_weight,
    bias_one,
    upper_weight,
    bias_two,
    upper_neighbours,
    out_cotangent,
):
    n_dom = lax.axis_size("dom")
    n_cols = lax.axis_size("cols")
    capacity = edge_source.shape[2]
    width = features.shape[1]
    hidden = upper_weight.shape[1]
    tgt_loc = upper_neighbours.shape[0]
    tgt_dev = tgt_loc * n_cols
    w_rows = neigh_weight.shape[0]
    up_rows = upper_weight.shape[0]

    packed = jnp.concatenate([neigh_weight, self_weight, upper_weight], axis=0)
    gathered = lax.all_gather(packed, "cols", axis=0, tiled=False)
    neigh_full = gathered[:, :w_rows]
    self_full = gathered[:, w_rows : 2 * w_rows]
    full_upper = gathered[:, 2 * w_rows :].reshape(n_cols * up_rows, hidden)

    outgoing = jnp.take(features, edge_source[0].reshape(-1), axis=0)
    received = lax.all_to_all(outgoing, "dom", split_axis=0, concat_axis=0, tiled=True)
    summed, counts = aggregate(edge_target[0], received, tgt_dev)
    mean_feats = (summed / jnp.maximum(counts[:, :1], 1.0)).astype(jnp.bfloat16)
    own_feats = features[:tgt_dev]

    both = jnp.concatenate([mean_feats, own_feats], axis=1)
    got = lax.all_to_all(both, "cols", split_axis=0, concat_axis=0, tiled=True).reshape(
        n_cols, tgt_loc, 2 * width
    )
    pre_one = (
        jnp.einsum(
            "ctf,cfh->th", got[:, :, :width], neigh_full, preferred_element_type=jnp.float32
        )
        + jnp.einsum(
            "ctf,cfh->th", got[:, :, width:], self_full, preferred_element_type=jnp.float32
        )
        + bias_one
    )
    hidden_one = jax.nn.silu(pre_one).astype(jnp.bfloat16)
    mix_matrix = mixing(upper_neighbours, tgt_loc)
    upper_input = jnp.dot(
        mix_matrix, hidden_one.astype(jnp.float32), precision=lax.Precision.HIGHEST
    ).astype(jnp.bfloat16)
    pre_two = jnp.dot(upper_input, full_upper, preferred_element_type=jnp.float32) + bias_two
    hidden_two = jax.nn.silu(pre_two).astype(jnp.bfloat16)
    slope_two = (out_cotangent.astype(jnp.float32) * swish_slope(pre_two)).astype(jnp.bfloat16)

    local_grad = contract_rows(upper_input, slope_two).astype(jnp.bfloat16)
    col_parts = lax.all_to_all(local_grad, "cols", split_axis=0, concat_axis=0, tiled=True)
    col_sum = jnp.sum(
        col_parts.reshape(n_cols, up_rows, hidden).astype(jnp.float32), axis=0
    )
    grad_upper = lax.psum(col_sum, "dom")

    back_mixed = lax.dot_general(
        slope_two, full_upper, (((1,), (1,)), ((), ())), preferred_element_type=jnp.float32
    )
    back_one = jnp.dot(mix_matrix.T, back_mixed, precision=lax.Precision.HIGHEST)
    slope_one = (back_one * swish_slope(pre_one)).astype(jnp.bfloat16)
    slab_rows = lax.all_to_all(
        jnp.broadcast_to(slope_one[None], (n_cols, tgt_loc, hidden)).reshape(
            n_cols * tgt_loc, hidden
        ),
        "cols",
        split_axis=0,
        concat_axis=0,
        tiled=True,
    )
    neigh_total = contract_rows(mean_feats, slab_rows)
    self_total = contract_rows(own_feats, slab_rows)
    stacked = jnp.concatenate([neigh_total, self_total], axis=0).astype(jnp.bfloat16)
    dom_cols = hidden // n_dom
    dom_parts = lax.all_to_all(stacked, "dom", split_axis=1, concat_axis=0, tiled=True)
    dom_sum = jnp.sum(
        dom_parts.reshape(n_dom, 2 * w_rows, dom_cols).astype(jnp.float32), axis=0
    )
    grad_neigh = dom_sum[:w_rows]
    grad_self = dom_sum[w_rows:]
    return (hidden_two, grad_neigh, grad_self, grad_upper)


def solution(mesh):
    in_specs = (
        P(("groups", "dom"), "cols"),
        P(("groups", "dom"), None, None),
        P(("groups", "dom"), None, None),
        P("cols", None),
        P("cols", None),
        P(),
        P("cols", None),
        P(),
        P(("groups", "dom", "cols"), None),
        P(("groups", "dom", "cols"), None),
    )
    out_specs = (
        P(("groups", "dom", "cols"), None),
        P(("groups", "cols"), "dom"),
        P(("groups", "cols"), "dom"),
        P(("groups", "cols"), None),
    )
    return jax.shard_map(local, mesh=mesh, in_specs=in_specs, out_specs=out_specs, check_vma=False)
```

```python
import jax
import jax.numpy as jnp
from jax import lax
from jax.experimental import pallas as pl
from jax.experimental.pallas import tpu as pltpu
from jax.sharding import PartitionSpec as P


def swish_slope(preact):
    gate_val = jax.nn.sigmoid(preact)
    return gate_val * (1.0 + preact * (1.0 - gate_val))


def mixing(neighbours, block_len):
    positions = jnp.arange(block_len, dtype=jnp.int32)
    neighbour_hits = jnp.sum(
        (neighbours[:, :, None] == positions[None, None, :]).astype(jnp.float32), axis=1
    )
    return (jnp.eye(block_len, dtype=jnp.float32) + neighbour_hits) / (neighbours.shape[1] + 1.0)


def contract_rows(left_mat, right_mat):
    return lax.dot_general(
        left_mat, right_mat, (((0,), (0,)), ((), ())), preferred_element_type=jnp.float32
    )


def _aggregate_kernel(tgt_ref, rec_ref, sum_ref, cnt_ref):
    step = pl.program_id(0)

    @pl.when(step == 0)
    def _():
        sum_ref[...] = jnp.zeros_like(sum_ref)
        cnt_ref[...] = jnp.zeros_like(cnt_ref)

    targets = tgt_ref[0]
    n_tgt = sum_ref.shape[1]
    rows = lax.broadcasted_iota(jnp.int32, (n_tgt, targets.shape[1]), 0)
    hot = (rows == targets).astype(jnp.bfloat16)
    dims = (((1,), (1,)), ((), ()))
    sum_ref[...] += lax.dot_general(rec_ref[0], hot, dims, preferred_element_type=jnp.float32)
    ones = jnp.ones((cnt_ref.shape[0], targets.shape[1]), jnp.bfloat16)
    cnt_ref[...] += lax.dot_general(ones, hot, dims, preferred_element_type=jnp.float32)


def aggregate(targets, received_t, n_tgt):
    n_src, width, cap = received_t.shape
    targets = targets.reshape(n_src, 1, cap)
    return pl.pallas_call(
        _aggregate_kernel,
        grid=(n_src,),
        in_specs=[
            pl.BlockSpec((1, 1, cap), lambda s: (s, 0, 0)),
            pl.BlockSpec((1, width, cap), lambda s: (s, 0, 0)),
        ],
        out_specs=[
            pl.BlockSpec((width, n_tgt), lambda s: (0, 0)),
            pl.BlockSpec((8, n_tgt), lambda s: (0, 0)),
        ],
        out_shape=[
            jax.ShapeDtypeStruct((width, n_tgt), jnp.float32),
            jax.ShapeDtypeStruct((8, n_tgt), jnp.float32),
        ],
        cost_estimate=pl.CostEstimate(
            flops=2 * n_src * n_tgt * cap * (width + 8),
            transcendentals=0,
            bytes_accessed=n_src * cap * (width * 2 + 4) + n_tgt * (width + 8) * 4,
        ),
    )(targets, received_t)


def _xor_pairs(n, bit):
    return [(i, i ^ bit) for i in range(n)]


def _is_pow2(n):
    return n & (n - 1) == 0


def reduce_scatter_blocks(x, axis, n, send_dtype):
    if not _is_pow2(n):
        got = lax.all_to_all(x.astype(send_dtype), axis, 0, 0, tiled=True)
        return jnp.sum(got.astype(x.dtype), axis=0)
    me = lax.axis_index(axis)
    k = n.bit_length() - 1
    cur = x.reshape((2,) * k + x.shape[1:])
    for b in range(k):
        ax = k - 1 - b
        mine = (me >> b) & 1
        keep = lax.dynamic_index_in_dim(cur, mine, axis=ax, keepdims=False)
        send = lax.dynamic_index_in_dim(cur, 1 - mine, axis=ax, keepdims=False)
        got = lax.ppermute(send.astype(send_dtype), axis, _xor_pairs(n, 1 << b))
        cur = keep + got.astype(keep.dtype)
    return cur


def all_gather_blocks(x, axis, n):
    if not _is_pow2(n):
        return lax.all_gather(x, axis, axis=0, tiled=False)
    me = lax.axis_index(axis)
    k = n.bit_length() - 1
    cur = x
    for b in reversed(range(k)):
        mine = (me >> b) & 1
        got = lax.ppermute(cur, axis, _xor_pairs(n, 1 << b))
        low = jnp.where(mine == 0, cur, got)
        high = jnp.where(mine == 0, got, cur)
        cur = jnp.stack([low, high], axis=k - 1 - b)
    return cur.reshape((n,) + x.shape)


def local(
    features,
    edge_source,
    edge_target,
    neigh_weight,
    self_weight,
    bias_one,
    upper_weight,
    bias_two,
    upper_neighbours,
    out_cotangent,
):
    n_dom = lax.axis_size("dom")
    n_cols = lax.axis_size("cols")
    capacity = edge_source.shape[2]
    width = features.shape[1]
    hidden = upper_weight.shape[1]
    tgt_loc = upper_neighbours.shape[0]
    tgt_dev = tgt_loc * n_cols
    w_rows = neigh_weight.shape[0]
    up_rows = upper_weight.shape[0]

    packed = jnp.concatenate([neigh_weight, self_weight, upper_weight], axis=0)
    gathered = lax.all_gather(packed, "cols", axis=0, tiled=False)
    neigh_full = gathered[:, :w_rows]
    self_full = gathered[:, w_rows : 2 * w_rows]
    full_upper = gathered[:, 2 * w_rows :].reshape(n_cols * up_rows, hidden)

    outgoing = features.at[edge_source[0].reshape(-1)].get(mode="promise_in_bounds")
    received = lax.all_to_all(outgoing, "dom", split_axis=0, concat_axis=0, tiled=True)
    received_t = jnp.swapaxes(received.reshape(n_dom, capacity, width), 1, 2)
    summed_t, counts = aggregate(edge_target[0], received_t, tgt_dev)
    mean_t = (summed_t / jnp.maximum(counts[:1], 1.0)).astype(jnp.bfloat16)
    own_t = features[:tgt_dev].T
    both_t = jnp.concatenate([mean_t, own_t], axis=0)

    got = lax.all_to_all(both_t, "cols", split_axis=1, concat_axis=0, tiled=True).reshape(
        n_cols, 2 * width, tgt_loc
    )
    pre_one = (
        jnp.einsum(
            "cft,cfh->th", got[:, :width], neigh_full, preferred_element_type=jnp.float32
        )
        + jnp.einsum(
            "cft,cfh->th", got[:, width:], self_full, preferred_element_type=jnp.float32
        )
        + bias_one
    )
    hidden_one = jax.nn.silu(pre_one).astype(jnp.bfloat16)
    mix_matrix = mixing(upper_neighbours, tgt_loc)
    upper_input = jnp.dot(
        mix_matrix, hidden_one.astype(jnp.float32), precision=lax.Precision.HIGHEST
    ).astype(jnp.bfloat16)
    pre_two = jnp.dot(upper_input, full_upper, preferred_element_type=jnp.float32) + bias_two
    hidden_two = jax.nn.silu(pre_two).astype(jnp.bfloat16)
    slope_two = (out_cotangent.astype(jnp.float32) * swish_slope(pre_two)).astype(jnp.bfloat16)

    local_grad = contract_rows(upper_input, slope_two)
    col_sum = reduce_scatter_blocks(
        local_grad.reshape(n_cols, up_rows, hidden), "cols", n_cols, jnp.bfloat16
    )
    dom_rows = up_rows // n_dom
    dom_sum = reduce_scatter_blocks(
        col_sum.reshape(n_dom, dom_rows, hidden), "dom", n_dom, jnp.bfloat16
    )
    grad_upper = lax.all_to_all(
        jnp.broadcast_to(dom_sum.astype(jnp.bfloat16)[None], (n_dom, dom_rows, hidden)),
        "dom",
        split_axis=0,
        concat_axis=0,
        tiled=True,
    ).reshape(up_rows, hidden).astype(jnp.float32)

    back_mixed = lax.dot_general(
        slope_two, full_upper, (((1,), (1,)), ((), ())), preferred_element_type=jnp.float32
    )
    back_one = jnp.dot(mix_matrix.T, back_mixed, precision=lax.Precision.HIGHEST)
    slope_one = (back_one * swish_slope(pre_one)).astype(jnp.bfloat16)
    slab_rows = all_gather_blocks(slope_one, "cols", n_cols).reshape(tgt_dev, hidden)
    stacked = jnp.dot(both_t, slab_rows, preferred_element_type=jnp.float32)
    dom_cols = hidden // n_dom
    grad_layer = reduce_scatter_blocks(
        jnp.swapaxes(stacked.reshape(2 * width, n_dom, dom_cols), 0, 1),
        "dom",
        n_dom,
        jnp.bfloat16,
    )
    grad_neigh = grad_layer[:w_rows]
    grad_self = grad_layer[w_rows:]
    return (hidden_two, grad_neigh, grad_self, grad_upper)


def solution(mesh):
    in_specs = (
        P(("groups", "dom"), "cols"),
        P(("groups", "dom"), None, None),
        P(("groups", "dom"), None, None),
        P("cols", None),
        P("cols", None),
        P(),
        P("cols", None),
        P(),
        P(("groups", "dom", "cols"), None),
        P(("groups", "dom", "cols"), None),
    )
    out_specs = (
        P(("groups", "dom", "cols"), None),
        P(("groups", "cols"), "dom"),
        P(("groups", "cols"), "dom"),
        P(("groups", "cols"), None),
    )
    return jax.shard_map(local, mesh=mesh, in_specs=in_specs, out_specs=out_specs, check_vma=False)
```

```python
import jax
import jax.numpy as jnp
from jax import lax
from jax.experimental import pallas as pl
from jax.experimental.pallas import tpu as pltpu
from jax.sharding import PartitionSpec as P


def swish_slope(preact):
    gate_val = jax.nn.sigmoid(preact)
    return gate_val * (1.0 + preact * (1.0 - gate_val))


def mixing(neighbours, block_len):
    positions = jnp.arange(block_len, dtype=jnp.int32)
    neighbour_hits = jnp.sum(
        (neighbours[:, :, None] == positions[None, None, :]).astype(jnp.float32), axis=1
    )
    return (jnp.eye(block_len, dtype=jnp.float32) + neighbour_hits) / (neighbours.shape[1] + 1.0)


def contract_rows(left_mat, right_mat):
    return lax.dot_general(
        left_mat, right_mat, (((0,), (0,)), ((), ())), preferred_element_type=jnp.float32
    )


def _accumulate_kernel(tgt_ref, rec_ref, sum_in, cnt_in, sum_ref, cnt_ref):
    targets = tgt_ref[...]
    n_tgt = sum_ref.shape[1]
    rows = lax.broadcasted_iota(jnp.int32, (n_tgt, targets.shape[1]), 0)
    hot = (rows == targets).astype(jnp.bfloat16)
    dims = (((1,), (1,)), ((), ()))
    sum_ref[...] = sum_in[...] + lax.dot_general(
        rec_ref[...], hot, dims, preferred_element_type=jnp.float32
    )
    ones = jnp.ones((cnt_ref.shape[0], targets.shape[1]), jnp.bfloat16)
    cnt_ref[...] = cnt_in[...] + lax.dot_general(
        ones, hot, dims, preferred_element_type=jnp.float32
    )


def accumulate(targets, rec_t, acc_sum, acc_cnt):
    width, cap = rec_t.shape
    n_tgt = acc_sum.shape[1]
    return pl.pallas_call(
        _accumulate_kernel,
        out_shape=[
            jax.ShapeDtypeStruct(acc_sum.shape, jnp.float32),
            jax.ShapeDtypeStruct(acc_cnt.shape, jnp.float32),
        ],
        input_output_aliases={2: 0, 3: 1},
        cost_estimate=pl.CostEstimate(
            flops=2 * n_tgt * cap * (width + acc_cnt.shape[0]),
            transcendentals=0,
            bytes_accessed=cap * (width * 2 + 4) + 2 * n_tgt * (width + acc_cnt.shape[0]) * 4,
        ),
    )(targets, rec_t, acc_sum, acc_cnt)


def _shift_pairs(n, shift):
    return [(i, (i + shift) % n) for i in range(n)]


def _xor_pairs(n, bit):
    return [(i, i ^ bit) for i in range(n)]


def _is_pow2(n):
    return n & (n - 1) == 0


def reduce_scatter_blocks(x, axis, n, send_dtype):
    if not _is_pow2(n):
        got = lax.all_to_all(x.astype(send_dtype), axis, 0, 0, tiled=True)
        return jnp.sum(got.astype(x.dtype), axis=0)
    me = lax.axis_index(axis)
    k = n.bit_length() - 1
    cur = x.reshape((2,) * k + x.shape[1:])
    for b in range(k):
        ax = k - 1 - b
        mine = (me >> b) & 1
        keep = lax.dynamic_index_in_dim(cur, mine, axis=ax, keepdims=False)
        send = lax.dynamic_index_in_dim(cur, 1 - mine, axis=ax, keepdims=False)
        got = lax.ppermute(send.astype(send_dtype), axis, _xor_pairs(n, 1 << b))
        cur = keep + got.astype(keep.dtype)
    return cur


def all_gather_blocks(x, axis, n):
    if not _is_pow2(n):
        return lax.all_gather(x, axis, axis=0, tiled=False)
    me = lax.axis_index(axis)
    k = n.bit_length() - 1
    cur = x
    for b in reversed(range(k)):
        mine = (me >> b) & 1
        got = lax.ppermute(cur, axis, _xor_pairs(n, 1 << b))
        low = jnp.where(mine == 0, cur, got)
        high = jnp.where(mine == 0, got, cur)
        cur = jnp.stack([low, high], axis=k - 1 - b)
    return cur.reshape((n,) + x.shape)


def local(
    features,
    edge_source,
    edge_target,
    neigh_weight,
    self_weight,
    bias_one,
    upper_weight,
    bias_two,
    upper_neighbours,
    out_cotangent,
):
    n_dom = lax.axis_size("dom")
    n_cols = lax.axis_size("cols")
    capacity = edge_source.shape[2]
    width = features.shape[1]
    hidden = upper_weight.shape[1]
    tgt_loc = upper_neighbours.shape[0]
    tgt_dev = tgt_loc * n_cols
    w_rows = neigh_weight.shape[0]
    up_rows = upper_weight.shape[0]

    packed = jnp.concatenate([neigh_weight, self_weight, upper_weight], axis=0)
    gathered = lax.all_gather(packed, "cols", axis=0, tiled=False)
    neigh_full = gathered[:, :w_rows]
    self_full = gathered[:, w_rows : 2 * w_rows]
    full_upper = gathered[:, 2 * w_rows :].reshape(n_cols * up_rows, hidden)

    me_dom = lax.axis_index("dom")
    me_col = lax.axis_index("cols")
    own_t = features[:tgt_dev].T
    own_pre = bias_one
    for shift in range(n_cols):
        dest = (me_col + shift) % n_cols
        src = (me_col - shift) % n_cols
        chunk = lax.dynamic_slice_in_dim(own_t, dest * tgt_loc, tgt_loc, axis=1)
        if shift:
            chunk = lax.ppermute(chunk, "cols", _shift_pairs(n_cols, shift))
        weight = lax.dynamic_index_in_dim(self_full, src, 0, keepdims=False)
        own_pre = own_pre + contract_rows(chunk, weight)

    summed_t = jnp.zeros((width, tgt_dev), jnp.float32)
    counts = jnp.zeros((8, tgt_dev), jnp.float32)
    for shift in range(n_dom):
        dest = (me_dom + shift) % n_dom
        src = (me_dom - shift) % n_dom
        slots = lax.dynamic_index_in_dim(edge_source[0], dest, 0, keepdims=False)
        rows_t = features.at[slots].get(mode="promise_in_bounds").T
        if shift:
            rows_t = lax.ppermute(rows_t, "dom", _shift_pairs(n_dom, shift))
        targets = lax.dynamic_index_in_dim(edge_target[0], src, 0, keepdims=True)
        summed_t, counts = accumulate(targets, rows_t, summed_t, counts)
    mean_t = (summed_t / jnp.maximum(counts[:1], 1.0)).astype(jnp.bfloat16)
    both_t = jnp.concatenate([mean_t, own_t], axis=0)

    pre_one = own_pre
    for shift in range(n_cols):
        dest = (me_col + shift) % n_cols
        src = (me_col - shift) % n_cols
        chunk = lax.dynamic_slice_in_dim(mean_t, dest * tgt_loc, tgt_loc, axis=1)
        if shift:
            chunk = lax.ppermute(chunk, "cols", _shift_pairs(n_cols, shift))
        weight = lax.dynamic_index_in_dim(neigh_full, src, 0, keepdims=False)
        pre_one = pre_one + contract_rows(chunk, weight)
    hidden_one = jax.nn.silu(pre_one).astype(jnp.bfloat16)
    mix_matrix = mixing(upper_neighbours, tgt_loc)
    upper_input = jnp.dot(
        mix_matrix, hidden_one.astype(jnp.float32), precision=lax.Precision.HIGHEST
    ).astype(jnp.bfloat16)
    pre_two = jnp.dot(upper_input, full_upper, preferred_element_type=jnp.float32) + bias_two
    hidden_two = jax.nn.silu(pre_two).astype(jnp.bfloat16)
    slope_two = (out_cotangent.astype(jnp.float32) * swish_slope(pre_two)).astype(jnp.bfloat16)

    local_grad = contract_rows(upper_input, slope_two)
    col_sum = reduce_scatter_blocks(
        local_grad.reshape(n_cols, up_rows, hidden), "cols", n_cols, jnp.bfloat16
    )
    back_mixed = lax.dot_general(
        slope_two, full_upper, (((1,), (1,)), ((), ())), preferred_element_type=jnp.float32
    )
    back_one = jnp.dot(mix_matrix.T, back_mixed, precision=lax.Precision.HIGHEST)
    slope_one = (back_one * swish_slope(pre_one)).astype(jnp.bfloat16)
    slab_rows = all_gather_blocks(slope_one, "cols", n_cols).reshape(tgt_dev, hidden)
    stacked = jnp.dot(both_t, slab_rows, preferred_element_type=jnp.float32)
    dom_cols = hidden // n_dom
    dom_rows = up_rows // n_dom
    upper_len = dom_rows * hidden
    payload = jnp.concatenate(
        [
            col_sum.reshape(n_dom, upper_len),
            jnp.swapaxes(stacked.reshape(2 * width, n_dom, dom_cols), 0, 1).reshape(n_dom, -1),
        ],
        axis=1,
    )
    reduced = reduce_scatter_blocks(payload, "dom", n_dom, jnp.bfloat16)
    grad_layer = reduced[upper_len:].reshape(2 * width, dom_cols)
    grad_upper = lax.all_to_all(
        jnp.broadcast_to(
            reduced[:upper_len].astype(jnp.bfloat16).reshape(1, dom_rows, hidden),
            (n_dom, dom_rows, hidden),
        ),
        "dom",
        split_axis=0,
        concat_axis=0,
        tiled=True,
    ).reshape(up_rows, hidden).astype(jnp.float32)
    grad_neigh = grad_layer[:w_rows]
    grad_self = grad_layer[w_rows:]
    return (hidden_two, grad_neigh, grad_self, grad_upper)


def solution(mesh):
    in_specs = (
        P(("groups", "dom"), "cols"),
        P(("groups", "dom"), None, None),
        P(("groups", "dom"), None, None),
        P("cols", None),
        P("cols", None),
        P(),
        P("cols", None),
        P(),
        P(("groups", "dom", "cols"), None),
        P(("groups", "dom", "cols"), None),
    )
    out_specs = (
        P(("groups", "dom", "cols"), None),
        P(("groups", "cols"), "dom"),
        P(("groups", "cols"), "dom"),
        P(("groups", "cols"), None),
    )
    return jax.shard_map(local, mesh=mesh, in_specs=in_specs, out_specs=out_specs, check_vma=False)
```

```python
import jax
import jax.numpy as jnp
from jax import lax
from jax.experimental import pallas as pl
from jax.experimental.pallas import tpu as pltpu
from jax.sharding import PartitionSpec as P


def swish_slope(preact):
    gate_val = jax.nn.sigmoid(preact)
    return gate_val * (1.0 + preact * (1.0 - gate_val))


def mixing(neighbours, block_len):
    positions = jnp.arange(block_len, dtype=jnp.int32)
    neighbour_hits = jnp.sum(
        (neighbours[:, :, None] == positions[None, None, :]).astype(jnp.float32), axis=1
    )
    return (jnp.eye(block_len, dtype=jnp.float32) + neighbour_hits) / (neighbours.shape[1] + 1.0)


def contract_rows(left_mat, right_mat):
    return lax.dot_general(
        left_mat, right_mat, (((0,), (0,)), ((), ())), preferred_element_type=jnp.float32
    )


def _accumulate_kernel(tgt_ref, rec_ref, sum_in, cnt_in, sum_ref, cnt_ref):
    targets = tgt_ref[...]
    n_tgt = sum_ref.shape[1]
    rows = lax.broadcasted_iota(jnp.int32, (n_tgt, targets.shape[1]), 0)
    hot = (rows == targets).astype(jnp.bfloat16)
    dims = (((1,), (1,)), ((), ()))
    sum_ref[...] = sum_in[...] + lax.dot_general(
        rec_ref[...], hot, dims, preferred_element_type=jnp.float32
    )
    ones = jnp.ones((cnt_ref.shape[0], targets.shape[1]), jnp.bfloat16)
    cnt_ref[...] = cnt_in[...] + lax.dot_general(
        ones, hot, dims, preferred_element_type=jnp.float32
    )


def accumulate(targets, rec_t, acc_sum, acc_cnt):
    width, cap = rec_t.shape
    n_tgt = acc_sum.shape[1]
    return pl.pallas_call(
        _accumulate_kernel,
        out_shape=[
            jax.ShapeDtypeStruct(acc_sum.shape, jnp.float32),
            jax.ShapeDtypeStruct(acc_cnt.shape, jnp.float32),
        ],
        input_output_aliases={2: 0, 3: 1},
        cost_estimate=pl.CostEstimate(
            flops=2 * n_tgt * cap * (width + acc_cnt.shape[0]),
            transcendentals=0,
            bytes_accessed=cap * (width * 2 + 4) + 2 * n_tgt * (width + acc_cnt.shape[0]) * 4,
        ),
    )(targets, rec_t, acc_sum, acc_cnt)


def _shift_pairs(n, shift):
    return [(i, (i + shift) % n) for i in range(n)]


def _xor_pairs(n, bit):
    return [(i, i ^ bit) for i in range(n)]


def _is_pow2(n):
    return n & (n - 1) == 0


def reduce_scatter_blocks(x, axis, n, send_dtype, high_first=False):
    if not _is_pow2(n):
        got = lax.all_to_all(x.astype(send_dtype), axis, 0, 0, tiled=True)
        return jnp.sum(got.astype(x.dtype), axis=0)
    me = lax.axis_index(axis)
    k = n.bit_length() - 1
    cur = x.reshape((2,) * k + x.shape[1:])
    axis_bits = list(reversed(range(k)))
    for b in (axis_bits[:] if high_first else list(range(k))):
        ax = axis_bits.index(b)
        axis_bits.remove(b)
        mine = (me >> b) & 1
        keep = lax.dynamic_index_in_dim(cur, mine, axis=ax, keepdims=False)
        send = lax.dynamic_index_in_dim(cur, 1 - mine, axis=ax, keepdims=False)
        got = lax.ppermute(send.astype(send_dtype), axis, _xor_pairs(n, 1 << b))
        cur = keep + got.astype(keep.dtype)
    return cur


def all_gather_blocks(x, axis, n):
    if not _is_pow2(n):
        return lax.all_gather(x, axis, axis=0, tiled=False)
    me = lax.axis_index(axis)
    k = n.bit_length() - 1
    cur = x
    for b in reversed(range(k)):
        mine = (me >> b) & 1
        got = lax.ppermute(cur, axis, _xor_pairs(n, 1 << b))
        low = jnp.where(mine == 0, cur, got)
        high = jnp.where(mine == 0, got, cur)
        cur = jnp.stack([low, high], axis=k - 1 - b)
    return cur.reshape((n,) + x.shape)


def local(
    features,
    edge_source,
    edge_target,
    neigh_weight,
    self_weight,
    bias_one,
    upper_weight,
    bias_two,
    upper_neighbours,
    out_cotangent,
):
    n_dom = lax.axis_size("dom")
    n_cols = lax.axis_size("cols")
    capacity = edge_source.shape[2]
    width = features.shape[1]
    hidden = upper_weight.shape[1]
    tgt_loc = upper_neighbours.shape[0]
    tgt_dev = tgt_loc * n_cols
    w_rows = neigh_weight.shape[0]
    up_rows = upper_weight.shape[0]

    packed = jnp.concatenate([neigh_weight, self_weight, upper_weight], axis=0)
    gathered = lax.all_gather(packed, "cols", axis=0, tiled=False)
    neigh_full = gathered[:, :w_rows]
    self_full = gathered[:, w_rows : 2 * w_rows]
    full_upper = gathered[:, 2 * w_rows :].reshape(n_cols * up_rows, hidden)

    me_dom = lax.axis_index("dom")
    me_col = lax.axis_index("cols")
    own_t = features[:tgt_dev].T
    own_pre = bias_one
    for shift in range(n_cols):
        dest = (me_col + shift) % n_cols
        src = (me_col - shift) % n_cols
        chunk = lax.dynamic_slice_in_dim(own_t, dest * tgt_loc, tgt_loc, axis=1)
        if shift:
            chunk = lax.ppermute(chunk, "cols", _shift_pairs(n_cols, shift))
        weight = lax.dynamic_index_in_dim(self_full, src, 0, keepdims=False)
        own_pre = own_pre + contract_rows(chunk, weight)

    summed_t = jnp.zeros((width, tgt_dev), jnp.float32)
    counts = jnp.zeros((8, tgt_dev), jnp.float32)
    for shift in range(n_dom):
        dest = (me_dom + shift) % n_dom
        src = (me_dom - shift) % n_dom
        slots = lax.dynamic_index_in_dim(edge_source[0], dest, 0, keepdims=False)
        rows_t = features.at[slots].get(mode="promise_in_bounds").T
        if shift:
            rows_t = lax.ppermute(rows_t, "dom", _shift_pairs(n_dom, shift))
        targets = lax.dynamic_index_in_dim(edge_target[0], src, 0, keepdims=True)
        summed_t, counts = accumulate(targets, rows_t, summed_t, counts)
    mean_t = (summed_t / jnp.maximum(counts[:1], 1.0)).astype(jnp.bfloat16)
    both_t = jnp.concatenate([mean_t, own_t], axis=0)

    pre_one = own_pre
    for shift in range(n_cols):
        dest = (me_col + shift) % n_cols
        src = (me_col - shift) % n_cols
        chunk = lax.dynamic_slice_in_dim(mean_t, dest * tgt_loc, tgt_loc, axis=1)
        if shift:
            chunk = lax.ppermute(chunk, "cols", _shift_pairs(n_cols, shift))
        weight = lax.dynamic_index_in_dim(neigh_full, src, 0, keepdims=False)
        pre_one = pre_one + contract_rows(chunk, weight)
    hidden_one = jax.nn.silu(pre_one).astype(jnp.bfloat16)
    mix_matrix = mixing(upper_neighbours, tgt_loc)
    upper_input = jnp.dot(
        mix_matrix, hidden_one.astype(jnp.float32), precision=lax.Precision.HIGHEST
    ).astype(jnp.bfloat16)
    pre_two = jnp.dot(upper_input, full_upper, preferred_element_type=jnp.float32) + bias_two
    hidden_two = jax.nn.silu(pre_two).astype(jnp.bfloat16)
    slope_two = (out_cotangent.astype(jnp.float32) * swish_slope(pre_two)).astype(jnp.bfloat16)

    local_grad = contract_rows(upper_input, slope_two)
    col_sum = reduce_scatter_blocks(
        local_grad.reshape(n_cols, up_rows, hidden), "cols", n_cols, jnp.bfloat16
    )
    back_mixed = lax.dot_general(
        slope_two, full_upper, (((1,), (1,)), ((), ())), preferred_element_type=jnp.float32
    )
    back_one = jnp.dot(mix_matrix.T, back_mixed, precision=lax.Precision.HIGHEST)
    slope_one = (back_one * swish_slope(pre_one)).astype(jnp.bfloat16)
    slab_rows = all_gather_blocks(slope_one, "cols", n_cols).reshape(tgt_dev, hidden)
    stacked = jnp.dot(both_t, slab_rows, preferred_element_type=jnp.float32)
    dom_cols = hidden // n_dom
    dom_rows = up_rows // n_dom
    upper_part = reduce_scatter_blocks(
        col_sum.reshape(n_dom, dom_rows, hidden), "dom", n_dom, jnp.bfloat16, high_first=True
    )
    grad_upper = all_gather_blocks(upper_part.astype(jnp.bfloat16), "dom", n_dom)
    grad_upper = grad_upper.reshape(up_rows, hidden).astype(jnp.float32)
    grad_layer = reduce_scatter_blocks(
        jnp.swapaxes(stacked.reshape(2 * width, n_dom, dom_cols), 0, 1),
        "dom",
        n_dom,
        jnp.bfloat16,
    )
    grad_neigh = grad_layer[:w_rows]
    grad_self = grad_layer[w_rows:]
    return (hidden_two, grad_neigh, grad_self, grad_upper)


def solution(mesh):
    in_specs = (
        P(("groups", "dom"), "cols"),
        P(("groups", "dom"), None, None),
        P(("groups", "dom"), None, None),
        P("cols", None),
        P("cols", None),
        P(),
        P("cols", None),
        P(),
        P(("groups", "dom", "cols"), None),
        P(("groups", "dom", "cols"), None),
    )
    out_specs = (
        P(("groups", "dom", "cols"), None),
        P(("groups", "cols"), "dom"),
        P(("groups", "cols"), "dom"),
        P(("groups", "cols"), None),
    )
    return jax.shard_map(local, mesh=mesh, in_specs=in_specs, out_specs=out_specs, check_vma=False)
```

```python
import jax
import jax.numpy as jnp
from jax import lax
from jax.experimental import pallas as pl
from jax.experimental.pallas import tpu as pltpu
from jax.sharding import PartitionSpec as P


def swish_slope(preact):
    gate_val = jax.nn.sigmoid(preact)
    return gate_val * (1.0 + preact * (1.0 - gate_val))


def mixing(neighbours, block_len):
    positions = jnp.arange(block_len, dtype=jnp.int32)
    neighbour_hits = jnp.sum(
        (neighbours[:, :, None] == positions[None, None, :]).astype(jnp.float32), axis=1
    )
    return (jnp.eye(block_len, dtype=jnp.float32) + neighbour_hits) / (neighbours.shape[1] + 1.0)


def contract_rows(left_mat, right_mat):
    return lax.dot_general(
        left_mat, right_mat, (((0,), (0,)), ((), ())), preferred_element_type=jnp.float32
    )


def _accumulate_kernel(tgt_ref, rec_ref, sum_in, cnt_in, sum_ref, cnt_ref):
    targets = tgt_ref[...]
    n_tgt = sum_ref.shape[1]
    rows = lax.broadcasted_iota(jnp.int32, (n_tgt, targets.shape[1]), 0)
    hot = (rows == targets).astype(jnp.bfloat16)
    dims = (((1,), (1,)), ((), ()))
    sum_ref[...] = sum_in[...] + lax.dot_general(
        rec_ref[...], hot, dims, preferred_element_type=jnp.float32
    )
    ones = jnp.ones((cnt_ref.shape[0], targets.shape[1]), jnp.bfloat16)
    cnt_ref[...] = cnt_in[...] + lax.dot_general(
        ones, hot, dims, preferred_element_type=jnp.float32
    )


def accumulate(targets, rec_t, acc_sum, acc_cnt):
    width, cap = rec_t.shape
    n_tgt = acc_sum.shape[1]
    return pl.pallas_call(
        _accumulate_kernel,
        out_shape=[
            jax.ShapeDtypeStruct(acc_sum.shape, jnp.float32),
            jax.ShapeDtypeStruct(acc_cnt.shape, jnp.float32),
        ],
        input_output_aliases={2: 0, 3: 1},
        cost_estimate=pl.CostEstimate(
            flops=2 * n_tgt * cap * (width + acc_cnt.shape[0]),
            transcendentals=0,
            bytes_accessed=cap * (width * 2 + 4) + 2 * n_tgt * (width + acc_cnt.shape[0]) * 4,
        ),
    )(targets, rec_t, acc_sum, acc_cnt)


def _shift_pairs(n, shift):
    return [(i, (i + shift) % n) for i in range(n)]


def _xor_pairs(n, bit):
    return [(i, i ^ bit) for i in range(n)]


def _is_pow2(n):
    return n & (n - 1) == 0


def reduce_scatter_blocks(x, axis, n, send_dtype, high_first=False):
    if not _is_pow2(n):
        got = lax.all_to_all(x.astype(send_dtype), axis, 0, 0, tiled=True)
        return jnp.sum(got.astype(x.dtype), axis=0)
    k = n.bit_length() - 1
    axis_bits = list(reversed(range(k)))
    order = axis_bits[:] if high_first else list(range(k))
    return _butterfly_reduce(
        x.reshape((2,) * k + x.shape[1:]), axis, n, axis_bits, order, send_dtype
    )


def _butterfly_reduce(cur, axis, n, axis_bits, order, send_dtype):
    me = lax.axis_index(axis)
    axis_bits = list(axis_bits)
    for b in order:
        ax = axis_bits.index(b)
        axis_bits.remove(b)
        mine = (me >> b) & 1
        keep = lax.dynamic_index_in_dim(cur, mine, axis=ax, keepdims=False)
        send = lax.dynamic_index_in_dim(cur, 1 - mine, axis=ax, keepdims=False)
        got = lax.ppermute(send.astype(send_dtype), axis, _xor_pairs(n, 1 << b))
        cur = keep + got.astype(keep.dtype)
    return cur


def reduce_scatter_grid(x, n_dom, n_cols, send_dtype):
    if not (_is_pow2(n_dom) and _is_pow2(n_cols)):
        part = reduce_scatter_blocks(x, "cols", n_cols, send_dtype)
        return reduce_scatter_blocks(part, "dom", n_dom, send_dtype)
    kc = n_cols.bit_length() - 1
    kd = n_dom.bit_length() - 1
    axis_bits = [kc - 1 - i for i in range(kc)] + [kc + kd - 1 - i for i in range(kd)]
    order = list(range(min(kc, 1))) + list(range(kc, kc + kd)) + list(range(1, kc))
    cur = x.reshape((2,) * (kc + kd) + x.shape[2:])
    return _butterfly_reduce(
        cur, ("dom", "cols"), n_dom * n_cols, axis_bits, order, send_dtype
    )


def all_gather_blocks(x, axis, n):
    if not _is_pow2(n):
        return lax.all_gather(x, axis, axis=0, tiled=False)
    me = lax.axis_index(axis)
    k = n.bit_length() - 1
    cur = x
    for b in reversed(range(k)):
        mine = (me >> b) & 1
        got = lax.ppermute(cur, axis, _xor_pairs(n, 1 << b))
        low = jnp.where(mine == 0, cur, got)
        high = jnp.where(mine == 0, got, cur)
        cur = jnp.stack([low, high], axis=k - 1 - b)
    return cur.reshape((n,) + x.shape)


def local(
    features,
    edge_source,
    edge_target,
    neigh_weight,
    self_weight,
    bias_one,
    upper_weight,
    bias_two,
    upper_neighbours,
    out_cotangent,
):
    n_dom = lax.axis_size("dom")
    n_cols = lax.axis_size("cols")
    capacity = edge_source.shape[2]
    width = features.shape[1]
    hidden = upper_weight.shape[1]
    tgt_loc = upper_neighbours.shape[0]
    tgt_dev = tgt_loc * n_cols
    w_rows = neigh_weight.shape[0]
    up_rows = upper_weight.shape[0]

    packed = jnp.concatenate([neigh_weight, self_weight], axis=0)
    gathered = lax.all_gather(packed, "cols", axis=0, tiled=False)
    neigh_full = gathered[:, :w_rows]
    self_full = gathered[:, w_rows:]
    full_upper = lax.all_gather(upper_weight, "cols", axis=0, tiled=True)

    me_dom = lax.axis_index("dom")
    me_col = lax.axis_index("cols")
    own_t = features[:tgt_dev].T
    own_pre = bias_one
    for shift in range(n_cols):
        dest = (me_col + shift) % n_cols
        src = (me_col - shift) % n_cols
        chunk = lax.dynamic_slice_in_dim(own_t, dest * tgt_loc, tgt_loc, axis=1)
        if shift:
            chunk = lax.ppermute(chunk, "cols", _shift_pairs(n_cols, shift))
        weight = lax.dynamic_index_in_dim(self_full, src, 0, keepdims=False)
        own_pre = own_pre + contract_rows(chunk, weight)

    summed_t = jnp.zeros((width, tgt_dev), jnp.float32)
    counts = jnp.zeros((8, tgt_dev), jnp.float32)
    for shift in range(n_dom):
        dest = (me_dom + shift) % n_dom
        src = (me_dom - shift) % n_dom
        slots = lax.dynamic_index_in_dim(edge_source[0], dest, 0, keepdims=False)
        rows_t = features.at[slots].get(mode="promise_in_bounds").T
        if shift:
            rows_t = lax.ppermute(rows_t, "dom", _shift_pairs(n_dom, shift))
        targets = lax.dynamic_index_in_dim(edge_target[0], src, 0, keepdims=True)
        summed_t, counts = accumulate(targets, rows_t, summed_t, counts)
    mean_t = (summed_t / jnp.maximum(counts[:1], 1.0)).astype(jnp.bfloat16)
    both_t = jnp.concatenate([mean_t, own_t], axis=0)

    pre_one = own_pre
    for shift in range(n_cols):
        dest = (me_col + shift) % n_cols
        src = (me_col - shift) % n_cols
        chunk = lax.dynamic_slice_in_dim(mean_t, dest * tgt_loc, tgt_loc, axis=1)
        if shift:
            chunk = lax.ppermute(chunk, "cols", _shift_pairs(n_cols, shift))
        weight = lax.dynamic_index_in_dim(neigh_full, src, 0, keepdims=False)
        pre_one = pre_one + contract_rows(chunk, weight)
    hidden_one = jax.nn.silu(pre_one).astype(jnp.bfloat16)
    mix_matrix = mixing(upper_neighbours, tgt_loc)
    upper_input = jnp.dot(
        mix_matrix, hidden_one.astype(jnp.float32), precision=lax.Precision.HIGHEST
    ).astype(jnp.bfloat16)
    pre_two = jnp.dot(upper_input, full_upper, preferred_element_type=jnp.float32) + bias_two
    hidden_two = jax.nn.silu(pre_two).astype(jnp.bfloat16)
    slope_two = (out_cotangent.astype(jnp.float32) * swish_slope(pre_two)).astype(jnp.bfloat16)

    local_grad = contract_rows(upper_input, slope_two)
    dom_rows = up_rows // n_dom
    upper_part = reduce_scatter_grid(
        local_grad.reshape(n_cols, n_dom, dom_rows, hidden), n_dom, n_cols, jnp.bfloat16
    )
    back_mixed = lax.dot_general(
        slope_two, full_upper, (((1,), (1,)), ((), ())), preferred_element_type=jnp.float32
    )
    back_one = jnp.dot(mix_matrix.T, back_mixed, precision=lax.Precision.HIGHEST)
    slope_one = (back_one * swish_slope(pre_one)).astype(jnp.bfloat16)
    slab_rows = all_gather_blocks(slope_one, "cols", n_cols).reshape(tgt_dev, hidden)
    stacked = jnp.dot(both_t, slab_rows, preferred_element_type=jnp.float32)
    dom_cols = hidden // n_dom
    grad_upper = all_gather_blocks(upper_part.astype(jnp.bfloat16), "dom", n_dom)
    grad_upper = grad_upper.reshape(up_rows, hidden).astype(jnp.float32)
    grad_layer = reduce_scatter_blocks(
        jnp.swapaxes(stacked.reshape(2 * width, n_dom, dom_cols), 0, 1),
        "dom",
        n_dom,
        jnp.bfloat16,
    )
    grad_neigh = grad_layer[:w_rows]
    grad_self = grad_layer[w_rows:]
    return (hidden_two, grad_neigh, grad_self, grad_upper)


def solution(mesh):
    in_specs = (
        P(("groups", "dom"), "cols"),
        P(("groups", "dom"), None, None),
        P(("groups", "dom"), None, None),
        P("cols", None),
        P("cols", None),
        P(),
        P("cols", None),
        P(),
        P(("groups", "dom", "cols"), None),
        P(("groups", "dom", "cols"), None),
    )
    out_specs = (
        P(("groups", "dom", "cols"), None),
        P(("groups", "cols"), "dom"),
        P(("groups", "cols"), "dom"),
        P(("groups", "cols"), None),
    )
    return jax.shard_map(local, mesh=mesh, in_specs=in_specs, out_specs=out_specs, check_vma=False)
```

```python
import jax
import jax.numpy as jnp
from jax import lax
from jax.experimental import pallas as pl
from jax.experimental.pallas import tpu as pltpu
from jax.sharding import PartitionSpec as P


def swish_slope(preact):
    gate_val = jax.nn.sigmoid(preact)
    return gate_val * (1.0 + preact * (1.0 - gate_val))


def mixing(neighbours, block_len):
    positions = jnp.arange(block_len, dtype=jnp.int32)
    neighbour_hits = jnp.sum(
        (neighbours[:, :, None] == positions[None, None, :]).astype(jnp.float32), axis=1
    )
    return (jnp.eye(block_len, dtype=jnp.float32) + neighbour_hits) / (neighbours.shape[1] + 1.0)


def contract_rows(left_mat, right_mat):
    return lax.dot_general(
        left_mat, right_mat, (((0,), (0,)), ((), ())), preferred_element_type=jnp.float32
    )


def _accumulate_kernel(tgt_ref, rec_ref, sum_in, cnt_in, sum_ref, cnt_ref):
    targets = tgt_ref[...]
    n_tgt = sum_ref.shape[1]
    rows = lax.broadcasted_iota(jnp.int32, (n_tgt, targets.shape[1]), 0)
    hot = (rows == targets).astype(jnp.bfloat16)
    dims = (((1,), (1,)), ((), ()))
    sum_ref[...] = sum_in[...] + lax.dot_general(
        rec_ref[...], hot, dims, preferred_element_type=jnp.float32
    )
    ones = jnp.ones((cnt_ref.shape[0], targets.shape[1]), jnp.bfloat16)
    cnt_ref[...] = cnt_in[...] + lax.dot_general(
        ones, hot, dims, preferred_element_type=jnp.float32
    )


def accumulate(targets, rec_t, acc_sum, acc_cnt):
    width, cap = rec_t.shape
    n_tgt = acc_sum.shape[1]
    return pl.pallas_call(
        _accumulate_kernel,
        out_shape=[
            jax.ShapeDtypeStruct(acc_sum.shape, jnp.float32),
            jax.ShapeDtypeStruct(acc_cnt.shape, jnp.float32),
        ],
        input_output_aliases={2: 0, 3: 1},
        cost_estimate=pl.CostEstimate(
            flops=2 * n_tgt * cap * (width + acc_cnt.shape[0]),
            transcendentals=0,
            bytes_accessed=cap * (width * 2 + 4) + 2 * n_tgt * (width + acc_cnt.shape[0]) * 4,
        ),
    )(targets, rec_t, acc_sum, acc_cnt)


def _shift_pairs(n, shift):
    return [(i, (i + shift) % n) for i in range(n)]


def _xor_pairs(n, bit):
    return [(i, i ^ bit) for i in range(n)]


def _is_pow2(n):
    return n & (n - 1) == 0


def reduce_scatter_blocks(x, axis, n, send_dtype, high_first=False):
    if not _is_pow2(n):
        got = lax.all_to_all(x.astype(send_dtype), axis, 0, 0, tiled=True)
        return jnp.sum(got.astype(x.dtype), axis=0)
    k = n.bit_length() - 1
    axis_bits = list(reversed(range(k)))
    order = axis_bits[:] if high_first else list(range(k))
    return _butterfly_reduce(
        x.reshape((2,) * k + x.shape[1:]), axis, n, axis_bits, order, send_dtype
    )


def _butterfly_reduce(cur, axis, n, axis_bits, order, send_dtype):
    me = lax.axis_index(axis)
    axis_bits = list(axis_bits)
    for b in order:
        ax = axis_bits.index(b)
        axis_bits.remove(b)
        mine = (me >> b) & 1
        keep = lax.dynamic_index_in_dim(cur, mine, axis=ax, keepdims=False)
        send = lax.dynamic_index_in_dim(cur, 1 - mine, axis=ax, keepdims=False)
        got = lax.ppermute(send.astype(send_dtype), axis, _xor_pairs(n, 1 << b))
        cur = keep + got.astype(keep.dtype)
    return cur


def reduce_scatter_grid(x, n_dom, n_cols, send_dtype):
    if not (_is_pow2(n_dom) and _is_pow2(n_cols)):
        part = reduce_scatter_blocks(x, "cols", n_cols, send_dtype)
        return reduce_scatter_blocks(part, "dom", n_dom, send_dtype)
    kc = n_cols.bit_length() - 1
    kd = n_dom.bit_length() - 1
    axis_bits = [kc - 1 - i for i in range(kc)] + [kc + kd - 1 - i for i in range(kd)]
    order = list(range(min(kc, 1))) + list(range(kc, kc + kd)) + list(range(1, kc))
    cur = x.reshape((2,) * (kc + kd) + x.shape[2:])
    return _butterfly_reduce(
        cur, ("dom", "cols"), n_dom * n_cols, axis_bits, order, send_dtype
    )


def all_gather_blocks(x, axis, n):
    if not _is_pow2(n):
        return lax.all_gather(x, axis, axis=0, tiled=False)
    me = lax.axis_index(axis)
    k = n.bit_length() - 1
    cur = x
    for b in reversed(range(k)):
        mine = (me >> b) & 1
        got = lax.ppermute(cur, axis, _xor_pairs(n, 1 << b))
        low = jnp.where(mine == 0, cur, got)
        high = jnp.where(mine == 0, got, cur)
        cur = jnp.stack([low, high], axis=k - 1 - b)
    return cur.reshape((n,) + x.shape)


def local(
    features,
    edge_source,
    edge_target,
    neigh_weight,
    self_weight,
    bias_one,
    upper_weight,
    bias_two,
    upper_neighbours,
    out_cotangent,
):
    n_dom = lax.axis_size("dom")
    n_cols = lax.axis_size("cols")
    capacity = edge_source.shape[2]
    width = features.shape[1]
    hidden = upper_weight.shape[1]
    tgt_loc = upper_neighbours.shape[0]
    tgt_dev = tgt_loc * n_cols
    w_rows = neigh_weight.shape[0]
    up_rows = upper_weight.shape[0]

    packed = jnp.concatenate([neigh_weight, self_weight], axis=0)
    gathered = lax.all_gather(packed, "cols", axis=0, tiled=False)
    neigh_full = gathered[:, :w_rows]
    self_full = gathered[:, w_rows:]
    full_upper = lax.all_gather(upper_weight, "cols", axis=0, tiled=True)

    me_dom = lax.axis_index("dom")
    me_col = lax.axis_index("cols")
    own_t = features[:tgt_dev].T
    own_pre = bias_one
    for shift in range(n_cols):
        dest = (me_col + shift) % n_cols
        src = (me_col - shift) % n_cols
        chunk = lax.dynamic_slice_in_dim(own_t, dest * tgt_loc, tgt_loc, axis=1)
        if shift:
            chunk = lax.ppermute(chunk, "cols", _shift_pairs(n_cols, shift))
        weight = lax.dynamic_index_in_dim(self_full, src, 0, keepdims=False)
        own_pre = own_pre + contract_rows(chunk, weight)

    summed_t = jnp.zeros((width, tgt_dev), jnp.float32)
    counts = jnp.zeros((8, tgt_dev), jnp.float32)
    for shift in range(n_dom):
        dest = (me_dom + shift) % n_dom
        src = (me_dom - shift) % n_dom
        slots = lax.dynamic_index_in_dim(edge_source[0], dest, 0, keepdims=False)
        rows_t = features.at[slots].get(mode="promise_in_bounds").T
        if shift:
            rows_t = lax.ppermute(rows_t, "dom", _shift_pairs(n_dom, shift))
        targets = lax.dynamic_index_in_dim(edge_target[0], src, 0, keepdims=True)
        summed_t, counts = accumulate(targets, rows_t, summed_t, counts)
    mean_t = (summed_t / jnp.maximum(counts[:1], 1.0)).astype(jnp.bfloat16)
    both_t = jnp.concatenate([mean_t, own_t], axis=0)

    pre_one = own_pre
    for shift in range(n_cols):
        dest = (me_col + shift) % n_cols
        src = (me_col - shift) % n_cols
        chunk = lax.dynamic_slice_in_dim(mean_t, dest * tgt_loc, tgt_loc, axis=1)
        if shift:
            chunk = lax.ppermute(chunk, "cols", _shift_pairs(n_cols, shift))
        weight = lax.dynamic_index_in_dim(neigh_full, src, 0, keepdims=False)
        pre_one = pre_one + contract_rows(chunk, weight)
    hidden_one = jax.nn.silu(pre_one).astype(jnp.bfloat16)
    mix_matrix = mixing(upper_neighbours, tgt_loc)
    upper_input = jnp.dot(
        mix_matrix, hidden_one.astype(jnp.float32), precision=lax.Precision.HIGHEST
    ).astype(jnp.bfloat16)
    pre_two = jnp.dot(upper_input, full_upper, preferred_element_type=jnp.float32) + bias_two
    hidden_two = jax.nn.silu(pre_two).astype(jnp.bfloat16)
    slope_two = (out_cotangent.astype(jnp.float32) * swish_slope(pre_two)).astype(jnp.bfloat16)

    local_grad = contract_rows(upper_input, slope_two)
    dom_rows = up_rows // n_dom
    upper_part = reduce_scatter_grid(
        local_grad.reshape(n_cols, n_dom, dom_rows, hidden), n_dom, n_cols, jnp.bfloat16
    )
    back_mixed = lax.dot_general(
        slope_two, full_upper, (((1,), (1,)), ((), ())), preferred_element_type=jnp.float32
    )
    back_one = jnp.dot(mix_matrix.T, back_mixed, precision=lax.Precision.HIGHEST)
    slope_one = (back_one * swish_slope(pre_one)).astype(jnp.bfloat16)
    slab_rows = all_gather_blocks(slope_one, "cols", n_cols).reshape(tgt_dev, hidden)
    stacked = jnp.dot(both_t, slab_rows, preferred_element_type=jnp.float32)
    dom_cols = hidden // n_dom
    grad_upper = all_gather_blocks(upper_part.astype(jnp.bfloat16), "dom", n_dom)
    grad_upper = grad_upper.reshape(up_rows, hidden).astype(jnp.float32)
    grad_layer = lax.psum_scatter(
        stacked.astype(jnp.bfloat16), "dom", scatter_dimension=1, tiled=True
    ).astype(jnp.float32)
    grad_neigh = grad_layer[:w_rows]
    grad_self = grad_layer[w_rows:]
    return (hidden_two, grad_neigh, grad_self, grad_upper)


def solution(mesh):
    in_specs = (
        P(("groups", "dom"), "cols"),
        P(("groups", "dom"), None, None),
        P(("groups", "dom"), None, None),
        P("cols", None),
        P("cols", None),
        P(),
        P("cols", None),
        P(),
        P(("groups", "dom", "cols"), None),
        P(("groups", "dom", "cols"), None),
    )
    out_specs = (
        P(("groups", "dom", "cols"), None),
        P(("groups", "cols"), "dom"),
        P(("groups", "cols"), "dom"),
        P(("groups", "cols"), None),
    )
    return jax.shard_map(local, mesh=mesh, in_specs=in_specs, out_specs=out_specs, check_vma=False)
```

```python
import jax
import jax.numpy as jnp
from jax import lax
from jax.experimental import pallas as pl
from jax.experimental.pallas import tpu as pltpu
from jax.sharding import PartitionSpec as P


def swish_slope(preact):
    gate_val = jax.nn.sigmoid(preact)
    return gate_val * (1.0 + preact * (1.0 - gate_val))


def mixing(neighbours, block_len):
    positions = jnp.arange(block_len, dtype=jnp.int32)
    neighbour_hits = jnp.sum(
        (neighbours[:, :, None] == positions[None, None, :]).astype(jnp.float32), axis=1
    )
    return (jnp.eye(block_len, dtype=jnp.float32) + neighbour_hits) / (neighbours.shape[1] + 1.0)


def contract_rows(left_mat, right_mat):
    return lax.dot_general(
        left_mat, right_mat, (((0,), (0,)), ((), ())), preferred_element_type=jnp.float32
    )


def _accumulate_kernel(tgt_ref, rec_ref, sum_in, cnt_in, sum_ref, cnt_ref):
    targets = tgt_ref[...]
    n_tgt = sum_ref.shape[1]
    rows = lax.broadcasted_iota(jnp.int32, (n_tgt, targets.shape[1]), 0)
    hot = (rows == targets).astype(jnp.bfloat16)
    dims = (((1,), (1,)), ((), ()))
    sum_ref[...] = sum_in[...] + lax.dot_general(
        rec_ref[...], hot, dims, preferred_element_type=jnp.float32
    )
    ones = jnp.ones((cnt_ref.shape[0], targets.shape[1]), jnp.bfloat16)
    cnt_ref[...] = cnt_in[...] + lax.dot_general(
        ones, hot, dims, preferred_element_type=jnp.float32
    )


def accumulate(targets, rec_t, acc_sum, acc_cnt):
    width, cap = rec_t.shape
    n_tgt = acc_sum.shape[1]
    return pl.pallas_call(
        _accumulate_kernel,
        out_shape=[
            jax.ShapeDtypeStruct(acc_sum.shape, jnp.float32),
            jax.ShapeDtypeStruct(acc_cnt.shape, jnp.float32),
        ],
        input_output_aliases={2: 0, 3: 1},
        cost_estimate=pl.CostEstimate(
            flops=2 * n_tgt * cap * (width + acc_cnt.shape[0]),
            transcendentals=0,
            bytes_accessed=cap * (width * 2 + 4) + 2 * n_tgt * (width + acc_cnt.shape[0]) * 4,
        ),
    )(targets, rec_t, acc_sum, acc_cnt)


def _shift_pairs(n, shift):
    return [(i, (i + shift) % n) for i in range(n)]


def _xor_pairs(n, bit):
    return [(i, i ^ bit) for i in range(n)]


def _is_pow2(n):
    return n & (n - 1) == 0


def reduce_scatter_blocks(x, axis, n, send_dtype, high_first=False):
    if not _is_pow2(n):
        got = lax.all_to_all(x.astype(send_dtype), axis, 0, 0, tiled=True)
        return jnp.sum(got.astype(x.dtype), axis=0)
    k = n.bit_length() - 1
    axis_bits = list(reversed(range(k)))
    order = axis_bits[:] if high_first else list(range(k))
    return _butterfly_reduce(
        x.reshape((2,) * k + x.shape[1:]), axis, n, axis_bits, order, send_dtype
    )


def _butterfly_reduce(cur, axis, n, axis_bits, order, send_dtype):
    me = lax.axis_index(axis)
    axis_bits = list(axis_bits)
    for b in order:
        ax = axis_bits.index(b)
        axis_bits.remove(b)
        mine = (me >> b) & 1
        keep = lax.dynamic_index_in_dim(cur, mine, axis=ax, keepdims=False)
        send = lax.dynamic_index_in_dim(cur, 1 - mine, axis=ax, keepdims=False)
        got = lax.ppermute(send.astype(send_dtype), axis, _xor_pairs(n, 1 << b))
        cur = keep + got.astype(keep.dtype)
    return cur


def reduce_scatter_grid(x, n_dom, n_cols, send_dtype, carried):
    if not (_is_pow2(n_dom) and _is_pow2(n_cols)):
        part = reduce_scatter_blocks(x, "cols", n_cols, send_dtype)
        return reduce_scatter_blocks(part, "dom", n_dom, send_dtype), carried
    kc = n_cols.bit_length() - 1
    kd = n_dom.bit_length() - 1
    axis_bits = [kc - 1 - i for i in range(kc)] + [kc + kd - 1 - i for i in range(kd)]
    order = list(range(min(kc, 1))) + list(range(kc, kc + kd)) + list(range(1, kc))
    cur = x.reshape((2,) * (kc + kd) + x.shape[2:])
    axes = ("dom", "cols")
    n = n_dom * n_cols
    cur = _butterfly_reduce(cur, axes, n, axis_bits, order[:1], send_dtype)
    cur, carried = lax.optimization_barrier((cur, carried))
    rest = [b for b in axis_bits if b != order[0]]
    return _butterfly_reduce(cur, axes, n, rest, order[1:], send_dtype), carried


def all_gather_blocks(x, axis, n):
    if not _is_pow2(n):
        return lax.all_gather(x, axis, axis=0, tiled=False)
    me = lax.axis_index(axis)
    k = n.bit_length() - 1
    cur = x
    for b in reversed(range(k)):
        mine = (me >> b) & 1
        got = lax.ppermute(cur, axis, _xor_pairs(n, 1 << b))
        low = jnp.where(mine == 0, cur, got)
        high = jnp.where(mine == 0, got, cur)
        cur = jnp.stack([low, high], axis=k - 1 - b)
    return cur.reshape((n,) + x.shape)


def local(
    features,
    edge_source,
    edge_target,
    neigh_weight,
    self_weight,
    bias_one,
    upper_weight,
    bias_two,
    upper_neighbours,
    out_cotangent,
):
    n_dom = lax.axis_size("dom")
    n_cols = lax.axis_size("cols")
    capacity = edge_source.shape[2]
    width = features.shape[1]
    hidden = upper_weight.shape[1]
    tgt_loc = upper_neighbours.shape[0]
    tgt_dev = tgt_loc * n_cols
    w_rows = neigh_weight.shape[0]
    up_rows = upper_weight.shape[0]

    packed = jnp.concatenate([neigh_weight, self_weight], axis=0)
    gathered = lax.all_gather(packed, "cols", axis=0, tiled=False)
    neigh_full = gathered[:, :w_rows]
    self_full = gathered[:, w_rows:]
    full_upper = lax.all_gather(upper_weight, "cols", axis=0, tiled=True)

    me_dom = lax.axis_index("dom")
    me_col = lax.axis_index("cols")
    own_t = features[:tgt_dev].T
    own_pre = bias_one
    for shift in range(n_cols):
        dest = (me_col + shift) % n_cols
        src = (me_col - shift) % n_cols
        chunk = lax.dynamic_slice_in_dim(own_t, dest * tgt_loc, tgt_loc, axis=1)
        if shift:
            chunk = lax.ppermute(chunk, "cols", _shift_pairs(n_cols, shift))
        weight = lax.dynamic_index_in_dim(self_full, src, 0, keepdims=False)
        own_pre = own_pre + contract_rows(chunk, weight)

    summed_t = jnp.zeros((width, tgt_dev), jnp.float32)
    counts = jnp.zeros((8, tgt_dev), jnp.float32)
    for shift in range(n_dom):
        dest = (me_dom + shift) % n_dom
        src = (me_dom - shift) % n_dom
        slots = lax.dynamic_index_in_dim(edge_source[0], dest, 0, keepdims=False)
        rows_t = features.at[slots].get(mode="promise_in_bounds").T
        if shift:
            rows_t = lax.ppermute(rows_t, "dom", _shift_pairs(n_dom, shift))
        targets = lax.dynamic_index_in_dim(edge_target[0], src, 0, keepdims=True)
        summed_t, counts = accumulate(targets, rows_t, summed_t, counts)
    mean_t = (summed_t / jnp.maximum(counts[:1], 1.0)).astype(jnp.bfloat16)
    both_t = jnp.concatenate([mean_t, own_t], axis=0)

    pre_one = own_pre
    for shift in range(n_cols):
        dest = (me_col + shift) % n_cols
        src = (me_col - shift) % n_cols
        chunk = lax.dynamic_slice_in_dim(mean_t, dest * tgt_loc, tgt_loc, axis=1)
        if shift:
            chunk = lax.ppermute(chunk, "cols", _shift_pairs(n_cols, shift))
        weight = lax.dynamic_index_in_dim(neigh_full, src, 0, keepdims=False)
        pre_one = pre_one + contract_rows(chunk, weight)
    hidden_one = jax.nn.silu(pre_one).astype(jnp.bfloat16)
    mix_matrix = mixing(upper_neighbours, tgt_loc)
    upper_input = jnp.dot(
        mix_matrix, hidden_one.astype(jnp.float32), precision=lax.Precision.HIGHEST
    ).astype(jnp.bfloat16)
    pre_two = jnp.dot(upper_input, full_upper, preferred_element_type=jnp.float32) + bias_two
    hidden_two = jax.nn.silu(pre_two).astype(jnp.bfloat16)
    slope_two = (out_cotangent.astype(jnp.float32) * swish_slope(pre_two)).astype(jnp.bfloat16)

    local_grad = contract_rows(upper_input, slope_two)
    back_mixed = lax.dot_general(
        slope_two, full_upper, (((1,), (1,)), ((), ())), preferred_element_type=jnp.float32
    )
    back_one = jnp.dot(mix_matrix.T, back_mixed, precision=lax.Precision.HIGHEST)
    slope_one = (back_one * swish_slope(pre_one)).astype(jnp.bfloat16)
    dom_rows = up_rows // n_dom
    upper_part, slope_one = reduce_scatter_grid(
        local_grad.reshape(n_cols, n_dom, dom_rows, hidden),
        n_dom,
        n_cols,
        jnp.bfloat16,
        slope_one,
    )
    slab_rows = all_gather_blocks(slope_one, "cols", n_cols).reshape(tgt_dev, hidden)
    stacked = jnp.dot(both_t, slab_rows, preferred_element_type=jnp.float32)
    dom_cols = hidden // n_dom
    grad_upper = all_gather_blocks(upper_part.astype(jnp.bfloat16), "dom", n_dom)
    grad_upper = grad_upper.reshape(up_rows, hidden).astype(jnp.float32)
    grad_layer = lax.psum_scatter(
        stacked.astype(jnp.bfloat16), "dom", scatter_dimension=1, tiled=True
    ).astype(jnp.float32)
    grad_neigh = grad_layer[:w_rows]
    grad_self = grad_layer[w_rows:]
    return (hidden_two, grad_neigh, grad_self, grad_upper)


def solution(mesh):
    in_specs = (
        P(("groups", "dom"), "cols"),
        P(("groups", "dom"), None, None),
        P(("groups", "dom"), None, None),
        P("cols", None),
        P("cols", None),
        P(),
        P("cols", None),
        P(),
        P(("groups", "dom", "cols"), None),
        P(("groups", "dom", "cols"), None),
    )
    out_specs = (
        P(("groups", "dom", "cols"), None),
        P(("groups", "cols"), "dom"),
        P(("groups", "cols"), "dom"),
        P(("groups", "cols"), None),
    )
    return jax.shard_map(local, mesh=mesh, in_specs=in_specs, out_specs=out_specs, check_vma=False)
```

```python
import jax
import jax.numpy as jnp
from jax import lax
from jax.experimental import pallas as pl
from jax.experimental.pallas import tpu as pltpu
from jax.sharding import PartitionSpec as P


def swish_slope(preact):
    gate_val = jax.nn.sigmoid(preact)
    return gate_val * (1.0 + preact * (1.0 - gate_val))


def mixing(neighbours, block_len):
    positions = jnp.arange(block_len, dtype=jnp.int32)
    neighbour_hits = jnp.sum(
        (neighbours[:, :, None] == positions[None, None, :]).astype(jnp.float32), axis=1
    )
    return (jnp.eye(block_len, dtype=jnp.float32) + neighbour_hits) / (neighbours.shape[1] + 1.0)


def contract_rows(left_mat, right_mat):
    return lax.dot_general(
        left_mat, right_mat, (((0,), (0,)), ((), ())), preferred_element_type=jnp.float32
    )


def _accumulate_kernel(tgt_ref, rec_ref, sum_in, cnt_in, sum_ref, cnt_ref):
    targets = tgt_ref[...]
    n_tgt = sum_ref.shape[1]
    rows = lax.broadcasted_iota(jnp.int32, (n_tgt, targets.shape[1]), 0)
    hot = (rows == targets).astype(jnp.bfloat16)
    dims = (((1,), (1,)), ((), ()))
    sum_ref[...] = sum_in[...] + lax.dot_general(
        rec_ref[...], hot, dims, preferred_element_type=jnp.float32
    )
    ones = jnp.ones((cnt_ref.shape[0], targets.shape[1]), jnp.bfloat16)
    cnt_ref[...] = cnt_in[...] + lax.dot_general(
        ones, hot, dims, preferred_element_type=jnp.float32
    )


def accumulate(targets, rec_t, acc_sum, acc_cnt):
    width, cap = rec_t.shape
    n_tgt = acc_sum.shape[1]
    return pl.pallas_call(
        _accumulate_kernel,
        out_shape=[
            jax.ShapeDtypeStruct(acc_sum.shape, jnp.float32),
            jax.ShapeDtypeStruct(acc_cnt.shape, jnp.float32),
        ],
        input_output_aliases={2: 0, 3: 1},
        cost_estimate=pl.CostEstimate(
            flops=2 * n_tgt * cap * (width + acc_cnt.shape[0]),
            transcendentals=0,
            bytes_accessed=cap * (width * 2 + 4) + 2 * n_tgt * (width + acc_cnt.shape[0]) * 4,
        ),
    )(targets, rec_t, acc_sum, acc_cnt)


def _shift_pairs(n, shift):
    return [(i, (i + shift) % n) for i in range(n)]


def _xor_pairs(n, bit):
    return [(i, i ^ bit) for i in range(n)]


def _is_pow2(n):
    return n & (n - 1) == 0


def reduce_scatter_blocks(x, axis, n, send_dtype, high_first=False):
    if not _is_pow2(n):
        got = lax.all_to_all(x.astype(send_dtype), axis, 0, 0, tiled=True)
        return jnp.sum(got.astype(x.dtype), axis=0)
    k = n.bit_length() - 1
    axis_bits = list(reversed(range(k)))
    order = axis_bits[:] if high_first else list(range(k))
    return _butterfly_reduce(
        x.reshape((2,) * k + x.shape[1:]), axis, n, axis_bits, order, send_dtype
    )


def _butterfly_reduce(cur, axis, n, axis_bits, order, send_dtype):
    me = lax.axis_index(axis)
    axis_bits = list(axis_bits)
    for b in order:
        ax = axis_bits.index(b)
        axis_bits.remove(b)
        mine = (me >> b) & 1
        keep = lax.dynamic_index_in_dim(cur, mine, axis=ax, keepdims=False)
        send = lax.dynamic_index_in_dim(cur, 1 - mine, axis=ax, keepdims=False)
        got = lax.ppermute(send.astype(send_dtype), axis, _xor_pairs(n, 1 << b))
        cur = keep + got.astype(keep.dtype)
    return cur


def reduce_scatter_grid(x, n_dom, n_cols, send_dtype, carried):
    if not (_is_pow2(n_dom) and _is_pow2(n_cols)):
        part = reduce_scatter_blocks(x, "cols", n_cols, send_dtype)
        return reduce_scatter_blocks(part, "dom", n_dom, send_dtype), carried
    kc = n_cols.bit_length() - 1
    kd = n_dom.bit_length() - 1
    axis_bits = [kc - 1 - i for i in range(kc)] + [kc + kd - 1 - i for i in range(kd)]
    order = list(range(min(kc, 1))) + list(range(kc, kc + kd)) + list(range(1, kc))
    cur = x.reshape((2,) * (kc + kd) + x.shape[2:])
    axes = ("dom", "cols")
    n = n_dom * n_cols
    cur = _butterfly_reduce(cur, axes, n, axis_bits, order[:1], send_dtype)
    cur, carried = lax.optimization_barrier((cur, carried))
    rest = [b for b in axis_bits if b != order[0]]
    return _butterfly_reduce(cur, axes, n, rest, order[1:], send_dtype), carried


def all_gather_blocks(x, axis, n):
    if not _is_pow2(n):
        return jax.tree.map(lambda leaf: lax.all_gather(leaf, axis, axis=0, tiled=False), x)
    me = lax.axis_index(axis)
    k = n.bit_length() - 1
    cur = x
    for b in reversed(range(k)):
        mine = (me >> b) & 1
        got = lax.ppermute(cur, axis, _xor_pairs(n, 1 << b))

        def join(held, came, b=b, mine=mine):
            low = jnp.where(mine == 0, held, came)
            high = jnp.where(mine == 0, came, held)
            return jnp.stack([low, high], axis=k - 1 - b)

        cur = jax.tree.map(join, cur, got)
    return jax.tree.map(lambda leaf, orig: leaf.reshape((n,) + orig.shape), cur, x)


def local(
    features,
    edge_source,
    edge_target,
    neigh_weight,
    self_weight,
    bias_one,
    upper_weight,
    bias_two,
    upper_neighbours,
    out_cotangent,
):
    n_dom = lax.axis_size("dom")
    n_cols = lax.axis_size("cols")
    capacity = edge_source.shape[2]
    width = features.shape[1]
    hidden = upper_weight.shape[1]
    tgt_loc = upper_neighbours.shape[0]
    tgt_dev = tgt_loc * n_cols
    w_rows = neigh_weight.shape[0]
    up_rows = upper_weight.shape[0]

    neigh_full, self_full, full_upper = all_gather_blocks(
        (neigh_weight, self_weight, upper_weight), "cols", n_cols
    )
    full_upper = full_upper.reshape(n_cols * up_rows, hidden)

    me_dom = lax.axis_index("dom")
    me_col = lax.axis_index("cols")
    own_t = features[:tgt_dev].T
    own_pre = bias_one
    for shift in range(n_cols):
        dest = (me_col + shift) % n_cols
        src = (me_col - shift) % n_cols
        chunk = lax.dynamic_slice_in_dim(own_t, dest * tgt_loc, tgt_loc, axis=1)
        if shift:
            chunk = lax.ppermute(chunk, "cols", _shift_pairs(n_cols, shift))
        weight = lax.dynamic_index_in_dim(self_full, src, 0, keepdims=False)
        own_pre = own_pre + contract_rows(chunk, weight)

    summed_t = jnp.zeros((width, tgt_dev), jnp.float32)
    counts = jnp.zeros((8, tgt_dev), jnp.float32)
    for shift in range(n_dom):
        dest = (me_dom + shift) % n_dom
        src = (me_dom - shift) % n_dom
        slots = lax.dynamic_index_in_dim(edge_source[0], dest, 0, keepdims=False)
        rows_t = features.at[slots].get(mode="promise_in_bounds").T
        if shift:
            rows_t = lax.ppermute(rows_t, "dom", _shift_pairs(n_dom, shift))
        targets = lax.dynamic_index_in_dim(edge_target[0], src, 0, keepdims=True)
        summed_t, counts = accumulate(targets, rows_t, summed_t, counts)
    mean_t = (summed_t / jnp.maximum(counts[:1], 1.0)).astype(jnp.bfloat16)
    both_t = jnp.concatenate([mean_t, own_t], axis=0)

    pre_one = own_pre
    for shift in range(n_cols):
        dest = (me_col + shift) % n_cols
        src = (me_col - shift) % n_cols
        chunk = lax.dynamic_slice_in_dim(mean_t, dest * tgt_loc, tgt_loc, axis=1)
        if shift:
            chunk = lax.ppermute(chunk, "cols", _shift_pairs(n_cols, shift))
        weight = lax.dynamic_index_in_dim(neigh_full, src, 0, keepdims=False)
        pre_one = pre_one + contract_rows(chunk, weight)
    hidden_one = jax.nn.silu(pre_one).astype(jnp.bfloat16)
    mix_matrix = mixing(upper_neighbours, tgt_loc)
    upper_input = jnp.dot(
        mix_matrix, hidden_one.astype(jnp.float32), precision=lax.Precision.HIGHEST
    ).astype(jnp.bfloat16)
    pre_two = jnp.dot(upper_input, full_upper, preferred_element_type=jnp.float32) + bias_two
    hidden_two = jax.nn.silu(pre_two).astype(jnp.bfloat16)
    slope_two = (out_cotangent.astype(jnp.float32) * swish_slope(pre_two)).astype(jnp.bfloat16)

    local_grad = contract_rows(upper_input, slope_two)
    back_mixed = lax.dot_general(
        slope_two, full_upper, (((1,), (1,)), ((), ())), preferred_element_type=jnp.float32
    )
    back_one = jnp.dot(mix_matrix.T, back_mixed, precision=lax.Precision.HIGHEST)
    slope_one = (back_one * swish_slope(pre_one)).astype(jnp.bfloat16)
    dom_rows = up_rows // n_dom
    upper_part, slope_one = reduce_scatter_grid(
        local_grad.reshape(n_cols, n_dom, dom_rows, hidden),
        n_dom,
        n_cols,
        jnp.bfloat16,
        slope_one,
    )
    slab_rows = all_gather_blocks(slope_one, "cols", n_cols).reshape(tgt_dev, hidden)
    stacked = jnp.dot(both_t, slab_rows, preferred_element_type=jnp.float32)
    dom_cols = hidden // n_dom
    grad_upper = all_gather_blocks(upper_part.astype(jnp.bfloat16), "dom", n_dom)
    grad_upper = grad_upper.reshape(up_rows, hidden).astype(jnp.float32)
    grad_layer = reduce_scatter_blocks(
        jnp.swapaxes(stacked.reshape(2 * width, n_dom, dom_cols), 0, 1),
        "dom",
        n_dom,
        jnp.bfloat16,
    )
    grad_neigh = grad_layer[:w_rows]
    grad_self = grad_layer[w_rows:]
    return (hidden_two, grad_neigh, grad_self, grad_upper)


def solution(mesh):
    in_specs = (
        P(("groups", "dom"), "cols"),
        P(("groups", "dom"), None, None),
        P(("groups", "dom"), None, None),
        P("cols", None),
        P("cols", None),
        P(),
        P("cols", None),
        P(),
        P(("groups", "dom", "cols"), None),
        P(("groups", "dom", "cols"), None),
    )
    out_specs = (
        P(("groups", "dom", "cols"), None),
        P(("groups", "cols"), "dom"),
        P(("groups", "cols"), "dom"),
        P(("groups", "cols"), None),
    )
    return jax.shard_map(local, mesh=mesh, in_specs=in_specs, out_specs=out_specs, check_vma=False)
```

```python
import jax
import jax.numpy as jnp
from jax import lax
from jax.experimental import pallas as pl
from jax.experimental.pallas import tpu as pltpu
from jax.sharding import PartitionSpec as P


def swish_slope(preact):
    gate_val = jax.nn.sigmoid(preact)
    return gate_val * (1.0 + preact * (1.0 - gate_val))


def mixing(neighbours, block_len):
    positions = jnp.arange(block_len, dtype=jnp.int32)
    neighbour_hits = jnp.sum(
        (neighbours[:, :, None] == positions[None, None, :]).astype(jnp.float32), axis=1
    )
    return (jnp.eye(block_len, dtype=jnp.float32) + neighbour_hits) / (neighbours.shape[1] + 1.0)


def contract_rows(left_mat, right_mat):
    return lax.dot_general(
        left_mat, right_mat, (((0,), (0,)), ((), ())), preferred_element_type=jnp.float32
    )


def _accumulate_kernel(tgt_ref, rec_ref, sum_in, cnt_in, sum_ref, cnt_ref):
    targets = tgt_ref[...]
    n_tgt = sum_ref.shape[1]
    rows = lax.broadcasted_iota(jnp.int32, (n_tgt, targets.shape[1]), 0)
    hot = (rows == targets).astype(jnp.bfloat16)
    dims = (((1,), (1,)), ((), ()))
    sum_ref[...] = sum_in[...] + lax.dot_general(
        rec_ref[...], hot, dims, preferred_element_type=jnp.float32
    )
    ones = jnp.ones((cnt_ref.shape[0], targets.shape[1]), jnp.bfloat16)
    cnt_ref[...] = cnt_in[...] + lax.dot_general(
        ones, hot, dims, preferred_element_type=jnp.float32
    )


def accumulate(targets, rec_t, acc_sum, acc_cnt):
    width, cap = rec_t.shape
    n_tgt = acc_sum.shape[1]
    return pl.pallas_call(
        _accumulate_kernel,
        out_shape=[
            jax.ShapeDtypeStruct(acc_sum.shape, jnp.float32),
            jax.ShapeDtypeStruct(acc_cnt.shape, jnp.float32),
        ],
        input_output_aliases={2: 0, 3: 1},
        cost_estimate=pl.CostEstimate(
            flops=2 * n_tgt * cap * (width + acc_cnt.shape[0]),
            transcendentals=0,
            bytes_accessed=cap * (width * 2 + 4) + 2 * n_tgt * (width + acc_cnt.shape[0]) * 4,
        ),
    )(targets, rec_t, acc_sum, acc_cnt)


def _shift_pairs(n, shift):
    return [(i, (i + shift) % n) for i in range(n)]


def _xor_pairs(n, bit):
    return [(i, i ^ bit) for i in range(n)]


def _is_pow2(n):
    return n & (n - 1) == 0


def reduce_scatter_blocks(x, axis, n, send_dtype, high_first=False):
    if not _is_pow2(n):
        got = lax.all_to_all(x.astype(send_dtype), axis, 0, 0, tiled=True)
        return jnp.sum(got.astype(x.dtype), axis=0)
    k = n.bit_length() - 1
    axis_bits = list(reversed(range(k)))
    order = axis_bits[:] if high_first else list(range(k))
    return _butterfly_reduce(
        x.reshape((2,) * k + x.shape[1:]), axis, n, axis_bits, order, send_dtype
    )


def _butterfly_reduce(cur, axis, n, axis_bits, order, send_dtype):
    me = lax.axis_index(axis)
    axis_bits = list(axis_bits)
    for b in order:
        ax = axis_bits.index(b)
        axis_bits.remove(b)
        mine = (me >> b) & 1
        keep = lax.dynamic_index_in_dim(cur, mine, axis=ax, keepdims=False)
        send = lax.dynamic_index_in_dim(cur, 1 - mine, axis=ax, keepdims=False)
        got = lax.ppermute(send.astype(send_dtype), axis, _xor_pairs(n, 1 << b))
        cur = keep + got.astype(keep.dtype)
    return cur


def reduce_scatter_grid(x, n_dom, n_cols, send_dtype, carried):
    if not (_is_pow2(n_dom) and _is_pow2(n_cols)):
        part = reduce_scatter_blocks(x, "cols", n_cols, send_dtype)
        return reduce_scatter_blocks(part, "dom", n_dom, send_dtype), carried
    kc = n_cols.bit_length() - 1
    kd = n_dom.bit_length() - 1
    axis_bits = [kc - 1 - i for i in range(kc)] + [kc + kd - 1 - i for i in range(kd)]
    order = list(range(min(kc, 1))) + list(range(kc, kc + kd)) + list(range(1, kc))
    cur = x.reshape((2,) * (kc + kd) + x.shape[2:])
    axes = ("dom", "cols")
    n = n_dom * n_cols
    cur = _butterfly_reduce(cur, axes, n, axis_bits, order[:1], send_dtype)
    cur, carried = lax.optimization_barrier((cur, carried))
    rest = [b for b in axis_bits if b != order[0]]
    return _butterfly_reduce(cur, axes, n, rest, order[1:], send_dtype), carried


def all_gather_blocks(x, axis, n):
    if not _is_pow2(n):
        return jax.tree.map(lambda leaf: lax.all_gather(leaf, axis, axis=0, tiled=False), x)
    me = lax.axis_index(axis)
    k = n.bit_length() - 1
    cur = x
    for b in reversed(range(k)):
        mine = (me >> b) & 1
        got = lax.ppermute(cur, axis, _xor_pairs(n, 1 << b))

        def join(held, came, b=b, mine=mine):
            low = jnp.where(mine == 0, held, came)
            high = jnp.where(mine == 0, came, held)
            return jnp.stack([low, high], axis=k - 1 - b)

        cur = jax.tree.map(join, cur, got)
    return jax.tree.map(lambda leaf, orig: leaf.reshape((n,) + orig.shape), cur, x)


def local(
    features,
    edge_source,
    edge_target,
    neigh_weight,
    self_weight,
    bias_one,
    upper_weight,
    bias_two,
    upper_neighbours,
    out_cotangent,
):
    n_dom = lax.axis_size("dom")
    n_cols = lax.axis_size("cols")
    capacity = edge_source.shape[2]
    width = features.shape[1]
    hidden = upper_weight.shape[1]
    tgt_loc = upper_neighbours.shape[0]
    tgt_dev = tgt_loc * n_cols
    w_rows = neigh_weight.shape[0]
    up_rows = upper_weight.shape[0]

    me_dom = lax.axis_index("dom")
    me_col = lax.axis_index("cols")
    sent = []
    for shift in range(1, n_dom):
        dest = (me_dom + shift) % n_dom
        slots = lax.dynamic_index_in_dim(edge_source[0], dest, 0, keepdims=False)
        rows_t = features.at[slots].get(mode="promise_in_bounds").T
        if shift == 1:
            rows_t, weights, own_rows = lax.optimization_barrier(
                (rows_t, (neigh_weight, self_weight, upper_weight), features[:tgt_dev])
            )
        sent.append(lax.ppermute(rows_t, "dom", _shift_pairs(n_dom, shift)))
    neigh_full, self_full, full_upper = all_gather_blocks(weights, "cols", n_cols)
    full_upper = full_upper.reshape(n_cols * up_rows, hidden)
    own_t = own_rows.T
    own_pre = bias_one
    for shift in range(n_cols):
        dest = (me_col + shift) % n_cols
        src = (me_col - shift) % n_cols
        chunk = lax.dynamic_slice_in_dim(own_t, dest * tgt_loc, tgt_loc, axis=1)
        if shift:
            chunk = lax.ppermute(chunk, "cols", _shift_pairs(n_cols, shift))
        weight = lax.dynamic_index_in_dim(self_full, src, 0, keepdims=False)
        own_pre = own_pre + contract_rows(chunk, weight)

    summed_t = jnp.zeros((width, tgt_dev), jnp.float32)
    counts = jnp.zeros((8, tgt_dev), jnp.float32)
    for shift in range(n_dom):
        src = (me_dom - shift) % n_dom
        if shift:
            rows_t = sent[shift - 1]
        else:
            slots = lax.dynamic_index_in_dim(edge_source[0], me_dom, 0, keepdims=False)
            rows_t = features.at[slots].get(mode="promise_in_bounds").T
        targets = lax.dynamic_index_in_dim(edge_target[0], src, 0, keepdims=True)
        summed_t, counts = accumulate(targets, rows_t, summed_t, counts)
    mean_t = (summed_t / jnp.maximum(counts[:1], 1.0)).astype(jnp.bfloat16)
    both_t = jnp.concatenate([mean_t, own_t], axis=0)

    pre_one = own_pre
    for shift in range(n_cols):
        dest = (me_col + shift) % n_cols
        src = (me_col - shift) % n_cols
        chunk = lax.dynamic_slice_in_dim(mean_t, dest * tgt_loc, tgt_loc, axis=1)
        if shift:
            chunk = lax.ppermute(chunk, "cols", _shift_pairs(n_cols, shift))
        weight = lax.dynamic_index_in_dim(neigh_full, src, 0, keepdims=False)
        pre_one = pre_one + contract_rows(chunk, weight)
    hidden_one = jax.nn.silu(pre_one).astype(jnp.bfloat16)
    mix_matrix = mixing(upper_neighbours, tgt_loc)
    upper_input = jnp.dot(
        mix_matrix, hidden_one.astype(jnp.float32), precision=lax.Precision.HIGHEST
    ).astype(jnp.bfloat16)
    pre_two = jnp.dot(upper_input, full_upper, preferred_element_type=jnp.float32) + bias_two
    hidden_two = jax.nn.silu(pre_two).astype(jnp.bfloat16)
    slope_two = (out_cotangent.astype(jnp.float32) * swish_slope(pre_two)).astype(jnp.bfloat16)

    local_grad = contract_rows(upper_input, slope_two)
    back_mixed = lax.dot_general(
        slope_two, full_upper, (((1,), (1,)), ((), ())), preferred_element_type=jnp.float32
    )
    back_one = jnp.dot(mix_matrix.T, back_mixed, precision=lax.Precision.HIGHEST)
    slope_one = (back_one * swish_slope(pre_one)).astype(jnp.bfloat16)
    dom_rows = up_rows // n_dom
    upper_part, slope_one = reduce_scatter_grid(
        local_grad.reshape(n_cols, n_dom, dom_rows, hidden),
        n_dom,
        n_cols,
        jnp.bfloat16,
        slope_one,
    )
    slab_rows = all_gather_blocks(slope_one, "cols", n_cols).reshape(tgt_dev, hidden)
    stacked = jnp.dot(both_t, slab_rows, preferred_element_type=jnp.float32)
    dom_cols = hidden // n_dom
    grad_upper = all_gather_blocks(upper_part.astype(jnp.bfloat16), "dom", n_dom)
    grad_upper = grad_upper.reshape(up_rows, hidden).astype(jnp.float32)
    grad_layer = reduce_scatter_blocks(
        jnp.swapaxes(stacked.reshape(2 * width, n_dom, dom_cols), 0, 1),
        "dom",
        n_dom,
        jnp.bfloat16,
    )
    grad_neigh = grad_layer[:w_rows]
    grad_self = grad_layer[w_rows:]
    return (hidden_two, grad_neigh, grad_self, grad_upper)


def solution(mesh):
    in_specs = (
        P(("groups", "dom"), "cols"),
        P(("groups", "dom"), None, None),
        P(("groups", "dom"), None, None),
        P("cols", None),
        P("cols", None),
        P(),
        P("cols", None),
        P(),
        P(("groups", "dom", "cols"), None),
        P(("groups", "dom", "cols"), None),
    )
    out_specs = (
        P(("groups", "dom", "cols"), None),
        P(("groups", "cols"), "dom"),
        P(("groups", "cols"), "dom"),
        P(("groups", "cols"), None),
    )
    return jax.shard_map(local, mesh=mesh, in_specs=in_specs, out_specs=out_specs, check_vma=False)
```

```python
import jax
import jax.numpy as jnp
from jax import lax
from jax.experimental import pallas as pl
from jax.experimental.pallas import tpu as pltpu
from jax.sharding import PartitionSpec as P


def swish_slope(preact):
    gate_val = jax.nn.sigmoid(preact)
    return gate_val * (1.0 + preact * (1.0 - gate_val))


def mixing(neighbours, block_len):
    positions = jnp.arange(block_len, dtype=jnp.int32)
    neighbour_hits = jnp.sum(
        (neighbours[:, :, None] == positions[None, None, :]).astype(jnp.float32), axis=1
    )
    return (jnp.eye(block_len, dtype=jnp.float32) + neighbour_hits) / (neighbours.shape[1] + 1.0)


def contract_rows(left_mat, right_mat):
    return lax.dot_general(
        left_mat, right_mat, (((0,), (0,)), ((), ())), preferred_element_type=jnp.float32
    )


def _accumulate_kernel(tgt_ref, rec_ref, sum_in, cnt_in, sum_ref, cnt_ref):
    targets = tgt_ref[...]
    n_tgt = sum_ref.shape[1]
    rows = lax.broadcasted_iota(jnp.int32, (n_tgt, targets.shape[1]), 0)
    hot = (rows == targets).astype(jnp.bfloat16)
    dims = (((1,), (1,)), ((), ()))
    sum_ref[...] = sum_in[...] + lax.dot_general(
        rec_ref[...], hot, dims, preferred_element_type=jnp.float32
    )
    ones = jnp.ones((cnt_ref.shape[0], targets.shape[1]), jnp.bfloat16)
    cnt_ref[...] = cnt_in[...] + lax.dot_general(
        ones, hot, dims, preferred_element_type=jnp.float32
    )


def accumulate(targets, rec_t, acc_sum, acc_cnt):
    width, cap = rec_t.shape
    n_tgt = acc_sum.shape[1]
    return pl.pallas_call(
        _accumulate_kernel,
        out_shape=[
            jax.ShapeDtypeStruct(acc_sum.shape, jnp.float32),
            jax.ShapeDtypeStruct(acc_cnt.shape, jnp.float32),
        ],
        input_output_aliases={2: 0, 3: 1},
        cost_estimate=pl.CostEstimate(
            flops=2 * n_tgt * cap * (width + acc_cnt.shape[0]),
            transcendentals=0,
            bytes_accessed=cap * (width * 2 + 4) + 2 * n_tgt * (width + acc_cnt.shape[0]) * 4,
        ),
    )(targets, rec_t, acc_sum, acc_cnt)


def _shift_pairs(n, shift):
    return [(i, (i + shift) % n) for i in range(n)]


def _xor_pairs(n, bit):
    return [(i, i ^ bit) for i in range(n)]


def _is_pow2(n):
    return n & (n - 1) == 0


def reduce_scatter_blocks(x, axis, n, send_dtype, high_first=False):
    if not _is_pow2(n):
        got = lax.all_to_all(x.astype(send_dtype), axis, 0, 0, tiled=True)
        return jnp.sum(got.astype(x.dtype), axis=0)
    k = n.bit_length() - 1
    axis_bits = list(reversed(range(k)))
    order = axis_bits[:] if high_first else list(range(k))
    return _butterfly_reduce(
        x.reshape((2,) * k + x.shape[1:]), axis, n, axis_bits, order, send_dtype
    )


def _butterfly_reduce(cur, axis, n, axis_bits, order, send_dtype):
    me = lax.axis_index(axis)
    axis_bits = list(axis_bits)
    for b in order:
        ax = axis_bits.index(b)
        axis_bits.remove(b)
        mine = (me >> b) & 1
        keep = lax.dynamic_index_in_dim(cur, mine, axis=ax, keepdims=False)
        send = lax.dynamic_index_in_dim(cur, 1 - mine, axis=ax, keepdims=False)
        got = lax.ppermute(send.astype(send_dtype), axis, _xor_pairs(n, 1 << b))
        cur = keep + got.astype(keep.dtype)
    return cur


def reduce_scatter_grid(x, n_dom, n_cols, send_dtype, carried):
    if not (_is_pow2(n_dom) and _is_pow2(n_cols)):
        part = reduce_scatter_blocks(x, "cols", n_cols, send_dtype)
        return reduce_scatter_blocks(part, "dom", n_dom, send_dtype), carried
    kc = n_cols.bit_length() - 1
    kd = n_dom.bit_length() - 1
    axis_bits = [kc - 1 - i for i in range(kc)] + [kc + kd - 1 - i for i in range(kd)]
    order = list(range(min(kc, 1))) + list(range(kc, kc + kd)) + list(range(1, kc))
    cur = x.reshape((2,) * (kc + kd) + x.shape[2:])
    axes = ("dom", "cols")
    n = n_dom * n_cols
    cur = _butterfly_reduce(cur, axes, n, axis_bits, order[:1], send_dtype)
    cur, carried = lax.optimization_barrier((cur, carried))
    rest = [b for b in axis_bits if b != order[0]]
    return _butterfly_reduce(cur, axes, n, rest, order[1:], send_dtype), carried


def all_gather_blocks(x, axis, n):
    if not _is_pow2(n):
        return jax.tree.map(lambda leaf: lax.all_gather(leaf, axis, axis=0, tiled=False), x)
    me = lax.axis_index(axis)
    k = n.bit_length() - 1
    cur = x
    for b in reversed(range(k)):
        mine = (me >> b) & 1
        got = lax.ppermute(cur, axis, _xor_pairs(n, 1 << b))

        def join(held, came, b=b, mine=mine):
            low = jnp.where(mine == 0, held, came)
            high = jnp.where(mine == 0, came, held)
            return jnp.stack([low, high], axis=k - 1 - b)

        cur = jax.tree.map(join, cur, got)
    return jax.tree.map(lambda leaf, orig: leaf.reshape((n,) + orig.shape), cur, x)


def local(
    features,
    edge_source,
    edge_target,
    neigh_weight,
    self_weight,
    bias_one,
    upper_weight,
    bias_two,
    upper_neighbours,
    out_cotangent,
):
    n_dom = lax.axis_size("dom")
    n_cols = lax.axis_size("cols")
    capacity = edge_source.shape[2]
    width = features.shape[1]
    hidden = upper_weight.shape[1]
    tgt_loc = upper_neighbours.shape[0]
    tgt_dev = tgt_loc * n_cols
    w_rows = neigh_weight.shape[0]
    up_rows = upper_weight.shape[0]

    neigh_full, self_full, full_upper = all_gather_blocks(
        (neigh_weight, self_weight, upper_weight), "cols", n_cols
    )
    full_upper = full_upper.reshape(n_cols * up_rows, hidden)

    me_dom = lax.axis_index("dom")
    me_col = lax.axis_index("cols")
    own_t = features[:tgt_dev].T
    own_pre = bias_one
    for shift in range(n_cols):
        dest = (me_col + shift) % n_cols
        src = (me_col - shift) % n_cols
        chunk = lax.dynamic_slice_in_dim(own_t, dest * tgt_loc, tgt_loc, axis=1)
        if shift:
            chunk = lax.ppermute(chunk, "cols", _shift_pairs(n_cols, shift))
        weight = lax.dynamic_index_in_dim(self_full, src, 0, keepdims=False)
        own_pre = own_pre + contract_rows(chunk, weight)

    summed_t = jnp.zeros((width, tgt_dev), jnp.float32)
    counts = jnp.zeros((8, tgt_dev), jnp.float32)
    for shift in range(n_dom):
        dest = (me_dom + shift) % n_dom
        src = (me_dom - shift) % n_dom
        slots = lax.dynamic_index_in_dim(edge_source[0], dest, 0, keepdims=False)
        rows_t = features.at[slots].get(mode="promise_in_bounds").T
        if shift:
            rows_t = lax.ppermute(rows_t, "dom", _shift_pairs(n_dom, shift))
        targets = lax.dynamic_index_in_dim(edge_target[0], src, 0, keepdims=True)
        summed_t, counts = accumulate(targets, rows_t, summed_t, counts)
        if shift == min(1, n_dom - 1):
            summed_t, counts, neigh_full, full_upper = lax.optimization_barrier(
                (summed_t, counts, neigh_full, full_upper)
            )
    mean_t = (summed_t / jnp.maximum(counts[:1], 1.0)).astype(jnp.bfloat16)
    both_t = jnp.concatenate([mean_t, own_t], axis=0)

    pre_one = own_pre
    for shift in range(n_cols):
        dest = (me_col + shift) % n_cols
        src = (me_col - shift) % n_cols
        chunk = lax.dynamic_slice_in_dim(mean_t, dest * tgt_loc, tgt_loc, axis=1)
        if shift:
            chunk = lax.ppermute(chunk, "cols", _shift_pairs(n_cols, shift))
        weight = lax.dynamic_index_in_dim(neigh_full, src, 0, keepdims=False)
        pre_one = pre_one + contract_rows(chunk, weight)
    hidden_one = jax.nn.silu(pre_one).astype(jnp.bfloat16)
    mix_matrix = mixing(upper_neighbours, tgt_loc)
    upper_input = jnp.dot(
        mix_matrix, hidden_one.astype(jnp.float32), precision=lax.Precision.HIGHEST
    ).astype(jnp.bfloat16)
    pre_two = jnp.dot(upper_input, full_upper, preferred_element_type=jnp.float32) + bias_two
    hidden_two = jax.nn.silu(pre_two).astype(jnp.bfloat16)
    slope_two = (out_cotangent.astype(jnp.float32) * swish_slope(pre_two)).astype(jnp.bfloat16)

    local_grad = contract_rows(upper_input, slope_two)
    back_mixed = lax.dot_general(
        slope_two, full_upper, (((1,), (1,)), ((), ())), preferred_element_type=jnp.float32
    )
    back_one = jnp.dot(mix_matrix.T, back_mixed, precision=lax.Precision.HIGHEST)
    slope_one = (back_one * swish_slope(pre_one)).astype(jnp.bfloat16)
    dom_rows = up_rows // n_dom
    upper_part, slope_one = reduce_scatter_grid(
        local_grad.reshape(n_cols, n_dom, dom_rows, hidden),
        n_dom,
        n_cols,
        jnp.bfloat16,
        slope_one,
    )
    slab_rows = all_gather_blocks(slope_one, "cols", n_cols).reshape(tgt_dev, hidden)
    stacked = jnp.dot(both_t, slab_rows, preferred_element_type=jnp.float32)
    dom_cols = hidden // n_dom
    grad_upper = all_gather_blocks(upper_part.astype(jnp.bfloat16), "dom", n_dom)
    grad_upper = grad_upper.reshape(up_rows, hidden).astype(jnp.float32)
    grad_layer = reduce_scatter_blocks(
        jnp.swapaxes(stacked.reshape(2 * width, n_dom, dom_cols), 0, 1),
        "dom",
        n_dom,
        jnp.bfloat16,
    )
    grad_neigh = grad_layer[:w_rows]
    grad_self = grad_layer[w_rows:]
    return (hidden_two, grad_neigh, grad_self, grad_upper)


def solution(mesh):
    in_specs = (
        P(("groups", "dom"), "cols"),
        P(("groups", "dom"), None, None),
        P(("groups", "dom"), None, None),
        P("cols", None),
        P("cols", None),
        P(),
        P("cols", None),
        P(),
        P(("groups", "dom", "cols"), None),
        P(("groups", "dom", "cols"), None),
    )
    out_specs = (
        P(("groups", "dom", "cols"), None),
        P(("groups", "cols"), "dom"),
        P(("groups", "cols"), "dom"),
        P(("groups", "cols"), None),
    )
    return jax.shard_map(local, mesh=mesh, in_specs=in_specs, out_specs=out_specs, check_vma=False)
```

```python
import jax
import jax.numpy as jnp
from jax import lax
from jax.experimental import pallas as pl
from jax.experimental.pallas import tpu as pltpu
from jax.sharding import PartitionSpec as P


def swish_slope(preact):
    gate_val = jax.nn.sigmoid(preact)
    return gate_val * (1.0 + preact * (1.0 - gate_val))


def mixing(neighbours, block_len):
    positions = jnp.arange(block_len, dtype=jnp.int32)
    neighbour_hits = jnp.sum(
        (neighbours[:, :, None] == positions[None, None, :]).astype(jnp.float32), axis=1
    )
    return (jnp.eye(block_len, dtype=jnp.float32) + neighbour_hits) / (neighbours.shape[1] + 1.0)


def contract_rows(left_mat, right_mat):
    return lax.dot_general(
        left_mat, right_mat, (((0,), (0,)), ((), ())), preferred_element_type=jnp.float32
    )


def _accumulate_kernel(tgt_ref, rec_ref, sum_in, cnt_in, sum_ref, cnt_ref):
    targets = tgt_ref[...]
    n_tgt = sum_ref.shape[1]
    cols = lax.broadcasted_iota(jnp.int32, (targets.shape[0], n_tgt), 1)
    hot = (cols == targets).astype(jnp.bfloat16)
    sum_ref[...] = sum_in[...] + jnp.dot(
        rec_ref[...], hot, preferred_element_type=jnp.float32
    )
    ones = jnp.ones((cnt_ref.shape[0], targets.shape[0]), jnp.bfloat16)
    cnt_ref[...] = cnt_in[...] + jnp.dot(ones, hot, preferred_element_type=jnp.float32)


def accumulate(targets, rec_t, acc_sum, acc_cnt):
    width, cap = rec_t.shape
    assert targets.shape == (cap, 1)
    n_tgt = acc_sum.shape[1]
    return pl.pallas_call(
        _accumulate_kernel,
        out_shape=[
            jax.ShapeDtypeStruct(acc_sum.shape, jnp.float32),
            jax.ShapeDtypeStruct(acc_cnt.shape, jnp.float32),
        ],
        input_output_aliases={2: 0, 3: 1},
        cost_estimate=pl.CostEstimate(
            flops=2 * n_tgt * cap * (width + acc_cnt.shape[0]),
            transcendentals=0,
            bytes_accessed=cap * (width * 2 + 4) + 2 * n_tgt * (width + acc_cnt.shape[0]) * 4,
        ),
    )(targets, rec_t, acc_sum, acc_cnt)


def _shift_pairs(n, shift):
    return [(i, (i + shift) % n) for i in range(n)]


def _xor_pairs(n, bit):
    return [(i, i ^ bit) for i in range(n)]


def _is_pow2(n):
    return n & (n - 1) == 0


def reduce_scatter_blocks(x, axis, n, send_dtype, high_first=False):
    if not _is_pow2(n):
        got = lax.all_to_all(x.astype(send_dtype), axis, 0, 0, tiled=True)
        return jnp.sum(got.astype(x.dtype), axis=0)
    k = n.bit_length() - 1
    axis_bits = list(reversed(range(k)))
    order = axis_bits[:] if high_first else list(range(k))
    return _butterfly_reduce(
        x.reshape((2,) * k + x.shape[1:]), axis, n, axis_bits, order, send_dtype
    )


def _butterfly_reduce(cur, axis, n, axis_bits, order, send_dtype):
    me = lax.axis_index(axis)
    axis_bits = list(axis_bits)
    for b in order:
        ax = axis_bits.index(b)
        axis_bits.remove(b)
        mine = (me >> b) & 1
        keep = lax.dynamic_index_in_dim(cur, mine, axis=ax, keepdims=False)
        send = lax.dynamic_index_in_dim(cur, 1 - mine, axis=ax, keepdims=False)
        got = lax.ppermute(send.astype(send_dtype), axis, _xor_pairs(n, 1 << b))
        cur = keep + got.astype(keep.dtype)
    return cur


def reduce_scatter_grid(x, n_dom, n_cols, send_dtype, carried):
    if not (_is_pow2(n_dom) and _is_pow2(n_cols)):
        part = reduce_scatter_blocks(x, "cols", n_cols, send_dtype)
        return reduce_scatter_blocks(part, "dom", n_dom, send_dtype), carried
    kc = n_cols.bit_length() - 1
    kd = n_dom.bit_length() - 1
    axis_bits = [kc - 1 - i for i in range(kc)] + [kc + kd - 1 - i for i in range(kd)]
    order = list(range(min(kc, 1))) + list(range(kc, kc + kd)) + list(range(1, kc))
    cur = x.reshape((2,) * (kc + kd) + x.shape[2:])
    axes = ("dom", "cols")
    n = n_dom * n_cols
    cur = _butterfly_reduce(cur, axes, n, axis_bits, order[:1], send_dtype)
    cur, carried = lax.optimization_barrier((cur, carried))
    rest = [b for b in axis_bits if b != order[0]]
    return _butterfly_reduce(cur, axes, n, rest, order[1:], send_dtype), carried


def all_gather_blocks(x, axis, n):
    if not _is_pow2(n):
        return jax.tree.map(lambda leaf: lax.all_gather(leaf, axis, axis=0, tiled=False), x)
    me = lax.axis_index(axis)
    k = n.bit_length() - 1
    cur = x
    for b in reversed(range(k)):
        mine = (me >> b) & 1
        got = lax.ppermute(cur, axis, _xor_pairs(n, 1 << b))

        def join(held, came, b=b, mine=mine):
            low = jnp.where(mine == 0, held, came)
            high = jnp.where(mine == 0, came, held)
            return jnp.stack([low, high], axis=k - 1 - b)

        cur = jax.tree.map(join, cur, got)
    return jax.tree.map(lambda leaf, orig: leaf.reshape((n,) + orig.shape), cur, x)


def local(
    features,
    edge_source,
    edge_target,
    neigh_weight,
    self_weight,
    bias_one,
    upper_weight,
    bias_two,
    upper_neighbours,
    out_cotangent,
):
    n_dom = lax.axis_size("dom")
    n_cols = lax.axis_size("cols")
    capacity = edge_source.shape[2]
    width = features.shape[1]
    hidden = upper_weight.shape[1]
    tgt_loc = upper_neighbours.shape[0]
    tgt_dev = tgt_loc * n_cols
    w_rows = neigh_weight.shape[0]
    up_rows = upper_weight.shape[0]

    neigh_full, self_full, full_upper = all_gather_blocks(
        (neigh_weight, self_weight, upper_weight), "cols", n_cols
    )
    full_upper = full_upper.reshape(n_cols * up_rows, hidden)

    me_dom = lax.axis_index("dom")
    me_col = lax.axis_index("cols")
    own_t = features[:tgt_dev].T
    own_pre = bias_one
    for shift in range(n_cols):
        dest = (me_col + shift) % n_cols
        src = (me_col - shift) % n_cols
        chunk = lax.dynamic_slice_in_dim(own_t, dest * tgt_loc, tgt_loc, axis=1)
        if shift:
            chunk = lax.ppermute(chunk, "cols", _shift_pairs(n_cols, shift))
        weight = lax.dynamic_index_in_dim(self_full, src, 0, keepdims=False)
        own_pre = own_pre + contract_rows(chunk, weight)

    target_cols = edge_target[0].reshape(n_dom, capacity, 1)
    summed_t = jnp.zeros((width, tgt_dev), jnp.float32)
    counts = jnp.zeros((8, tgt_dev), jnp.float32)
    for shift in range(n_dom):
        dest = (me_dom + shift) % n_dom
        src = (me_dom - shift) % n_dom
        slots = lax.dynamic_index_in_dim(edge_source[0], dest, 0, keepdims=False)
        rows_t = features.at[slots].get(mode="promise_in_bounds").T
        if shift:
            rows_t = lax.ppermute(rows_t, "dom", _shift_pairs(n_dom, shift))
        targets = lax.dynamic_index_in_dim(target_cols, src, 0, keepdims=False)
        summed_t, counts = accumulate(targets, rows_t, summed_t, counts)
        if shift == min(1, n_dom - 1):
            summed_t, counts, neigh_full, full_upper = lax.optimization_barrier(
                (summed_t, counts, neigh_full, full_upper)
            )
    mean_t = (summed_t / jnp.maximum(counts[:1], 1.0)).astype(jnp.bfloat16)
    both_t = jnp.concatenate([mean_t, own_t], axis=0)

    pre_one = own_pre
    for shift in range(n_cols):
        dest = (me_col + shift) % n_cols
        src = (me_col - shift) % n_cols
        chunk = lax.dynamic_slice_in_dim(mean_t, dest * tgt_loc, tgt_loc, axis=1)
        if shift:
            chunk = lax.ppermute(chunk, "cols", _shift_pairs(n_cols, shift))
        weight = lax.dynamic_index_in_dim(neigh_full, src, 0, keepdims=False)
        pre_one = pre_one + contract_rows(chunk, weight)
    hidden_one = jax.nn.silu(pre_one).astype(jnp.bfloat16)
    mix_matrix = mixing(upper_neighbours, tgt_loc)
    upper_input = jnp.dot(
        mix_matrix, hidden_one.astype(jnp.float32), precision=lax.Precision.HIGHEST
    ).astype(jnp.bfloat16)
    pre_two = jnp.dot(upper_input, full_upper, preferred_element_type=jnp.float32) + bias_two
    hidden_two = jax.nn.silu(pre_two).astype(jnp.bfloat16)
    slope_two = (out_cotangent.astype(jnp.float32) * swish_slope(pre_two)).astype(jnp.bfloat16)

    local_grad = contract_rows(upper_input, slope_two)
    back_mixed = lax.dot_general(
        slope_two, full_upper, (((1,), (1,)), ((), ())), preferred_element_type=jnp.float32
    )
    back_one = jnp.dot(mix_matrix.T, back_mixed, precision=lax.Precision.HIGHEST)
    slope_one = (back_one * swish_slope(pre_one)).astype(jnp.bfloat16)
    dom_rows = up_rows // n_dom
    upper_part, slope_one = reduce_scatter_grid(
        local_grad.reshape(n_cols, n_dom, dom_rows, hidden),
        n_dom,
        n_cols,
        jnp.bfloat16,
        slope_one,
    )
    slab_rows = all_gather_blocks(slope_one, "cols", n_cols).reshape(tgt_dev, hidden)
    stacked = jnp.dot(both_t, slab_rows, preferred_element_type=jnp.float32)
    dom_cols = hidden // n_dom
    grad_upper = all_gather_blocks(upper_part.astype(jnp.bfloat16), "dom", n_dom)
    grad_upper = grad_upper.reshape(up_rows, hidden).astype(jnp.float32)
    grad_layer = reduce_scatter_blocks(
        jnp.swapaxes(stacked.reshape(2 * width, n_dom, dom_cols), 0, 1),
        "dom",
        n_dom,
        jnp.bfloat16,
    )
    grad_neigh = grad_layer[:w_rows]
    grad_self = grad_layer[w_rows:]
    return (hidden_two, grad_neigh, grad_self, grad_upper)


def solution(mesh):
    in_specs = (
        P(("groups", "dom"), "cols"),
        P(("groups", "dom"), None, None),
        P(("groups", "dom"), None, None),
        P("cols", None),
        P("cols", None),
        P(),
        P("cols", None),
        P(),
        P(("groups", "dom", "cols"), None),
        P(("groups", "dom", "cols"), None),
    )
    out_specs = (
        P(("groups", "dom", "cols"), None),
        P(("groups", "cols"), "dom"),
        P(("groups", "cols"), "dom"),
        P(("groups", "cols"), None),
    )
    return jax.shard_map(local, mesh=mesh, in_specs=in_specs, out_specs=out_specs, check_vma=False)
```

```python
import jax
import jax.numpy as jnp
from jax import lax
from jax.experimental import pallas as pl
from jax.experimental.pallas import tpu as pltpu
from jax.sharding import PartitionSpec as P


def swish_slope(preact):
    gate_val = jax.nn.sigmoid(preact)
    return gate_val * (1.0 + preact * (1.0 - gate_val))


def mixing(neighbours, block_len):
    positions = jnp.arange(block_len, dtype=jnp.int32)
    neighbour_hits = jnp.sum(
        (neighbours[:, :, None] == positions[None, None, :]).astype(jnp.float32), axis=1
    )
    return (jnp.eye(block_len, dtype=jnp.float32) + neighbour_hits) / (neighbours.shape[1] + 1.0)


def contract_rows(left_mat, right_mat):
    return lax.dot_general(
        left_mat, right_mat, (((0,), (0,)), ((), ())), preferred_element_type=jnp.float32
    )


def _accumulate_kernel(tgt_ref, rec_ref, sum_in, cnt_in, sum_ref, cnt_ref):
    targets = tgt_ref[...]
    n_tgt = sum_ref.shape[1]
    rows = lax.broadcasted_iota(jnp.int32, (n_tgt, targets.shape[1]), 0)
    hot = (rows == targets).astype(jnp.bfloat16)
    dims = (((1,), (1,)), ((), ()))
    sum_ref[...] = sum_in[...] + lax.dot_general(
        rec_ref[...], hot, dims, preferred_element_type=jnp.float32
    )
    ones = jnp.ones((cnt_ref.shape[0], targets.shape[1]), jnp.bfloat16)
    cnt_ref[...] = cnt_in[...] + lax.dot_general(
        ones, hot, dims, preferred_element_type=jnp.float32
    )


def accumulate(targets, rec_t, acc_sum, acc_cnt):
    width, cap = rec_t.shape
    n_tgt = acc_sum.shape[1]
    return pl.pallas_call(
        _accumulate_kernel,
        out_shape=[
            jax.ShapeDtypeStruct(acc_sum.shape, jnp.float32),
            jax.ShapeDtypeStruct(acc_cnt.shape, jnp.float32),
        ],
        input_output_aliases={2: 0, 3: 1},
        cost_estimate=pl.CostEstimate(
            flops=2 * n_tgt * cap * (width + acc_cnt.shape[0]),
            transcendentals=0,
            bytes_accessed=cap * (width * 2 + 4) + 2 * n_tgt * (width + acc_cnt.shape[0]) * 4,
        ),
    )(targets, rec_t, acc_sum, acc_cnt)


def _shift_pairs(n, shift):
    return [(i, (i + shift) % n) for i in range(n)]


def _xor_pairs(n, bit):
    return [(i, i ^ bit) for i in range(n)]


def _is_pow2(n):
    return n & (n - 1) == 0


def reduce_scatter_blocks(x, axis, n, send_dtype, high_first=False):
    if not _is_pow2(n):
        got = lax.all_to_all(x.astype(send_dtype), axis, 0, 0, tiled=True)
        return jnp.sum(got.astype(x.dtype), axis=0)
    k = n.bit_length() - 1
    axis_bits = list(reversed(range(k)))
    order = axis_bits[:] if high_first else list(range(k))
    return _butterfly_reduce(
        x.reshape((2,) * k + x.shape[1:]), axis, n, axis_bits, order, send_dtype
    )


def _butterfly_reduce(cur, axis, n, axis_bits, order, send_dtype):
    me = lax.axis_index(axis)
    axis_bits = list(axis_bits)
    for b in order:
        ax = axis_bits.index(b)
        axis_bits.remove(b)
        mine = (me >> b) & 1
        keep = lax.dynamic_index_in_dim(cur, mine, axis=ax, keepdims=False)
        send = lax.dynamic_index_in_dim(cur, 1 - mine, axis=ax, keepdims=False)
        got = lax.ppermute(send.astype(send_dtype), axis, _xor_pairs(n, 1 << b))
        cur = keep + got.astype(keep.dtype)
    return cur


def reduce_scatter_grid(x, n_dom, n_cols, send_dtype, carried):
    if not (_is_pow2(n_dom) and _is_pow2(n_cols)):
        part = reduce_scatter_blocks(x, "cols", n_cols, send_dtype)
        return reduce_scatter_blocks(part, "dom", n_dom, send_dtype), carried
    kc = n_cols.bit_length() - 1
    kd = n_dom.bit_length() - 1
    axis_bits = [kc - 1 - i for i in range(kc)] + [kc + kd - 1 - i for i in range(kd)]
    order = list(range(min(kc, 1))) + list(range(kc, kc + kd)) + list(range(1, kc))
    cur = x.reshape((2,) * (kc + kd) + x.shape[2:])
    axes = ("dom", "cols")
    n = n_dom * n_cols
    cur = _butterfly_reduce(cur, axes, n, axis_bits, order[:1], send_dtype)
    cur, carried = lax.optimization_barrier((cur, carried))
    rest = [b for b in axis_bits if b != order[0]]
    return _butterfly_reduce(cur, axes, n, rest, order[1:], send_dtype), carried


def all_gather_blocks(x, axis, n):
    if not _is_pow2(n):
        return jax.tree.map(lambda leaf: lax.all_gather(leaf, axis, axis=0, tiled=False), x)
    me = lax.axis_index(axis)
    k = n.bit_length() - 1
    cur = x
    for b in reversed(range(k)):
        mine = (me >> b) & 1
        got = lax.ppermute(cur, axis, _xor_pairs(n, 1 << b))

        def join(held, came, b=b, mine=mine):
            low = jnp.where(mine == 0, held, came)
            high = jnp.where(mine == 0, came, held)
            return jnp.stack([low, high], axis=k - 1 - b)

        cur = jax.tree.map(join, cur, got)
    return jax.tree.map(lambda leaf, orig: leaf.reshape((n,) + orig.shape), cur, x)


def gather_block_list(x, axis, n):
    held = {0: x}
    for b in reversed(range(n.bit_length() - 1)):
        keys = sorted(held)
        came = lax.ppermute(tuple(held[q] for q in keys), axis, _xor_pairs(n, 1 << b))
        for q, blocks in zip(keys, came):
            held[q | (1 << b)] = blocks
    return [held[q] for q in range(n)]


def local(
    features,
    edge_source,
    edge_target,
    neigh_weight,
    self_weight,
    bias_one,
    upper_weight,
    bias_two,
    upper_neighbours,
    out_cotangent,
):
    n_dom = lax.axis_size("dom")
    n_cols = lax.axis_size("cols")
    capacity = edge_source.shape[2]
    width = features.shape[1]
    hidden = upper_weight.shape[1]
    tgt_loc = upper_neighbours.shape[0]
    tgt_dev = tgt_loc * n_cols
    w_rows = neigh_weight.shape[0]
    up_rows = upper_weight.shape[0]

    me_dom = lax.axis_index("dom")
    me_col = lax.axis_index("cols")
    if _is_pow2(n_cols):
        layer_weights = gather_block_list((neigh_weight, self_weight), "cols", n_cols)
        full_upper = all_gather_blocks(upper_weight, "cols", n_cols)
        partners = [(me_col ^ j, me_col ^ j, _xor_pairs(n_cols, j)) for j in range(n_cols)]
    else:
        neigh_full, self_full, full_upper = all_gather_blocks(
            (neigh_weight, self_weight, upper_weight), "cols", n_cols
        )
        partners = [
            ((me_col + j) % n_cols, (me_col - j) % n_cols, _shift_pairs(n_cols, j))
            for j in range(n_cols)
        ]
        layer_weights = [
            tuple(
                lax.dynamic_index_in_dim(full, partners[j][1], 0, keepdims=False)
                for full in (neigh_full, self_full)
            )
            for j in range(n_cols)
        ]
    full_upper = full_upper.reshape(n_cols * up_rows, hidden)

    own_t = features[:tgt_dev].T
    own_pre = bias_one
    for j, (dest, src, pairs) in enumerate(partners):
        chunk = lax.dynamic_slice_in_dim(own_t, dest * tgt_loc, tgt_loc, axis=1)
        if j:
            chunk = lax.ppermute(chunk, "cols", pairs)
        own_pre = own_pre + contract_rows(chunk, layer_weights[j][1])

    summed_t = jnp.zeros((width, tgt_dev), jnp.float32)
    counts = jnp.zeros((8, tgt_dev), jnp.float32)
    for shift in range(n_dom):
        dest = (me_dom + shift) % n_dom
        src = (me_dom - shift) % n_dom
        slots = lax.dynamic_index_in_dim(edge_source[0], dest, 0, keepdims=False)
        rows_t = features.at[slots].get(mode="promise_in_bounds").T
        if shift:
            rows_t = lax.ppermute(rows_t, "dom", _shift_pairs(n_dom, shift))
        targets = lax.dynamic_index_in_dim(edge_target[0], src, 0, keepdims=True)
        summed_t, counts = accumulate(targets, rows_t, summed_t, counts)
    mean_t = (summed_t / jnp.maximum(counts[:1], 1.0)).astype(jnp.bfloat16)
    both_t = jnp.concatenate([mean_t, own_t], axis=0)

    pre_one = own_pre
    for j, (dest, src, pairs) in enumerate(partners):
        chunk = lax.dynamic_slice_in_dim(mean_t, dest * tgt_loc, tgt_loc, axis=1)
        if j:
            chunk = lax.ppermute(chunk, "cols", pairs)
        pre_one = pre_one + contract_rows(chunk, layer_weights[j][0])
    hidden_one = jax.nn.silu(pre_one).astype(jnp.bfloat16)
    mix_matrix = mixing(upper_neighbours, tgt_loc)
    upper_input = jnp.dot(
        mix_matrix, hidden_one.astype(jnp.float32), precision=lax.Precision.HIGHEST
    ).astype(jnp.bfloat16)
    pre_two = jnp.dot(upper_input, full_upper, preferred_element_type=jnp.float32) + bias_two
    hidden_two = jax.nn.silu(pre_two).astype(jnp.bfloat16)
    slope_two = (out_cotangent.astype(jnp.float32) * swish_slope(pre_two)).astype(jnp.bfloat16)

    local_grad = contract_rows(upper_input, slope_two)
    back_mixed = lax.dot_general(
        slope_two, full_upper, (((1,), (1,)), ((), ())), preferred_element_type=jnp.float32
    )
    back_one = jnp.dot(mix_matrix.T, back_mixed, precision=lax.Precision.HIGHEST)
    slope_one = (back_one * swish_slope(pre_one)).astype(jnp.bfloat16)
    dom_rows = up_rows // n_dom
    upper_part, slope_one = reduce_scatter_grid(
        local_grad.reshape(n_cols, n_dom, dom_rows, hidden),
        n_dom,
        n_cols,
        jnp.bfloat16,
        slope_one,
    )
    slab_rows = all_gather_blocks(slope_one, "cols", n_cols).reshape(tgt_dev, hidden)
    stacked = jnp.dot(both_t, slab_rows, preferred_element_type=jnp.float32)
    dom_cols = hidden // n_dom
    grad_upper = all_gather_blocks(upper_part.astype(jnp.bfloat16), "dom", n_dom)
    grad_upper = grad_upper.reshape(up_rows, hidden).astype(jnp.float32)
    grad_layer = reduce_scatter_blocks(
        jnp.swapaxes(stacked.reshape(2 * width, n_dom, dom_cols), 0, 1),
        "dom",
        n_dom,
        jnp.bfloat16,
    )
    grad_neigh = grad_layer[:w_rows]
    grad_self = grad_layer[w_rows:]
    return (hidden_two, grad_neigh, grad_self, grad_upper)


def solution(mesh):
    in_specs = (
        P(("groups", "dom"), "cols"),
        P(("groups", "dom"), None, None),
        P(("groups", "dom"), None, None),
        P("cols", None),
        P("cols", None),
        P(),
        P("cols", None),
        P(),
        P(("groups", "dom", "cols"), None),
        P(("groups", "dom", "cols"), None),
    )
    out_specs = (
        P(("groups", "dom", "cols"), None),
        P(("groups", "cols"), "dom"),
        P(("groups", "cols"), "dom"),
        P(("groups", "cols"), None),
    )
    return jax.shard_map(local, mesh=mesh, in_specs=in_specs, out_specs=out_specs, check_vma=False)
```

```python
import jax
import jax.numpy as jnp
from jax import lax
from jax.experimental import pallas as pl
from jax.experimental.pallas import tpu as pltpu
from jax.sharding import PartitionSpec as P


def swish_slope(preact):
    gate_val = jax.nn.sigmoid(preact)
    return gate_val * (1.0 + preact * (1.0 - gate_val))


def mixing(neighbours, block_len):
    positions = jnp.arange(block_len, dtype=jnp.int32)
    neighbour_hits = jnp.sum(
        (neighbours[:, :, None] == positions[None, None, :]).astype(jnp.float32), axis=1
    )
    return (jnp.eye(block_len, dtype=jnp.float32) + neighbour_hits) / (neighbours.shape[1] + 1.0)


def contract_rows(left_mat, right_mat):
    return lax.dot_general(
        left_mat, right_mat, (((0,), (0,)), ((), ())), preferred_element_type=jnp.float32
    )


def _accumulate_kernel(tgt_ref, rec_ref, sum_in, cnt_in, sum_ref, cnt_ref):
    targets = tgt_ref[...]
    n_tgt = sum_ref.shape[1]
    rows = lax.broadcasted_iota(jnp.int32, (n_tgt, targets.shape[1]), 0)
    hot = (rows == targets).astype(jnp.bfloat16)
    dims = (((1,), (1,)), ((), ()))
    sum_ref[...] = sum_in[...] + lax.dot_general(
        rec_ref[...], hot, dims, preferred_element_type=jnp.float32
    )
    ones = jnp.ones((cnt_ref.shape[0], targets.shape[1]), jnp.bfloat16)
    cnt_ref[...] = cnt_in[...] + lax.dot_general(
        ones, hot, dims, preferred_element_type=jnp.float32
    )


def accumulate(targets, rec_t, acc_sum, acc_cnt):
    width, cap = rec_t.shape
    n_tgt = acc_sum.shape[1]
    return pl.pallas_call(
        _accumulate_kernel,
        out_shape=[
            jax.ShapeDtypeStruct(acc_sum.shape, jnp.float32),
            jax.ShapeDtypeStruct(acc_cnt.shape, jnp.float32),
        ],
        input_output_aliases={2: 0, 3: 1},
        cost_estimate=pl.CostEstimate(
            flops=2 * n_tgt * cap * (width + acc_cnt.shape[0]),
            transcendentals=0,
            bytes_accessed=cap * (width * 2 + 4) + 2 * n_tgt * (width + acc_cnt.shape[0]) * 4,
        ),
    )(targets, rec_t, acc_sum, acc_cnt)


def _shift_pairs(n, shift):
    return [(i, (i + shift) % n) for i in range(n)]


def _xor_pairs(n, bit):
    return [(i, i ^ bit) for i in range(n)]


def _is_pow2(n):
    return n & (n - 1) == 0


def reduce_scatter_blocks(x, axis, n, send_dtype, high_first=False):
    if not _is_pow2(n):
        got = lax.all_to_all(x.astype(send_dtype), axis, 0, 0, tiled=True)
        return jnp.sum(got.astype(x.dtype), axis=0)
    k = n.bit_length() - 1
    axis_bits = list(reversed(range(k)))
    order = axis_bits[:] if high_first else list(range(k))
    return _butterfly_reduce(
        x.reshape((2,) * k + x.shape[1:]), axis, n, axis_bits, order, send_dtype
    )


def _butterfly_reduce(cur, axis, n, axis_bits, order, send_dtype):
    me = lax.axis_index(axis)
    axis_bits = list(axis_bits)
    for b in order:
        ax = axis_bits.index(b)
        axis_bits.remove(b)
        mine = (me >> b) & 1
        keep = lax.dynamic_index_in_dim(cur, mine, axis=ax, keepdims=False)
        send = lax.dynamic_index_in_dim(cur, 1 - mine, axis=ax, keepdims=False)
        got = lax.ppermute(send.astype(send_dtype), axis, _xor_pairs(n, 1 << b))
        cur = keep + got.astype(keep.dtype)
    return cur


def reduce_scatter_grid(x, n_dom, n_cols, send_dtype, carried):
    if not (_is_pow2(n_dom) and _is_pow2(n_cols)):
        part = reduce_scatter_blocks(x, "cols", n_cols, send_dtype)
        return reduce_scatter_blocks(part, "dom", n_dom, send_dtype), carried
    kc = n_cols.bit_length() - 1
    kd = n_dom.bit_length() - 1
    axis_bits = [kc - 1 - i for i in range(kc)] + [kc + kd - 1 - i for i in range(kd)]
    order = list(range(min(kc, 1))) + list(range(kc, kc + kd)) + list(range(1, kc))
    cur = x.reshape((2,) * (kc + kd) + x.shape[2:])
    axes = ("dom", "cols")
    n = n_dom * n_cols
    cur = _butterfly_reduce(cur, axes, n, axis_bits, order[:1], send_dtype)
    cur, carried = lax.optimization_barrier((cur, carried))
    rest = [b for b in axis_bits if b != order[0]]
    return _butterfly_reduce(cur, axes, n, rest, order[1:], send_dtype), carried


def all_gather_blocks(x, axis, n):
    if not _is_pow2(n):
        return jax.tree.map(lambda leaf: lax.all_gather(leaf, axis, axis=0, tiled=False), x)
    me = lax.axis_index(axis)
    k = n.bit_length() - 1
    cur = x
    for b in reversed(range(k)):
        mine = (me >> b) & 1
        got = lax.ppermute(cur, axis, _xor_pairs(n, 1 << b))

        def join(held, came, b=b, mine=mine):
            low = jnp.where(mine == 0, held, came)
            high = jnp.where(mine == 0, came, held)
            return jnp.stack([low, high], axis=k - 1 - b)

        cur = jax.tree.map(join, cur, got)
    return jax.tree.map(lambda leaf, orig: leaf.reshape((n,) + orig.shape), cur, x)


def gather_block_list(x, axis, n):
    held = {0: x}
    for b in reversed(range(n.bit_length() - 1)):
        keys = sorted(held)
        came = lax.ppermute(tuple(held[q] for q in keys), axis, _xor_pairs(n, 1 << b))
        for q, blocks in zip(keys, came):
            held[q | (1 << b)] = blocks
    return [held[q] for q in range(n)]


def local(
    features,
    edge_source,
    edge_target,
    neigh_weight,
    self_weight,
    bias_one,
    upper_weight,
    bias_two,
    upper_neighbours,
    out_cotangent,
):
    n_dom = lax.axis_size("dom")
    n_cols = lax.axis_size("cols")
    capacity = edge_source.shape[2]
    width = features.shape[1]
    hidden = upper_weight.shape[1]
    tgt_loc = upper_neighbours.shape[0]
    tgt_dev = tgt_loc * n_cols
    w_rows = neigh_weight.shape[0]
    up_rows = upper_weight.shape[0]

    me_dom = lax.axis_index("dom")
    me_col = lax.axis_index("cols")
    if _is_pow2(n_cols):
        layer_weights = gather_block_list((neigh_weight, self_weight), "cols", n_cols)
        full_upper = all_gather_blocks(upper_weight, "cols", n_cols)
        partners = [(me_col ^ j, me_col ^ j, _xor_pairs(n_cols, j)) for j in range(n_cols)]
    else:
        neigh_full, self_full, full_upper = all_gather_blocks(
            (neigh_weight, self_weight, upper_weight), "cols", n_cols
        )
        partners = [
            ((me_col + j) % n_cols, (me_col - j) % n_cols, _shift_pairs(n_cols, j))
            for j in range(n_cols)
        ]
        layer_weights = [
            tuple(
                lax.dynamic_index_in_dim(full, partners[j][1], 0, keepdims=False)
                for full in (neigh_full, self_full)
            )
            for j in range(n_cols)
        ]
    full_upper = full_upper.reshape(n_cols * up_rows, hidden)

    own_t = features[:tgt_dev].T
    own_pre = bias_one
    for j, (dest, src, pairs) in enumerate(partners):
        chunk = lax.dynamic_slice_in_dim(own_t, dest * tgt_loc, tgt_loc, axis=1)
        if j:
            chunk = lax.ppermute(chunk, "cols", pairs)
        own_pre = own_pre + contract_rows(chunk, layer_weights[j][1])

    summed_t = jnp.zeros((width, tgt_dev), jnp.float32)
    counts = jnp.zeros((8, tgt_dev), jnp.float32)
    for shift in range(n_dom):
        dest = (me_dom + shift) % n_dom
        src = (me_dom - shift) % n_dom
        slots = lax.dynamic_index_in_dim(edge_source[0], dest, 0, keepdims=False)
        rows_t = features.at[slots].get(mode="promise_in_bounds").T
        if shift:
            rows_t = lax.ppermute(rows_t, "dom", _shift_pairs(n_dom, shift))
        targets = lax.dynamic_index_in_dim(edge_target[0], src, 0, keepdims=True)
        summed_t, counts = accumulate(targets, rows_t, summed_t, counts)
        if shift == min(1, n_dom - 1):
            summed_t, counts, layer_weights, full_upper = lax.optimization_barrier(
                (summed_t, counts, layer_weights, full_upper)
            )
    mean_t = (summed_t / jnp.maximum(counts[:1], 1.0)).astype(jnp.bfloat16)
    both_t = jnp.concatenate([mean_t, own_t], axis=0)

    pre_one = own_pre
    for j, (dest, src, pairs) in enumerate(partners):
        chunk = lax.dynamic_slice_in_dim(mean_t, dest * tgt_loc, tgt_loc, axis=1)
        if j:
            chunk = lax.ppermute(chunk, "cols", pairs)
        pre_one = pre_one + contract_rows(chunk, layer_weights[j][0])
    hidden_one = jax.nn.silu(pre_one).astype(jnp.bfloat16)
    mix_matrix = mixing(upper_neighbours, tgt_loc)
    upper_input = jnp.dot(
        mix_matrix, hidden_one.astype(jnp.float32), precision=lax.Precision.HIGHEST
    ).astype(jnp.bfloat16)
    pre_two = jnp.dot(upper_input, full_upper, preferred_element_type=jnp.float32) + bias_two
    hidden_two = jax.nn.silu(pre_two).astype(jnp.bfloat16)
    slope_two = (out_cotangent.astype(jnp.float32) * swish_slope(pre_two)).astype(jnp.bfloat16)

    local_grad = contract_rows(upper_input, slope_two)
    back_mixed = lax.dot_general(
        slope_two, full_upper, (((1,), (1,)), ((), ())), preferred_element_type=jnp.float32
    )
    back_one = jnp.dot(mix_matrix.T, back_mixed, precision=lax.Precision.HIGHEST)
    slope_one = (back_one * swish_slope(pre_one)).astype(jnp.bfloat16)
    dom_rows = up_rows // n_dom
    upper_part, slope_one = reduce_scatter_grid(
        local_grad.reshape(n_cols, n_dom, dom_rows, hidden),
        n_dom,
        n_cols,
        jnp.bfloat16,
        slope_one,
    )
    slab_rows = all_gather_blocks(slope_one, "cols", n_cols).reshape(tgt_dev, hidden)
    stacked = jnp.dot(both_t, slab_rows, preferred_element_type=jnp.float32)
    dom_cols = hidden // n_dom
    grad_upper = all_gather_blocks(upper_part.astype(jnp.bfloat16), "dom", n_dom)
    grad_upper = grad_upper.reshape(up_rows, hidden).astype(jnp.float32)
    grad_layer = reduce_scatter_blocks(
        jnp.swapaxes(stacked.reshape(2 * width, n_dom, dom_cols), 0, 1),
        "dom",
        n_dom,
        jnp.bfloat16,
    )
    grad_neigh = grad_layer[:w_rows]
    grad_self = grad_layer[w_rows:]
    return (hidden_two, grad_neigh, grad_self, grad_upper)


def solution(mesh):
    in_specs = (
        P(("groups", "dom"), "cols"),
        P(("groups", "dom"), None, None),
        P(("groups", "dom"), None, None),
        P("cols", None),
        P("cols", None),
        P(),
        P("cols", None),
        P(),
        P(("groups", "dom", "cols"), None),
        P(("groups", "dom", "cols"), None),
    )
    out_specs = (
        P(("groups", "dom", "cols"), None),
        P(("groups", "cols"), "dom"),
        P(("groups", "cols"), "dom"),
        P(("groups", "cols"), None),
    )
    return jax.shard_map(local, mesh=mesh, in_specs=in_specs, out_specs=out_specs, check_vma=False)
```

```python
import jax
import jax.numpy as jnp
from jax import lax
from jax.experimental import pallas as pl
from jax.experimental.pallas import tpu as pltpu
from jax.sharding import PartitionSpec as P


def swish_slope(preact):
    gate_val = jax.nn.sigmoid(preact)
    return gate_val * (1.0 + preact * (1.0 - gate_val))


def mixing(neighbours, block_len):
    positions = jnp.arange(block_len, dtype=jnp.int32)
    neighbour_hits = jnp.sum(
        (neighbours[:, :, None] == positions[None, None, :]).astype(jnp.float32), axis=1
    )
    return (jnp.eye(block_len, dtype=jnp.float32) + neighbour_hits) / (neighbours.shape[1] + 1.0)


def contract_rows(left_mat, right_mat):
    return lax.dot_general(
        left_mat, right_mat, (((0,), (0,)), ((), ())), preferred_element_type=jnp.float32
    )


def _accumulate_kernel(tgt_ref, rec_ref, sum_in, cnt_in, sum_ref, cnt_ref):
    targets = tgt_ref[...]
    n_tgt = sum_ref.shape[1]
    rows = lax.broadcasted_iota(jnp.int32, (n_tgt, targets.shape[1]), 0)
    hot = (rows == targets).astype(jnp.bfloat16)
    dims = (((1,), (1,)), ((), ()))
    sum_ref[...] = sum_in[...] + lax.dot_general(
        rec_ref[...], hot, dims, preferred_element_type=jnp.float32
    )
    ones = jnp.ones((cnt_ref.shape[0], targets.shape[1]), jnp.bfloat16)
    cnt_ref[...] = cnt_in[...] + lax.dot_general(
        ones, hot, dims, preferred_element_type=jnp.float32
    )


def accumulate(targets, rec_t, acc_sum, acc_cnt):
    width, cap = rec_t.shape
    n_tgt = acc_sum.shape[1]
    return pl.pallas_call(
        _accumulate_kernel,
        out_shape=[
            jax.ShapeDtypeStruct(acc_sum.shape, jnp.float32),
            jax.ShapeDtypeStruct(acc_cnt.shape, jnp.float32),
        ],
        input_output_aliases={2: 0, 3: 1},
        cost_estimate=pl.CostEstimate(
            flops=2 * n_tgt * cap * (width + acc_cnt.shape[0]),
            transcendentals=0,
            bytes_accessed=cap * (width * 2 + 4) + 2 * n_tgt * (width + acc_cnt.shape[0]) * 4,
        ),
    )(targets, rec_t, acc_sum, acc_cnt)


def _shift_pairs(n, shift):
    return [(i, (i + shift) % n) for i in range(n)]


def _xor_pairs(n, bit):
    return [(i, i ^ bit) for i in range(n)]


def _is_pow2(n):
    return n & (n - 1) == 0


def reduce_scatter_blocks(x, axis, n, send_dtype, high_first=False):
    if not _is_pow2(n):
        got = lax.all_to_all(x.astype(send_dtype), axis, 0, 0, tiled=True)
        return jnp.sum(got.astype(x.dtype), axis=0)
    k = n.bit_length() - 1
    axis_bits = list(reversed(range(k)))
    order = axis_bits[:] if high_first else list(range(k))
    return _butterfly_reduce(
        x.reshape((2,) * k + x.shape[1:]), axis, n, axis_bits, order, send_dtype
    )


def _butterfly_reduce(cur, axis, n, axis_bits, order, send_dtype):
    me = lax.axis_index(axis)
    axis_bits = list(axis_bits)
    for b in order:
        ax = axis_bits.index(b)
        axis_bits.remove(b)
        mine = (me >> b) & 1
        keep = lax.dynamic_index_in_dim(cur, mine, axis=ax, keepdims=False)
        send = lax.dynamic_index_in_dim(cur, 1 - mine, axis=ax, keepdims=False)
        got = lax.ppermute(send.astype(send_dtype), axis, _xor_pairs(n, 1 << b))
        cur = keep + got.astype(keep.dtype)
    return cur


def reduce_scatter_grid(x, n_dom, n_cols, send_dtype, carried, later):
    if not (_is_pow2(n_dom) and _is_pow2(n_cols)):
        part = reduce_scatter_blocks(x, "cols", n_cols, send_dtype)
        return reduce_scatter_blocks(part, "dom", n_dom, send_dtype), later(carried)
    kc = n_cols.bit_length() - 1
    kd = n_dom.bit_length() - 1
    axis_bits = [kc - 1 - i for i in range(kc)] + [kc + kd - 1 - i for i in range(kd)]
    order = list(range(min(kc, 1))) + list(range(kc, kc + kd)) + list(range(1, kc))
    cur = x.reshape((2,) * (kc + kd) + x.shape[2:])
    axes = ("dom", "cols")
    n = n_dom * n_cols
    cur = _butterfly_reduce(cur, axes, n, axis_bits, order[:1], send_dtype)
    cur, carried = lax.optimization_barrier((cur, carried))
    axis_bits = [b for b in axis_bits if b != order[0]]
    cur = _butterfly_reduce(cur, axes, n, axis_bits, order[1:2], send_dtype)
    axis_bits = [b for b in axis_bits if b not in order[:2]]
    result = later(carried)
    cur, result = lax.optimization_barrier((cur, result))
    return _butterfly_reduce(cur, axes, n, axis_bits, order[2:], send_dtype), result


def all_gather_blocks(x, axis, n):
    if not _is_pow2(n):
        return jax.tree.map(lambda leaf: lax.all_gather(leaf, axis, axis=0, tiled=False), x)
    me = lax.axis_index(axis)
    k = n.bit_length() - 1
    cur = x
    for b in reversed(range(k)):
        mine = (me >> b) & 1
        got = lax.ppermute(cur, axis, _xor_pairs(n, 1 << b))

        def join(held, came, b=b, mine=mine):
            low = jnp.where(mine == 0, held, came)
            high = jnp.where(mine == 0, came, held)
            return jnp.stack([low, high], axis=k - 1 - b)

        cur = jax.tree.map(join, cur, got)
    return jax.tree.map(lambda leaf, orig: leaf.reshape((n,) + orig.shape), cur, x)


def local(
    features,
    edge_source,
    edge_target,
    neigh_weight,
    self_weight,
    bias_one,
    upper_weight,
    bias_two,
    upper_neighbours,
    out_cotangent,
):
    n_dom = lax.axis_size("dom")
    n_cols = lax.axis_size("cols")
    capacity = edge_source.shape[2]
    width = features.shape[1]
    hidden = upper_weight.shape[1]
    tgt_loc = upper_neighbours.shape[0]
    tgt_dev = tgt_loc * n_cols
    w_rows = neigh_weight.shape[0]
    up_rows = upper_weight.shape[0]

    neigh_full, self_full, full_upper = all_gather_blocks(
        (neigh_weight, self_weight, upper_weight), "cols", n_cols
    )
    full_upper = full_upper.reshape(n_cols * up_rows, hidden)

    me_dom = lax.axis_index("dom")
    me_col = lax.axis_index("cols")
    own_t = features[:tgt_dev].T
    own_pre = bias_one
    for shift in range(n_cols):
        dest = (me_col + shift) % n_cols
        src = (me_col - shift) % n_cols
        chunk = lax.dynamic_slice_in_dim(own_t, dest * tgt_loc, tgt_loc, axis=1)
        if shift:
            chunk = lax.ppermute(chunk, "cols", _shift_pairs(n_cols, shift))
        weight = lax.dynamic_index_in_dim(self_full, src, 0, keepdims=False)
        own_pre = own_pre + contract_rows(chunk, weight)

    summed_t = jnp.zeros((width, tgt_dev), jnp.float32)
    counts = jnp.zeros((8, tgt_dev), jnp.float32)
    for shift in range(n_dom):
        dest = (me_dom + shift) % n_dom
        src = (me_dom - shift) % n_dom
        slots = lax.dynamic_index_in_dim(edge_source[0], dest, 0, keepdims=False)
        rows_t = features.at[slots].get(mode="promise_in_bounds").T
        if shift:
            rows_t = lax.ppermute(rows_t, "dom", _shift_pairs(n_dom, shift))
        targets = lax.dynamic_index_in_dim(edge_target[0], src, 0, keepdims=True)
        summed_t, counts = accumulate(targets, rows_t, summed_t, counts)
    mean_t = (summed_t / jnp.maximum(counts[:1], 1.0)).astype(jnp.bfloat16)
    both_t = jnp.concatenate([mean_t, own_t], axis=0)

    pre_one = own_pre
    for shift in range(n_cols):
        dest = (me_col + shift) % n_cols
        src = (me_col - shift) % n_cols
        chunk = lax.dynamic_slice_in_dim(mean_t, dest * tgt_loc, tgt_loc, axis=1)
        if shift:
            chunk = lax.ppermute(chunk, "cols", _shift_pairs(n_cols, shift))
        weight = lax.dynamic_index_in_dim(neigh_full, src, 0, keepdims=False)
        pre_one = pre_one + contract_rows(chunk, weight)
    hidden_one = jax.nn.silu(pre_one).astype(jnp.bfloat16)
    mix_matrix = mixing(upper_neighbours, tgt_loc)
    upper_input = jnp.dot(
        mix_matrix, hidden_one.astype(jnp.float32), precision=lax.Precision.HIGHEST
    ).astype(jnp.bfloat16)
    pre_two = jnp.dot(upper_input, full_upper, preferred_element_type=jnp.float32) + bias_two
    hidden_two = jax.nn.silu(pre_two).astype(jnp.bfloat16)
    slope_two = (out_cotangent.astype(jnp.float32) * swish_slope(pre_two)).astype(jnp.bfloat16)

    local_grad = contract_rows(upper_input, slope_two)
    back_mixed = lax.dot_general(
        slope_two, full_upper, (((1,), (1,)), ((), ())), preferred_element_type=jnp.float32
    )
    back_one = jnp.dot(mix_matrix.T, back_mixed, precision=lax.Precision.HIGHEST)
    slope_one = (back_one * swish_slope(pre_one)).astype(jnp.bfloat16)
    dom_rows = up_rows // n_dom

    def layer_grads(slope_rows):
        slab_rows = all_gather_blocks(slope_rows, "cols", n_cols).reshape(tgt_dev, hidden)
        return jnp.dot(both_t, slab_rows, preferred_element_type=jnp.float32)

    upper_part, stacked = reduce_scatter_grid(
        local_grad.reshape(n_cols, n_dom, dom_rows, hidden),
        n_dom,
        n_cols,
        jnp.bfloat16,
        slope_one,
        layer_grads,
    )
    dom_cols = hidden // n_dom
    grad_upper = all_gather_blocks(upper_part.astype(jnp.bfloat16), "dom", n_dom)
    grad_upper = grad_upper.reshape(up_rows, hidden).astype(jnp.float32)
    grad_layer = reduce_scatter_blocks(
        jnp.swapaxes(stacked.reshape(2 * width, n_dom, dom_cols), 0, 1),
        "dom",
        n_dom,
        jnp.bfloat16,
    )
    grad_neigh = grad_layer[:w_rows]
    grad_self = grad_layer[w_rows:]
    return (hidden_two, grad_neigh, grad_self, grad_upper)


def solution(mesh):
    in_specs = (
        P(("groups", "dom"), "cols"),
        P(("groups", "dom"), None, None),
        P(("groups", "dom"), None, None),
        P("cols", None),
        P("cols", None),
        P(),
        P("cols", None),
        P(),
        P(("groups", "dom", "cols"), None),
        P(("groups", "dom", "cols"), None),
    )
    out_specs = (
        P(("groups", "dom", "cols"), None),
        P(("groups", "cols"), "dom"),
        P(("groups", "cols"), "dom"),
        P(("groups", "cols"), None),
    )
    return jax.shard_map(local, mesh=mesh, in_specs=in_specs, out_specs=out_specs, check_vma=False)
```

```python
import jax
import jax.numpy as jnp
from jax import lax
from jax.experimental import pallas as pl
from jax.experimental.pallas import tpu as pltpu
from jax.sharding import PartitionSpec as P


def swish_slope(preact):
    gate_val = jax.nn.sigmoid(preact)
    return gate_val * (1.0 + preact * (1.0 - gate_val))


def mixing(neighbours, block_len):
    positions = jnp.arange(block_len, dtype=jnp.int32)
    neighbour_hits = jnp.sum(
        (neighbours[:, :, None] == positions[None, None, :]).astype(jnp.float32), axis=1
    )
    return (jnp.eye(block_len, dtype=jnp.float32) + neighbour_hits) / (neighbours.shape[1] + 1.0)


def contract_rows(left_mat, right_mat):
    return lax.dot_general(
        left_mat, right_mat, (((0,), (0,)), ((), ())), preferred_element_type=jnp.float32
    )


def _accumulate_kernel(tgt_ref, rec_ref, sum_in, cnt_in, sum_ref, cnt_ref):
    targets = tgt_ref[...]
    n_tgt = sum_ref.shape[1]
    rows = lax.broadcasted_iota(jnp.int32, (n_tgt, targets.shape[1]), 0)
    hot = (rows == targets).astype(jnp.bfloat16)
    dims = (((1,), (1,)), ((), ()))
    sum_ref[...] = sum_in[...] + lax.dot_general(
        rec_ref[...], hot, dims, preferred_element_type=jnp.float32
    )
    ones = jnp.ones((cnt_ref.shape[0], targets.shape[1]), jnp.bfloat16)
    cnt_ref[...] = cnt_in[...] + lax.dot_general(
        ones, hot, dims, preferred_element_type=jnp.float32
    )


def accumulate(targets, rec_t, acc_sum, acc_cnt):
    width, cap = rec_t.shape
    n_tgt = acc_sum.shape[1]
    return pl.pallas_call(
        _accumulate_kernel,
        out_shape=[
            jax.ShapeDtypeStruct(acc_sum.shape, jnp.float32),
            jax.ShapeDtypeStruct(acc_cnt.shape, jnp.float32),
        ],
        input_output_aliases={2: 0, 3: 1},
        cost_estimate=pl.CostEstimate(
            flops=2 * n_tgt * cap * (width + acc_cnt.shape[0]),
            transcendentals=0,
            bytes_accessed=cap * (width * 2 + 4) + 2 * n_tgt * (width + acc_cnt.shape[0]) * 4,
        ),
    )(targets, rec_t, acc_sum, acc_cnt)


def _shift_pairs(n, shift):
    return [(i, (i + shift) % n) for i in range(n)]


def _xor_pairs(n, bit):
    return [(i, i ^ bit) for i in range(n)]


def _is_pow2(n):
    return n & (n - 1) == 0


def reduce_scatter_blocks(x, axis, n, send_dtype, high_first=False):
    if not _is_pow2(n):
        got = lax.all_to_all(x.astype(send_dtype), axis, 0, 0, tiled=True)
        return jnp.sum(got.astype(x.dtype), axis=0)
    k = n.bit_length() - 1
    axis_bits = list(reversed(range(k)))
    order = axis_bits[:] if high_first else list(range(k))
    return _butterfly_reduce(
        x.reshape((2,) * k + x.shape[1:]), axis, n, axis_bits, order, send_dtype
    )


def _butterfly_reduce(cur, axis, n, axis_bits, order, send_dtype):
    me = lax.axis_index(axis)
    axis_bits = list(axis_bits)
    for b in order:
        ax = axis_bits.index(b)
        axis_bits.remove(b)
        mine = (me >> b) & 1
        keep = lax.dynamic_index_in_dim(cur, mine, axis=ax, keepdims=False)
        send = lax.dynamic_index_in_dim(cur, 1 - mine, axis=ax, keepdims=False)
        got = lax.ppermute(send.astype(send_dtype), axis, _xor_pairs(n, 1 << b))
        cur = keep + got.astype(keep.dtype)
    return cur


def reduce_scatter_grid(x, n_dom, n_cols, send_dtype, carried):
    if not (_is_pow2(n_dom) and _is_pow2(n_cols)):
        part = reduce_scatter_blocks(x, "cols", n_cols, send_dtype)
        return reduce_scatter_blocks(part, "dom", n_dom, send_dtype), carried
    kc = n_cols.bit_length() - 1
    kd = n_dom.bit_length() - 1
    axis_bits = [kc - 1 - i for i in range(kc)] + [kc + kd - 1 - i for i in range(kd)]
    order = list(range(min(kc, 1))) + list(range(kc, kc + kd)) + list(range(1, kc))
    cur = x.reshape((2,) * (kc + kd) + x.shape[2:])
    axes = ("dom", "cols")
    n = n_dom * n_cols
    cur = _butterfly_reduce(cur, axes, n, axis_bits, order[:1], send_dtype)
    cur, carried = lax.optimization_barrier((cur, carried))
    rest = [b for b in axis_bits if b != order[0]]
    return _butterfly_reduce(cur, axes, n, rest, order[1:], send_dtype), carried


def all_gather_blocks(x, axis, n):
    if not _is_pow2(n):
        return jax.tree.map(lambda leaf: lax.all_gather(leaf, axis, axis=0, tiled=False), x)
    me = lax.axis_index(axis)
    k = n.bit_length() - 1
    cur = x
    for b in reversed(range(k)):
        mine = (me >> b) & 1
        got = lax.ppermute(cur, axis, _xor_pairs(n, 1 << b))

        def join(held, came, b=b, mine=mine):
            low = jnp.where(mine == 0, held, came)
            high = jnp.where(mine == 0, came, held)
            return jnp.stack([low, high], axis=k - 1 - b)

        cur = jax.tree.map(join, cur, got)
    return jax.tree.map(lambda leaf, orig: leaf.reshape((n,) + orig.shape), cur, x)


def local(
    features,
    edge_source,
    edge_target,
    neigh_weight,
    self_weight,
    bias_one,
    upper_weight,
    bias_two,
    upper_neighbours,
    out_cotangent,
):
    n_dom = lax.axis_size("dom")
    n_cols = lax.axis_size("cols")
    capacity = edge_source.shape[2]
    width = features.shape[1]
    hidden = upper_weight.shape[1]
    tgt_loc = upper_neighbours.shape[0]
    tgt_dev = tgt_loc * n_cols
    w_rows = neigh_weight.shape[0]
    up_rows = upper_weight.shape[0]

    neigh_full, self_full, full_upper = all_gather_blocks(
        (neigh_weight, self_weight, upper_weight), "cols", n_cols
    )
    full_upper = full_upper.reshape(n_cols * up_rows, hidden)

    me_dom = lax.axis_index("dom")
    me_col = lax.axis_index("cols")
    own_t = features[:tgt_dev].T
    both_full = jnp.concatenate([neigh_full, self_full], axis=1)

    summed_t = jnp.zeros((width, tgt_dev), jnp.float32)
    counts = jnp.zeros((8, tgt_dev), jnp.float32)
    for shift in range(n_dom):
        dest = (me_dom + shift) % n_dom
        src = (me_dom - shift) % n_dom
        slots = lax.dynamic_index_in_dim(edge_source[0], dest, 0, keepdims=False)
        rows_t = features.at[slots].get(mode="promise_in_bounds").T
        if shift:
            rows_t = lax.ppermute(rows_t, "dom", _shift_pairs(n_dom, shift))
        targets = lax.dynamic_index_in_dim(edge_target[0], src, 0, keepdims=True)
        summed_t, counts = accumulate(targets, rows_t, summed_t, counts)
    mean_t = (summed_t / jnp.maximum(counts[:1], 1.0)).astype(jnp.bfloat16)
    both_t = jnp.concatenate([mean_t, own_t], axis=0)

    pre_one = bias_one
    for shift in range(n_cols):
        dest = (me_col + shift) % n_cols
        src = (me_col - shift) % n_cols
        chunk = lax.dynamic_slice_in_dim(both_t, dest * tgt_loc, tgt_loc, axis=1)
        if shift:
            chunk = lax.ppermute(chunk, "cols", _shift_pairs(n_cols, shift))
        weight = lax.dynamic_index_in_dim(both_full, src, 0, keepdims=False)
        pre_one = pre_one + contract_rows(chunk, weight)
    hidden_one = jax.nn.silu(pre_one).astype(jnp.bfloat16)
    mix_matrix = mixing(upper_neighbours, tgt_loc)
    upper_input = jnp.dot(
        mix_matrix, hidden_one.astype(jnp.float32), precision=lax.Precision.HIGHEST
    ).astype(jnp.bfloat16)
    pre_two = jnp.dot(upper_input, full_upper, preferred_element_type=jnp.float32) + bias_two
    hidden_two = jax.nn.silu(pre_two).astype(jnp.bfloat16)
    slope_two = (out_cotangent.astype(jnp.float32) * swish_slope(pre_two)).astype(jnp.bfloat16)

    local_grad = contract_rows(upper_input, slope_two)
    back_mixed = lax.dot_general(
        slope_two, full_upper, (((1,), (1,)), ((), ())), preferred_element_type=jnp.float32
    )
    back_one = jnp.dot(mix_matrix.T, back_mixed, precision=lax.Precision.HIGHEST)
    slope_one = (back_one * swish_slope(pre_one)).astype(jnp.bfloat16)
    dom_rows = up_rows // n_dom
    upper_part, slope_one = reduce_scatter_grid(
        local_grad.reshape(n_cols, n_dom, dom_rows, hidden),
        n_dom,
        n_cols,
        jnp.bfloat16,
        slope_one,
    )
    slab_rows = all_gather_blocks(slope_one, "cols", n_cols).reshape(tgt_dev, hidden)
    stacked = jnp.dot(both_t, slab_rows, preferred_element_type=jnp.float32)
    dom_cols = hidden // n_dom
    grad_upper = all_gather_blocks(upper_part.astype(jnp.bfloat16), "dom", n_dom)
    grad_upper = grad_upper.reshape(up_rows, hidden).astype(jnp.float32)
    grad_layer = reduce_scatter_blocks(
        jnp.swapaxes(stacked.reshape(2 * width, n_dom, dom_cols), 0, 1),
        "dom",
        n_dom,
        jnp.bfloat16,
    )
    grad_neigh = grad_layer[:w_rows]
    grad_self = grad_layer[w_rows:]
    return (hidden_two, grad_neigh, grad_self, grad_upper)


def solution(mesh):
    in_specs = (
        P(("groups", "dom"), "cols"),
        P(("groups", "dom"), None, None),
        P(("groups", "dom"), None, None),
        P("cols", None),
        P("cols", None),
        P(),
        P("cols", None),
        P(),
        P(("groups", "dom", "cols"), None),
        P(("groups", "dom", "cols"), None),
    )
    out_specs = (
        P(("groups", "dom", "cols"), None),
        P(("groups", "cols"), "dom"),
        P(("groups", "cols"), "dom"),
        P(("groups", "cols"), None),
    )
    return jax.shard_map(local, mesh=mesh, in_specs=in_specs, out_specs=out_specs, check_vma=False)
```

```python
import jax
import jax.numpy as jnp
from jax import lax
from jax.experimental import pallas as pl
from jax.experimental.pallas import tpu as pltpu
from jax.sharding import PartitionSpec as P


def swish_slope(preact):
    gate_val = jax.nn.sigmoid(preact)
    return gate_val * (1.0 + preact * (1.0 - gate_val))


def mixing(neighbours, block_len):
    positions = jnp.arange(block_len, dtype=jnp.int32)
    neighbour_hits = jnp.sum(
        (neighbours[:, :, None] == positions[None, None, :]).astype(jnp.float32), axis=1
    )
    return (jnp.eye(block_len, dtype=jnp.float32) + neighbour_hits) / (neighbours.shape[1] + 1.0)


def contract_rows(left_mat, right_mat):
    return lax.dot_general(
        left_mat, right_mat, (((0,), (0,)), ((), ())), preferred_element_type=jnp.float32
    )


def _accumulate_kernel(tgt_ref, rec_ref, sum_in, cnt_in, sum_ref, cnt_ref):
    targets = tgt_ref[...]
    n_tgt = sum_ref.shape[1]
    rows = lax.broadcasted_iota(jnp.int32, (n_tgt, targets.shape[1]), 0)
    hot = (rows == targets).astype(jnp.bfloat16)
    dims = (((1,), (1,)), ((), ()))
    sum_ref[...] = sum_in[...] + lax.dot_general(
        rec_ref[...], hot, dims, preferred_element_type=jnp.float32
    )
    ones = jnp.ones((cnt_ref.shape[0], targets.shape[1]), jnp.bfloat16)
    cnt_ref[...] = cnt_in[...] + lax.dot_general(
        ones, hot, dims, preferred_element_type=jnp.float32
    )


def accumulate(targets, rec_t, acc_sum, acc_cnt):
    width, cap = rec_t.shape
    n_tgt = acc_sum.shape[1]
    return pl.pallas_call(
        _accumulate_kernel,
        out_shape=[
            jax.ShapeDtypeStruct(acc_sum.shape, jnp.float32),
            jax.ShapeDtypeStruct(acc_cnt.shape, jnp.float32),
        ],
        input_output_aliases={2: 0, 3: 1},
        cost_estimate=pl.CostEstimate(
            flops=2 * n_tgt * cap * (width + acc_cnt.shape[0]),
            transcendentals=0,
            bytes_accessed=cap * (width * 2 + 4) + 2 * n_tgt * (width + acc_cnt.shape[0]) * 4,
        ),
    )(targets, rec_t, acc_sum, acc_cnt)


def _shift_pairs(n, shift):
    return [(i, (i + shift) % n) for i in range(n)]


def _xor_pairs(n, bit):
    return [(i, i ^ bit) for i in range(n)]


def _is_pow2(n):
    return n & (n - 1) == 0


def reduce_scatter_blocks(x, axis, n, send_dtype, high_first=False):
    if not _is_pow2(n):
        got = lax.all_to_all(x.astype(send_dtype), axis, 0, 0, tiled=True)
        return jnp.sum(got.astype(x.dtype), axis=0)
    k = n.bit_length() - 1
    axis_bits = list(reversed(range(k)))
    order = axis_bits[:] if high_first else list(range(k))
    return _butterfly_reduce(
        x.reshape((2,) * k + x.shape[1:]), axis, n, axis_bits, order, send_dtype
    )


def _butterfly_reduce(cur, axis, n, axis_bits, order, send_dtype):
    me = lax.axis_index(axis)
    axis_bits = list(axis_bits)
    for b in order:
        ax = axis_bits.index(b)
        axis_bits.remove(b)
        mine = (me >> b) & 1
        keep = lax.dynamic_index_in_dim(cur, mine, axis=ax, keepdims=False)
        send = lax.dynamic_index_in_dim(cur, 1 - mine, axis=ax, keepdims=False)
        got = lax.ppermute(send.astype(send_dtype), axis, _xor_pairs(n, 1 << b))
        cur = keep + got.astype(keep.dtype)
    return cur


def reduce_scatter_grid(x, n_dom, n_cols, send_dtype, carried):
    if not (_is_pow2(n_dom) and _is_pow2(n_cols)):
        part = reduce_scatter_blocks(x, "cols", n_cols, send_dtype)
        return reduce_scatter_blocks(part, "dom", n_dom, send_dtype), carried
    kc = n_cols.bit_length() - 1
    kd = n_dom.bit_length() - 1
    axis_bits = [kc - 1 - i for i in range(kc)] + [kc + kd - 1 - i for i in range(kd)]
    order = list(range(min(kc, 1))) + list(range(kc, kc + kd)) + list(range(1, kc))
    cur = x.reshape((2,) * (kc + kd) + x.shape[2:])
    axes = ("dom", "cols")
    n = n_dom * n_cols
    cur = _butterfly_reduce(cur, axes, n, axis_bits, order[:1], send_dtype)
    cur, carried = lax.optimization_barrier((cur, carried))
    rest = [b for b in axis_bits if b != order[0]]
    return _butterfly_reduce(cur, axes, n, rest, order[1:], send_dtype), carried


def all_gather_blocks(x, axis, n):
    if not _is_pow2(n):
        return jax.tree.map(lambda leaf: lax.all_gather(leaf, axis, axis=0, tiled=False), x)
    me = lax.axis_index(axis)
    k = n.bit_length() - 1
    cur = x
    for b in reversed(range(k)):
        mine = (me >> b) & 1
        got = lax.ppermute(cur, axis, _xor_pairs(n, 1 << b))

        def join(held, came, b=b, mine=mine):
            low = jnp.where(mine == 0, held, came)
            high = jnp.where(mine == 0, came, held)
            return jnp.stack([low, high], axis=k - 1 - b)

        cur = jax.tree.map(join, cur, got)
    return jax.tree.map(lambda leaf, orig: leaf.reshape((n,) + orig.shape), cur, x)


def local(
    features,
    edge_source,
    edge_target,
    neigh_weight,
    self_weight,
    bias_one,
    upper_weight,
    bias_two,
    upper_neighbours,
    out_cotangent,
):
    n_dom = lax.axis_size("dom")
    n_cols = lax.axis_size("cols")
    capacity = edge_source.shape[2]
    width = features.shape[1]
    hidden = upper_weight.shape[1]
    tgt_loc = upper_neighbours.shape[0]
    tgt_dev = tgt_loc * n_cols
    w_rows = neigh_weight.shape[0]
    up_rows = upper_weight.shape[0]

    both_full, full_upper = all_gather_blocks(
        (jnp.concatenate([neigh_weight, self_weight], axis=0), upper_weight), "cols", n_cols
    )
    full_upper = full_upper.reshape(n_cols * up_rows, hidden)

    me_dom = lax.axis_index("dom")
    me_col = lax.axis_index("cols")
    own_t = features[:tgt_dev].T

    summed_t = jnp.zeros((width, tgt_dev), jnp.float32)
    counts = jnp.zeros((8, tgt_dev), jnp.float32)
    for shift in range(n_dom):
        dest = (me_dom + shift) % n_dom
        src = (me_dom - shift) % n_dom
        slots = lax.dynamic_index_in_dim(edge_source[0], dest, 0, keepdims=False)
        rows_t = features.at[slots].get(mode="promise_in_bounds").T
        if shift:
            rows_t = lax.ppermute(rows_t, "dom", _shift_pairs(n_dom, shift))
        targets = lax.dynamic_index_in_dim(edge_target[0], src, 0, keepdims=True)
        summed_t, counts = accumulate(targets, rows_t, summed_t, counts)
    mean_t = (summed_t / jnp.maximum(counts[:1], 1.0)).astype(jnp.bfloat16)
    both_t = jnp.concatenate([mean_t, own_t], axis=0)

    pre_one = bias_one
    for shift in range(n_cols):
        dest = (me_col + shift) % n_cols
        src = (me_col - shift) % n_cols
        chunk = lax.dynamic_slice_in_dim(both_t, dest * tgt_loc, tgt_loc, axis=1)
        if shift:
            chunk = lax.ppermute(chunk, "cols", _shift_pairs(n_cols, shift))
        weight = lax.dynamic_index_in_dim(both_full, src, 0, keepdims=False)
        pre_one = pre_one + contract_rows(chunk, weight)
    hidden_one = jax.nn.silu(pre_one).astype(jnp.bfloat16)
    mix_matrix = mixing(upper_neighbours, tgt_loc)
    upper_input = jnp.dot(
        mix_matrix, hidden_one.astype(jnp.float32), precision=lax.Precision.HIGHEST
    ).astype(jnp.bfloat16)
    pre_two = jnp.dot(upper_input, full_upper, preferred_element_type=jnp.float32) + bias_two
    hidden_two = jax.nn.silu(pre_two).astype(jnp.bfloat16)
    slope_two = (out_cotangent.astype(jnp.float32) * swish_slope(pre_two)).astype(jnp.bfloat16)

    local_grad = contract_rows(upper_input, slope_two)
    back_mixed = lax.dot_general(
        slope_two, full_upper, (((1,), (1,)), ((), ())), preferred_element_type=jnp.float32
    )
    back_one = jnp.dot(mix_matrix.T, back_mixed, precision=lax.Precision.HIGHEST)
    slope_one = (back_one * swish_slope(pre_one)).astype(jnp.bfloat16)
    dom_rows = up_rows // n_dom
    upper_part, slope_one = reduce_scatter_grid(
        local_grad.reshape(n_cols, n_dom, dom_rows, hidden),
        n_dom,
        n_cols,
        jnp.bfloat16,
        slope_one,
    )
    slab_rows = all_gather_blocks(slope_one, "cols", n_cols).reshape(tgt_dev, hidden)
    stacked = jnp.dot(both_t, slab_rows, preferred_element_type=jnp.float32)
    dom_cols = hidden // n_dom
    grad_upper = all_gather_blocks(upper_part.astype(jnp.bfloat16), "dom", n_dom)
    grad_upper = grad_upper.reshape(up_rows, hidden).astype(jnp.float32)
    grad_layer = reduce_scatter_blocks(
        jnp.swapaxes(stacked.reshape(2 * width, n_dom, dom_cols), 0, 1),
        "dom",
        n_dom,
        jnp.bfloat16,
    )
    grad_neigh = grad_layer[:w_rows]
    grad_self = grad_layer[w_rows:]
    return (hidden_two, grad_neigh, grad_self, grad_upper)


def solution(mesh):
    in_specs = (
        P(("groups", "dom"), "cols"),
        P(("groups", "dom"), None, None),
        P(("groups", "dom"), None, None),
        P("cols", None),
        P("cols", None),
        P(),
        P("cols", None),
        P(),
        P(("groups", "dom", "cols"), None),
        P(("groups", "dom", "cols"), None),
    )
    out_specs = (
        P(("groups", "dom", "cols"), None),
        P(("groups", "cols"), "dom"),
        P(("groups", "cols"), "dom"),
        P(("groups", "cols"), None),
    )
    return jax.shard_map(local, mesh=mesh, in_specs=in_specs, out_specs=out_specs, check_vma=False)
```

```python
import jax
import jax.numpy as jnp
from jax import lax
from jax.experimental import pallas as pl
from jax.experimental.pallas import tpu as pltpu
from jax.sharding import PartitionSpec as P


def swish_slope(preact):
    gate_val = jax.nn.sigmoid(preact)
    return gate_val * (1.0 + preact * (1.0 - gate_val))


def mixing(neighbours, block_len):
    positions = jnp.arange(block_len, dtype=jnp.int32)
    neighbour_hits = jnp.sum(
        (neighbours[:, :, None] == positions[None, None, :]).astype(jnp.float32), axis=1
    )
    return (jnp.eye(block_len, dtype=jnp.float32) + neighbour_hits) / (neighbours.shape[1] + 1.0)


def contract_rows(left_mat, right_mat):
    return lax.dot_general(
        left_mat, right_mat, (((0,), (0,)), ((), ())), preferred_element_type=jnp.float32
    )


def _accumulate_kernel(tgt_ref, rec_ref, sum_in, cnt_in, sum_ref, cnt_ref):
    targets = tgt_ref[...]
    n_tgt = sum_ref.shape[1]
    rows = lax.broadcasted_iota(jnp.int32, (n_tgt, targets.shape[1]), 0)
    hot = (rows == targets).astype(jnp.bfloat16)
    dims = (((1,), (1,)), ((), ()))
    sum_ref[...] = sum_in[...] + lax.dot_general(
        rec_ref[...], hot, dims, preferred_element_type=jnp.float32
    )
    ones = jnp.ones((cnt_ref.shape[0], targets.shape[1]), jnp.bfloat16)
    cnt_ref[...] = cnt_in[...] + lax.dot_general(
        ones, hot, dims, preferred_element_type=jnp.float32
    )


def accumulate(targets, rec_t, acc_sum, acc_cnt):
    width, cap = rec_t.shape
    n_tgt = acc_sum.shape[1]
    return pl.pallas_call(
        _accumulate_kernel,
        out_shape=[
            jax.ShapeDtypeStruct(acc_sum.shape, jnp.float32),
            jax.ShapeDtypeStruct(acc_cnt.shape, jnp.float32),
        ],
        input_output_aliases={2: 0, 3: 1},
        cost_estimate=pl.CostEstimate(
            flops=2 * n_tgt * cap * (width + acc_cnt.shape[0]),
            transcendentals=0,
            bytes_accessed=cap * (width * 2 + 4) + 2 * n_tgt * (width + acc_cnt.shape[0]) * 4,
        ),
    )(targets, rec_t, acc_sum, acc_cnt)


def _shift_pairs(n, shift):
    return [(i, (i + shift) % n) for i in range(n)]


def _xor_pairs(n, bit):
    return [(i, i ^ bit) for i in range(n)]


def _is_pow2(n):
    return n & (n - 1) == 0


def reduce_scatter_blocks(x, axis, n, send_dtype, high_first=False):
    if not _is_pow2(n):
        got = lax.all_to_all(x.astype(send_dtype), axis, 0, 0, tiled=True)
        return jnp.sum(got.astype(x.dtype), axis=0)
    k = n.bit_length() - 1
    axis_bits = list(reversed(range(k)))
    order = axis_bits[:] if high_first else list(range(k))
    return _butterfly_reduce(
        x.reshape((2,) * k + x.shape[1:]), axis, n, axis_bits, order, send_dtype
    )


def _butterfly_reduce(cur, axis, n, axis_bits, order, send_dtype):
    me = lax.axis_index(axis)
    axis_bits = list(axis_bits)
    for b in order:
        ax = axis_bits.index(b)
        axis_bits.remove(b)
        mine = (me >> b) & 1
        keep = lax.dynamic_index_in_dim(cur, mine, axis=ax, keepdims=False)
        send = lax.dynamic_index_in_dim(cur, 1 - mine, axis=ax, keepdims=False)
        got = lax.ppermute(send.astype(send_dtype), axis, _xor_pairs(n, 1 << b))
        cur = keep + got.astype(keep.dtype)
    return cur


def reduce_scatter_grid(x, n_dom, n_cols, send_dtype, carried):
    if not (_is_pow2(n_dom) and _is_pow2(n_cols)):
        part = reduce_scatter_blocks(x, "cols", n_cols, send_dtype)
        return reduce_scatter_blocks(part, "dom", n_dom, send_dtype), carried
    kc = n_cols.bit_length() - 1
    kd = n_dom.bit_length() - 1
    axis_bits = [kc - 1 - i for i in range(kc)] + [kc + kd - 1 - i for i in range(kd)]
    order = list(range(min(kc, 1))) + list(range(kc, kc + kd)) + list(range(1, kc))
    cur = x.reshape((2,) * (kc + kd) + x.shape[2:])
    axes = ("dom", "cols")
    n = n_dom * n_cols
    cur = _butterfly_reduce(cur, axes, n, axis_bits, order[:1], send_dtype)
    cur, carried = lax.optimization_barrier((cur, carried))
    rest = [b for b in axis_bits if b != order[0]]
    return _butterfly_reduce(cur, axes, n, rest, order[1:], send_dtype), carried


def all_gather_blocks(x, axis, n):
    if not _is_pow2(n):
        return jax.tree.map(lambda leaf: lax.all_gather(leaf, axis, axis=0, tiled=False), x)
    me = lax.axis_index(axis)
    k = n.bit_length() - 1
    cur = x
    for b in reversed(range(k)):
        mine = (me >> b) & 1
        got = lax.ppermute(cur, axis, _xor_pairs(n, 1 << b))

        def join(held, came, b=b, mine=mine):
            low = jnp.where(mine == 0, held, came)
            high = jnp.where(mine == 0, came, held)
            return jnp.stack([low, high], axis=k - 1 - b)

        cur = jax.tree.map(join, cur, got)
    return jax.tree.map(lambda leaf, orig: leaf.reshape((n,) + orig.shape), cur, x)


def gather_block_list(x, axis, n):
    held = {0: x}
    for b in reversed(range(n.bit_length() - 1)):
        keys = sorted(held)
        came = lax.ppermute(tuple(held[q] for q in keys), axis, _xor_pairs(n, 1 << b))
        for q, blocks in zip(keys, came):
            held[q | (1 << b)] = blocks
    return [held[q] for q in range(n)]


def local(
    features,
    edge_source,
    edge_target,
    neigh_weight,
    self_weight,
    bias_one,
    upper_weight,
    bias_two,
    upper_neighbours,
    out_cotangent,
):
    n_dom = lax.axis_size("dom")
    n_cols = lax.axis_size("cols")
    capacity = edge_source.shape[2]
    width = features.shape[1]
    hidden = upper_weight.shape[1]
    tgt_loc = upper_neighbours.shape[0]
    tgt_dev = tgt_loc * n_cols
    w_rows = neigh_weight.shape[0]
    up_rows = upper_weight.shape[0]

    neigh_full, self_full, full_upper = all_gather_blocks(
        (neigh_weight, self_weight, upper_weight), "cols", n_cols
    )
    full_upper = full_upper.reshape(n_cols * up_rows, hidden)

    me_dom = lax.axis_index("dom")
    me_col = lax.axis_index("cols")
    own_t = features[:tgt_dev].T
    both_full = jnp.concatenate([neigh_full, self_full], axis=1)

    summed_t = jnp.zeros((width, tgt_dev), jnp.float32)
    counts = jnp.zeros((8, tgt_dev), jnp.float32)
    for shift in range(n_dom):
        dest = (me_dom + shift) % n_dom
        src = (me_dom - shift) % n_dom
        slots = lax.dynamic_index_in_dim(edge_source[0], dest, 0, keepdims=False)
        rows_t = features.at[slots].get(mode="promise_in_bounds").T
        if shift:
            rows_t = lax.ppermute(rows_t, "dom", _shift_pairs(n_dom, shift))
        targets = lax.dynamic_index_in_dim(edge_target[0], src, 0, keepdims=True)
        summed_t, counts = accumulate(targets, rows_t, summed_t, counts)
    mean_t = (summed_t / jnp.maximum(counts[:1], 1.0)).astype(jnp.bfloat16)
    both_t = jnp.concatenate([mean_t, own_t], axis=0)

    pre_one = bias_one
    for shift in range(n_cols):
        dest = (me_col + shift) % n_cols
        src = (me_col - shift) % n_cols
        chunk = lax.dynamic_slice_in_dim(both_t, dest * tgt_loc, tgt_loc, axis=1)
        if shift:
            chunk = lax.ppermute(chunk, "cols", _shift_pairs(n_cols, shift))
        weight = lax.dynamic_index_in_dim(both_full, src, 0, keepdims=False)
        pre_one = pre_one + contract_rows(chunk, weight)
    hidden_one = jax.nn.silu(pre_one).astype(jnp.bfloat16)
    mix_matrix = mixing(upper_neighbours, tgt_loc)
    upper_input = jnp.dot(
        mix_matrix, hidden_one.astype(jnp.float32), precision=lax.Precision.HIGHEST
    ).astype(jnp.bfloat16)
    pre_two = jnp.dot(upper_input, full_upper, preferred_element_type=jnp.float32) + bias_two
    hidden_two = jax.nn.silu(pre_two).astype(jnp.bfloat16)
    slope_two = (out_cotangent.astype(jnp.float32) * swish_slope(pre_two)).astype(jnp.bfloat16)

    local_grad = contract_rows(upper_input, slope_two)
    back_mixed = lax.dot_general(
        slope_two, full_upper, (((1,), (1,)), ((), ())), preferred_element_type=jnp.float32
    )
    back_one = jnp.dot(mix_matrix.T, back_mixed, precision=lax.Precision.HIGHEST)
    slope_one = (back_one * swish_slope(pre_one)).astype(jnp.bfloat16)
    dom_rows = up_rows // n_dom
    upper_part, slope_one = reduce_scatter_grid(
        local_grad.reshape(n_cols, n_dom, dom_rows, hidden),
        n_dom,
        n_cols,
        jnp.bfloat16,
        slope_one,
    )
    if _is_pow2(n_cols):
        slope_blocks = gather_block_list((slope_one,), "cols", n_cols)
        stacked = jnp.zeros((2 * width, hidden), jnp.float32)
        for j, (block,) in enumerate(slope_blocks):
            owner_cols = lax.dynamic_slice_in_dim(
                both_t, (me_col ^ j) * tgt_loc, tgt_loc, axis=1
            )
            stacked = stacked + jnp.dot(owner_cols, block, preferred_element_type=jnp.float32)
    else:
        slab_rows = all_gather_blocks(slope_one, "cols", n_cols).reshape(tgt_dev, hidden)
        stacked = jnp.dot(both_t, slab_rows, preferred_element_type=jnp.float32)
    dom_cols = hidden // n_dom
    grad_upper = all_gather_blocks(upper_part.astype(jnp.bfloat16), "dom", n_dom)
    grad_upper = grad_upper.reshape(up_rows, hidden).astype(jnp.float32)
    grad_layer = reduce_scatter_blocks(
        jnp.swapaxes(stacked.reshape(2 * width, n_dom, dom_cols), 0, 1),
        "dom",
        n_dom,
        jnp.bfloat16,
    )
    grad_neigh = grad_layer[:w_rows]
    grad_self = grad_layer[w_rows:]
    return (hidden_two, grad_neigh, grad_self, grad_upper)


def solution(mesh):
    in_specs = (
        P(("groups", "dom"), "cols"),
        P(("groups", "dom"), None, None),
        P(("groups", "dom"), None, None),
        P("cols", None),
        P("cols", None),
        P(),
        P("cols", None),
        P(),
        P(("groups", "dom", "cols"), None),
        P(("groups", "dom", "cols"), None),
    )
    out_specs = (
        P(("groups", "dom", "cols"), None),
        P(("groups", "cols"), "dom"),
        P(("groups", "cols"), "dom"),
        P(("groups", "cols"), None),
    )
    return jax.shard_map(local, mesh=mesh, in_specs=in_specs, out_specs=out_specs, check_vma=False)
```

```python
import jax
import jax.numpy as jnp
from jax import lax
from jax.experimental import pallas as pl
from jax.experimental.pallas import tpu as pltpu
from jax.sharding import PartitionSpec as P


def swish_slope(preact):
    gate_val = jax.nn.sigmoid(preact)
    return gate_val * (1.0 + preact * (1.0 - gate_val))


def mixing(neighbours, block_len):
    positions = jnp.arange(block_len, dtype=jnp.int32)
    neighbour_hits = jnp.sum(
        (neighbours[:, :, None] == positions[None, None, :]).astype(jnp.float32), axis=1
    )
    return (jnp.eye(block_len, dtype=jnp.float32) + neighbour_hits) / (neighbours.shape[1] + 1.0)


def contract_rows(left_mat, right_mat):
    return lax.dot_general(
        left_mat, right_mat, (((0,), (0,)), ((), ())), preferred_element_type=jnp.float32
    )


def _accumulate_kernel(tgt_ref, rec_ref, sum_in, cnt_in, sum_ref, cnt_ref):
    targets = tgt_ref[...]
    n_tgt = sum_ref.shape[1]
    rows = lax.broadcasted_iota(jnp.int32, (n_tgt, targets.shape[1]), 0)
    hot = (rows == targets).astype(jnp.bfloat16)
    dims = (((1,), (1,)), ((), ()))
    sum_ref[...] = sum_in[...] + lax.dot_general(
        rec_ref[...], hot, dims, preferred_element_type=jnp.float32
    )
    ones = jnp.ones((cnt_ref.shape[0], targets.shape[1]), jnp.bfloat16)
    cnt_ref[...] = cnt_in[...] + lax.dot_general(
        ones, hot, dims, preferred_element_type=jnp.float32
    )


def accumulate(targets, rec_t, acc_sum, acc_cnt):
    width, cap = rec_t.shape
    n_tgt = acc_sum.shape[1]
    return pl.pallas_call(
        _accumulate_kernel,
        out_shape=[
            jax.ShapeDtypeStruct(acc_sum.shape, jnp.float32),
            jax.ShapeDtypeStruct(acc_cnt.shape, jnp.float32),
        ],
        input_output_aliases={2: 0, 3: 1},
        cost_estimate=pl.CostEstimate(
            flops=2 * n_tgt * cap * (width + acc_cnt.shape[0]),
            transcendentals=0,
            bytes_accessed=cap * (width * 2 + 4) + 2 * n_tgt * (width + acc_cnt.shape[0]) * 4,
        ),
    )(targets, rec_t, acc_sum, acc_cnt)


def _shift_pairs(n, shift):
    return [(i, (i + shift) % n) for i in range(n)]


def _xor_pairs(n, bit):
    return [(i, i ^ bit) for i in range(n)]


def _is_pow2(n):
    return n & (n - 1) == 0


def reduce_scatter_blocks(x, axis, n, send_dtype, high_first=False):
    if not _is_pow2(n):
        got = lax.all_to_all(x.astype(send_dtype), axis, 0, 0, tiled=True)
        return jnp.sum(got.astype(x.dtype), axis=0)
    k = n.bit_length() - 1
    axis_bits = list(reversed(range(k)))
    order = axis_bits[:] if high_first else list(range(k))
    return _butterfly_reduce(
        x.reshape((2,) * k + x.shape[1:]), axis, n, axis_bits, order, send_dtype
    )


def _butterfly_reduce(cur, axis, n, axis_bits, order, send_dtype):
    me = lax.axis_index(axis)
    axis_bits = list(axis_bits)
    for b in order:
        ax = axis_bits.index(b)
        axis_bits.remove(b)
        mine = (me >> b) & 1
        keep = lax.dynamic_index_in_dim(cur, mine, axis=ax, keepdims=False)
        send = lax.dynamic_index_in_dim(cur, 1 - mine, axis=ax, keepdims=False)
        got = lax.ppermute(send.astype(send_dtype), axis, _xor_pairs(n, 1 << b))
        cur = keep + got.astype(keep.dtype)
    return cur


def reduce_scatter_grid(x, n_dom, n_cols, send_dtype, carried):
    if not (_is_pow2(n_dom) and _is_pow2(n_cols)):
        part = reduce_scatter_blocks(x, "cols", n_cols, send_dtype)
        return reduce_scatter_blocks(part, "dom", n_dom, send_dtype), carried
    kc = n_cols.bit_length() - 1
    kd = n_dom.bit_length() - 1
    axis_bits = [kc - 1 - i for i in range(kc)] + [kc + kd - 1 - i for i in range(kd)]
    order = list(range(min(kc, 1))) + list(range(kc, kc + kd)) + list(range(1, kc))
    cur = x.reshape((2,) * (kc + kd) + x.shape[2:])
    axes = ("dom", "cols")
    n = n_dom * n_cols
    cur = _butterfly_reduce(cur, axes, n, axis_bits, order[:1], send_dtype)
    cur, carried = lax.optimization_barrier((cur, carried))
    rest = [b for b in axis_bits if b != order[0]]
    return _butterfly_reduce(cur, axes, n, rest, order[1:], send_dtype), carried


def all_gather_blocks(x, axis, n):
    if not _is_pow2(n):
        return jax.tree.map(lambda leaf: lax.all_gather(leaf, axis, axis=0, tiled=False), x)
    me = lax.axis_index(axis)
    k = n.bit_length() - 1
    cur = x
    for b in reversed(range(k)):
        mine = (me >> b) & 1
        got = lax.ppermute(cur, axis, _xor_pairs(n, 1 << b))

        def join(held, came, b=b, mine=mine):
            low = jnp.where(mine == 0, held, came)
            high = jnp.where(mine == 0, came, held)
            return jnp.stack([low, high], axis=k - 1 - b)

        cur = jax.tree.map(join, cur, got)
    return jax.tree.map(lambda leaf, orig: leaf.reshape((n,) + orig.shape), cur, x)


def gather_block_list(x, axis, n):
    held = {0: x}
    for b in reversed(range(n.bit_length() - 1)):
        keys = sorted(held)
        came = lax.ppermute(tuple(held[q] for q in keys), axis, _xor_pairs(n, 1 << b))
        for q, blocks in zip(keys, came):
            held[q | (1 << b)] = blocks
    return [held[q] for q in range(n)]


def local(
    features,
    edge_source,
    edge_target,
    neigh_weight,
    self_weight,
    bias_one,
    upper_weight,
    bias_two,
    upper_neighbours,
    out_cotangent,
):
    n_dom = lax.axis_size("dom")
    n_cols = lax.axis_size("cols")
    capacity = edge_source.shape[2]
    width = features.shape[1]
    hidden = upper_weight.shape[1]
    tgt_loc = upper_neighbours.shape[0]
    tgt_dev = tgt_loc * n_cols
    w_rows = neigh_weight.shape[0]
    up_rows = upper_weight.shape[0]

    neigh_full, self_full, full_upper = all_gather_blocks(
        (neigh_weight, self_weight, upper_weight), "cols", n_cols
    )
    full_upper = full_upper.reshape(n_cols * up_rows, hidden)

    me_dom = lax.axis_index("dom")
    me_col = lax.axis_index("cols")
    own_t = features[:tgt_dev].T
    both_full = jnp.concatenate([neigh_full, self_full], axis=1)

    summed_t = jnp.zeros((width, tgt_dev), jnp.float32)
    counts = jnp.zeros((8, tgt_dev), jnp.float32)
    for shift in range(n_dom):
        dest = (me_dom + shift) % n_dom
        src = (me_dom - shift) % n_dom
        slots = lax.dynamic_index_in_dim(edge_source[0], dest, 0, keepdims=False)
        rows_t = features.at[slots].get(mode="promise_in_bounds").T
        if shift:
            rows_t = lax.ppermute(rows_t, "dom", _shift_pairs(n_dom, shift))
        targets = lax.dynamic_index_in_dim(edge_target[0], src, 0, keepdims=True)
        summed_t, counts = accumulate(targets, rows_t, summed_t, counts)
    mean_t = (summed_t / jnp.maximum(counts[:1], 1.0)).astype(jnp.bfloat16)
    both_t = jnp.concatenate([mean_t, own_t], axis=0)

    pre_one = bias_one
    for shift in range(n_cols):
        dest = (me_col + shift) % n_cols
        src = (me_col - shift) % n_cols
        chunk = lax.dynamic_slice_in_dim(both_t, dest * tgt_loc, tgt_loc, axis=1)
        if shift:
            chunk = lax.ppermute(chunk, "cols", _shift_pairs(n_cols, shift))
        weight = lax.dynamic_index_in_dim(both_full, src, 0, keepdims=False)
        pre_one = pre_one + contract_rows(chunk, weight)
    hidden_one = jax.nn.silu(pre_one).astype(jnp.bfloat16)
    mix_matrix = mixing(upper_neighbours, tgt_loc)
    upper_input = jnp.dot(
        mix_matrix, hidden_one.astype(jnp.float32), precision=lax.Precision.HIGHEST
    ).astype(jnp.bfloat16)
    pre_two = jnp.dot(upper_input, full_upper, preferred_element_type=jnp.float32) + bias_two
    hidden_two = jax.nn.silu(pre_two).astype(jnp.bfloat16)
    slope_two = (out_cotangent.astype(jnp.float32) * swish_slope(pre_two)).astype(jnp.bfloat16)

    local_grad = contract_rows(upper_input, slope_two)
    back_mixed = lax.dot_general(
        slope_two, full_upper, (((1,), (1,)), ((), ())), preferred_element_type=jnp.float32
    )
    back_one = jnp.dot(mix_matrix.T, back_mixed, precision=lax.Precision.HIGHEST)
    slope_one = (back_one * swish_slope(pre_one)).astype(jnp.bfloat16)
    dom_rows = up_rows // n_dom
    upper_part, slope_one = reduce_scatter_grid(
        local_grad.reshape(n_cols, n_dom, dom_rows, hidden),
        n_dom,
        n_cols,
        jnp.bfloat16,
        slope_one,
    )
    if _is_pow2(n_cols):
        slope_blocks = gather_block_list((slope_one,), "cols", n_cols)
        stacked = jnp.zeros((2 * width, hidden), jnp.float32)
        for j, (block,) in enumerate(slope_blocks):
            owner_cols = lax.dynamic_slice_in_dim(
                both_t, (me_col ^ j) * tgt_loc, tgt_loc, axis=1
            )
            stacked = stacked + jnp.dot(owner_cols, block, preferred_element_type=jnp.float32)
    else:
        slab_rows = all_gather_blocks(slope_one, "cols", n_cols).reshape(tgt_dev, hidden)
        stacked = jnp.dot(both_t, slab_rows, preferred_element_type=jnp.float32)
    dom_cols = hidden // n_dom
    if _is_pow2(n_dom):
        upper_blocks = gather_block_list((upper_part.astype(jnp.bfloat16),), "dom", n_dom)
        grad_upper = jnp.zeros((n_dom, dom_rows, hidden), jnp.float32)
        for j, (block,) in enumerate(upper_blocks):
            grad_upper = lax.dynamic_update_index_in_dim(
                grad_upper, block.astype(jnp.float32), me_dom ^ j, 0
            )
    else:
        grad_upper = all_gather_blocks(upper_part.astype(jnp.bfloat16), "dom", n_dom)
    grad_upper = grad_upper.reshape(up_rows, hidden).astype(jnp.float32)
    grad_layer = reduce_scatter_blocks(
        jnp.swapaxes(stacked.reshape(2 * width, n_dom, dom_cols), 0, 1),
        "dom",
        n_dom,
        jnp.bfloat16,
    )
    grad_neigh = grad_layer[:w_rows]
    grad_self = grad_layer[w_rows:]
    return (hidden_two, grad_neigh, grad_self, grad_upper)


def solution(mesh):
    in_specs = (
        P(("groups", "dom"), "cols"),
        P(("groups", "dom"), None, None),
        P(("groups", "dom"), None, None),
        P("cols", None),
        P("cols", None),
        P(),
        P("cols", None),
        P(),
        P(("groups", "dom", "cols"), None),
        P(("groups", "dom", "cols"), None),
    )
    out_specs = (
        P(("groups", "dom", "cols"), None),
        P(("groups", "cols"), "dom"),
        P(("groups", "cols"), "dom"),
        P(("groups", "cols"), None),
    )
    return jax.shard_map(local, mesh=mesh, in_specs=in_specs, out_specs=out_specs, check_vma=False)
```

```python
import jax
import jax.numpy as jnp
from jax import lax
from jax.experimental import pallas as pl
from jax.experimental.pallas import tpu as pltpu
from jax.sharding import PartitionSpec as P


def swish_slope(preact):
    gate_val = jax.nn.sigmoid(preact)
    return gate_val * (1.0 + preact * (1.0 - gate_val))


def mixing(neighbours, block_len):
    positions = jnp.arange(block_len, dtype=jnp.int32)
    neighbour_hits = jnp.sum(
        (neighbours[:, :, None] == positions[None, None, :]).astype(jnp.float32), axis=1
    )
    return (jnp.eye(block_len, dtype=jnp.float32) + neighbour_hits) / (neighbours.shape[1] + 1.0)


def contract_rows(left_mat, right_mat):
    return lax.dot_general(
        left_mat, right_mat, (((0,), (0,)), ((), ())), preferred_element_type=jnp.float32
    )


def _accumulate_kernel(tgt_ref, rec_ref, sum_in, cnt_in, sum_ref, cnt_ref):
    targets = tgt_ref[...]
    n_tgt = sum_ref.shape[1]
    rows = lax.broadcasted_iota(jnp.int32, (n_tgt, targets.shape[1]), 0)
    hot = (rows == targets).astype(jnp.bfloat16)
    dims = (((1,), (1,)), ((), ()))
    sum_ref[...] = sum_in[...] + lax.dot_general(
        rec_ref[...], hot, dims, preferred_element_type=jnp.float32
    )
    ones = jnp.ones((cnt_ref.shape[0], targets.shape[1]), jnp.bfloat16)
    cnt_ref[...] = cnt_in[...] + lax.dot_general(
        ones, hot, dims, preferred_element_type=jnp.float32
    )


def accumulate(targets, rec_t, acc_sum, acc_cnt):
    width, cap = rec_t.shape
    n_tgt = acc_sum.shape[1]
    return pl.pallas_call(
        _accumulate_kernel,
        out_shape=[
            jax.ShapeDtypeStruct(acc_sum.shape, jnp.float32),
            jax.ShapeDtypeStruct(acc_cnt.shape, jnp.float32),
        ],
        input_output_aliases={2: 0, 3: 1},
        cost_estimate=pl.CostEstimate(
            flops=2 * n_tgt * cap * (width + acc_cnt.shape[0]),
            transcendentals=0,
            bytes_accessed=cap * (width * 2 + 4) + 2 * n_tgt * (width + acc_cnt.shape[0]) * 4,
        ),
    )(targets, rec_t, acc_sum, acc_cnt)


def _shift_pairs(n, shift):
    return [(i, (i + shift) % n) for i in range(n)]


def _xor_pairs(n, bit):
    return [(i, i ^ bit) for i in range(n)]


def _is_pow2(n):
    return n & (n - 1) == 0


def reduce_scatter_blocks(x, axis, n, send_dtype, high_first=False):
    if not _is_pow2(n):
        got = lax.all_to_all(x.astype(send_dtype), axis, 0, 0, tiled=True)
        return jnp.sum(got.astype(x.dtype), axis=0)
    k = n.bit_length() - 1
    axis_bits = list(reversed(range(k)))
    order = axis_bits[:] if high_first else list(range(k))
    return _butterfly_reduce(
        x.reshape((2,) * k + x.shape[1:]), axis, n, axis_bits, order, send_dtype
    )


def _butterfly_reduce(cur, axis, n, axis_bits, order, send_dtype):
    me = lax.axis_index(axis)
    axis_bits = list(axis_bits)
    for b in order:
        ax = axis_bits.index(b)
        axis_bits.remove(b)
        mine = (me >> b) & 1
        keep = lax.dynamic_index_in_dim(cur, mine, axis=ax, keepdims=False)
        send = lax.dynamic_index_in_dim(cur, 1 - mine, axis=ax, keepdims=False)
        got = lax.ppermute(send.astype(send_dtype), axis, _xor_pairs(n, 1 << b))
        cur = keep + got.astype(keep.dtype)
    return cur


def reduce_scatter_grid(x, n_dom, n_cols, send_dtype, carried):
    if not (_is_pow2(n_dom) and _is_pow2(n_cols)):
        part = reduce_scatter_blocks(x, "cols", n_cols, send_dtype)
        return reduce_scatter_blocks(part, "dom", n_dom, send_dtype), carried
    kc = n_cols.bit_length() - 1
    kd = n_dom.bit_length() - 1
    axis_bits = [kc - 1 - i for i in range(kc)] + [kc + kd - 1 - i for i in range(kd)]
    order = list(range(min(kc, 1))) + list(range(kc, kc + kd)) + list(range(1, kc))
    cur = x.reshape((2,) * (kc + kd) + x.shape[2:])
    axes = ("dom", "cols")
    n = n_dom * n_cols
    cur = _butterfly_reduce(cur, axes, n, axis_bits, order[:1], send_dtype)
    cur, carried = lax.optimization_barrier((cur, carried))
    rest = [b for b in axis_bits if b != order[0]]
    return _butterfly_reduce(cur, axes, n, rest, order[1:], send_dtype), carried


def all_gather_blocks(x, axis, n):
    if not _is_pow2(n):
        return jax.tree.map(lambda leaf: lax.all_gather(leaf, axis, axis=0, tiled=False), x)
    me = lax.axis_index(axis)
    k = n.bit_length() - 1
    cur = x
    for b in reversed(range(k)):
        mine = (me >> b) & 1
        got = lax.ppermute(cur, axis, _xor_pairs(n, 1 << b))

        def join(held, came, b=b, mine=mine):
            low = jnp.where(mine == 0, held, came)
            high = jnp.where(mine == 0, came, held)
            return jnp.stack([low, high], axis=k - 1 - b)

        cur = jax.tree.map(join, cur, got)
    return jax.tree.map(lambda leaf, orig: leaf.reshape((n,) + orig.shape), cur, x)


def gather_block_list(x, axis, n):
    held = {0: x}
    for b in reversed(range(n.bit_length() - 1)):
        keys = sorted(held)
        came = lax.ppermute(tuple(held[q] for q in keys), axis, _xor_pairs(n, 1 << b))
        for q, blocks in zip(keys, came):
            held[q | (1 << b)] = blocks
    return [held[q] for q in range(n)]


def local(
    features,
    edge_source,
    edge_target,
    neigh_weight,
    self_weight,
    bias_one,
    upper_weight,
    bias_two,
    upper_neighbours,
    out_cotangent,
):
    n_dom = lax.axis_size("dom")
    n_cols = lax.axis_size("cols")
    capacity = edge_source.shape[2]
    width = features.shape[1]
    hidden = upper_weight.shape[1]
    tgt_loc = upper_neighbours.shape[0]
    tgt_dev = tgt_loc * n_cols
    w_rows = neigh_weight.shape[0]
    up_rows = upper_weight.shape[0]

    me_col = lax.axis_index("cols")
    if _is_pow2(n_cols):
        layer_weights = gather_block_list((neigh_weight, self_weight), "cols", n_cols)
        full_upper = all_gather_blocks(upper_weight, "cols", n_cols)
        partners = [(me_col ^ j, _xor_pairs(n_cols, j)) for j in range(n_cols)]
    else:
        neigh_full, self_full, full_upper = all_gather_blocks(
            (neigh_weight, self_weight, upper_weight), "cols", n_cols
        )
        partners = [((me_col + j) % n_cols, _shift_pairs(n_cols, j)) for j in range(n_cols)]
        layer_weights = [
            tuple(
                lax.dynamic_index_in_dim(full, (me_col - j) % n_cols, 0, keepdims=False)
                for full in (neigh_full, self_full)
            )
            for j in range(n_cols)
        ]
    full_upper = full_upper.reshape(n_cols * up_rows, hidden)

    me_dom = lax.axis_index("dom")
    me_col = lax.axis_index("cols")
    own_t = features[:tgt_dev].T

    summed_t = jnp.zeros((width, tgt_dev), jnp.float32)
    counts = jnp.zeros((8, tgt_dev), jnp.float32)
    for shift in range(n_dom):
        dest = (me_dom + shift) % n_dom
        src = (me_dom - shift) % n_dom
        slots = lax.dynamic_index_in_dim(edge_source[0], dest, 0, keepdims=False)
        rows_t = features.at[slots].get(mode="promise_in_bounds").T
        if shift:
            rows_t = lax.ppermute(rows_t, "dom", _shift_pairs(n_dom, shift))
        targets = lax.dynamic_index_in_dim(edge_target[0], src, 0, keepdims=True)
        summed_t, counts = accumulate(targets, rows_t, summed_t, counts)
    mean_t = (summed_t / jnp.maximum(counts[:1], 1.0)).astype(jnp.bfloat16)
    both_t = jnp.concatenate([mean_t, own_t], axis=0)

    pre_one = bias_one
    for j, (dest, pairs) in enumerate(partners):
        chunk = lax.dynamic_slice_in_dim(both_t, dest * tgt_loc, tgt_loc, axis=1)
        if j:
            chunk = lax.ppermute(chunk, "cols", pairs)
        neigh_j, self_j = layer_weights[j]
        pre_one = pre_one + contract_rows(chunk[:width], neigh_j)
        pre_one = pre_one + contract_rows(chunk[width:], self_j)
    hidden_one = jax.nn.silu(pre_one).astype(jnp.bfloat16)
    mix_matrix = mixing(upper_neighbours, tgt_loc)
    upper_input = jnp.dot(
        mix_matrix, hidden_one.astype(jnp.float32), precision=lax.Precision.HIGHEST
    ).astype(jnp.bfloat16)
    pre_two = jnp.dot(upper_input, full_upper, preferred_element_type=jnp.float32) + bias_two
    hidden_two = jax.nn.silu(pre_two).astype(jnp.bfloat16)
    slope_two = (out_cotangent.astype(jnp.float32) * swish_slope(pre_two)).astype(jnp.bfloat16)

    local_grad = contract_rows(upper_input, slope_two)
    back_mixed = lax.dot_general(
        slope_two, full_upper, (((1,), (1,)), ((), ())), preferred_element_type=jnp.float32
    )
    back_one = jnp.dot(mix_matrix.T, back_mixed, precision=lax.Precision.HIGHEST)
    slope_one = (back_one * swish_slope(pre_one)).astype(jnp.bfloat16)
    dom_rows = up_rows // n_dom
    upper_part, slope_one = reduce_scatter_grid(
        local_grad.reshape(n_cols, n_dom, dom_rows, hidden),
        n_dom,
        n_cols,
        jnp.bfloat16,
        slope_one,
    )
    if _is_pow2(n_cols):
        slope_blocks = gather_block_list((slope_one,), "cols", n_cols)
        stacked = jnp.zeros((2 * width, hidden), jnp.float32)
        for j, (block,) in enumerate(slope_blocks):
            owner_cols = lax.dynamic_slice_in_dim(
                both_t, (me_col ^ j) * tgt_loc, tgt_loc, axis=1
            )
            stacked = stacked + jnp.dot(owner_cols, block, preferred_element_type=jnp.float32)
    else:
        slab_rows = all_gather_blocks(slope_one, "cols", n_cols).reshape(tgt_dev, hidden)
        stacked = jnp.dot(both_t, slab_rows, preferred_element_type=jnp.float32)
    dom_cols = hidden // n_dom
    grad_upper = all_gather_blocks(upper_part.astype(jnp.bfloat16), "dom", n_dom)
    grad_upper = grad_upper.reshape(up_rows, hidden).astype(jnp.float32)
    grad_layer = reduce_scatter_blocks(
        jnp.swapaxes(stacked.reshape(2 * width, n_dom, dom_cols), 0, 1),
        "dom",
        n_dom,
        jnp.bfloat16,
    )
    grad_neigh = grad_layer[:w_rows]
    grad_self = grad_layer[w_rows:]
    return (hidden_two, grad_neigh, grad_self, grad_upper)


def solution(mesh):
    in_specs = (
        P(("groups", "dom"), "cols"),
        P(("groups", "dom"), None, None),
        P(("groups", "dom"), None, None),
        P("cols", None),
        P("cols", None),
        P(),
        P("cols", None),
        P(),
        P(("groups", "dom", "cols"), None),
        P(("groups", "dom", "cols"), None),
    )
    out_specs = (
        P(("groups", "dom", "cols"), None),
        P(("groups", "cols"), "dom"),
        P(("groups", "cols"), "dom"),
        P(("groups", "cols"), None),
    )
    return jax.shard_map(local, mesh=mesh, in_specs=in_specs, out_specs=out_specs, check_vma=False)
```

```python
import jax
import jax.numpy as jnp
from jax import lax
from jax.experimental import pallas as pl
from jax.experimental.pallas import tpu as pltpu
from jax.sharding import PartitionSpec as P


def swish_slope(preact):
    gate_val = jax.nn.sigmoid(preact)
    return gate_val * (1.0 + preact * (1.0 - gate_val))


def mixing(neighbours, block_len):
    positions = jnp.arange(block_len, dtype=jnp.int32)
    neighbour_hits = jnp.sum(
        (neighbours[:, :, None] == positions[None, None, :]).astype(jnp.float32), axis=1
    )
    return (jnp.eye(block_len, dtype=jnp.float32) + neighbour_hits) / (neighbours.shape[1] + 1.0)


def contract_rows(left_mat, right_mat):
    return lax.dot_general(
        left_mat, right_mat, (((0,), (0,)), ((), ())), preferred_element_type=jnp.float32
    )


def _accumulate_kernel(tgt_ref, rec_ref, sum_in, cnt_in, sum_ref, cnt_ref):
    targets = tgt_ref[...]
    n_tgt = sum_ref.shape[1]
    rows = lax.broadcasted_iota(jnp.int32, (n_tgt, targets.shape[1]), 0)
    hot = (rows == targets).astype(jnp.bfloat16)
    dims = (((1,), (1,)), ((), ()))
    sum_ref[...] = sum_in[...] + lax.dot_general(
        rec_ref[...], hot, dims, preferred_element_type=jnp.float32
    )
    ones = jnp.ones((cnt_ref.shape[0], targets.shape[1]), jnp.bfloat16)
    cnt_ref[...] = cnt_in[...] + lax.dot_general(
        ones, hot, dims, preferred_element_type=jnp.float32
    )


def accumulate(targets, rec_t, acc_sum, acc_cnt):
    width, cap = rec_t.shape
    n_tgt = acc_sum.shape[1]
    return pl.pallas_call(
        _accumulate_kernel,
        out_shape=[
            jax.ShapeDtypeStruct(acc_sum.shape, jnp.float32),
            jax.ShapeDtypeStruct(acc_cnt.shape, jnp.float32),
        ],
        input_output_aliases={2: 0, 3: 1},
        cost_estimate=pl.CostEstimate(
            flops=2 * n_tgt * cap * (width + acc_cnt.shape[0]),
            transcendentals=0,
            bytes_accessed=cap * (width * 2 + 4) + 2 * n_tgt * (width + acc_cnt.shape[0]) * 4,
        ),
    )(targets, rec_t, acc_sum, acc_cnt)


def _shift_pairs(n, shift):
    return [(i, (i + shift) % n) for i in range(n)]


def _xor_pairs(n, bit):
    return [(i, i ^ bit) for i in range(n)]


def _is_pow2(n):
    return n & (n - 1) == 0


def reduce_scatter_blocks(x, axis, n, send_dtype, high_first=False):
    if not _is_pow2(n):
        got = lax.all_to_all(x.astype(send_dtype), axis, 0, 0, tiled=True)
        return jnp.sum(got.astype(x.dtype), axis=0)
    k = n.bit_length() - 1
    axis_bits = list(reversed(range(k)))
    order = axis_bits[:] if high_first else list(range(k))
    return _butterfly_reduce(
        x.reshape((2,) * k + x.shape[1:]), axis, n, axis_bits, order, send_dtype
    )


def _butterfly_reduce(cur, axis, n, axis_bits, order, send_dtype):
    me = lax.axis_index(axis)
    axis_bits = list(axis_bits)
    for b in order:
        ax = axis_bits.index(b)
        axis_bits.remove(b)
        mine = (me >> b) & 1
        keep = lax.dynamic_index_in_dim(cur, mine, axis=ax, keepdims=False)
        send = lax.dynamic_index_in_dim(cur, 1 - mine, axis=ax, keepdims=False)
        got = lax.ppermute(send.astype(send_dtype), axis, _xor_pairs(n, 1 << b))
        cur = keep + got.astype(keep.dtype)
    return cur


def reduce_scatter_grid(x, n_dom, n_cols, send_dtype, carried):
    if not (_is_pow2(n_dom) and _is_pow2(n_cols)):
        part = reduce_scatter_blocks(x, "cols", n_cols, send_dtype)
        return reduce_scatter_blocks(part, "dom", n_dom, send_dtype), carried
    kc = n_cols.bit_length() - 1
    kd = n_dom.bit_length() - 1
    axis_bits = [kc - 1 - i for i in range(kc)] + [kc + kd - 1 - i for i in range(kd)]
    order = list(range(min(kc, 1))) + list(range(kc, kc + kd)) + list(range(1, kc))
    cur = x.reshape((2,) * (kc + kd) + x.shape[2:])
    axes = ("dom", "cols")
    n = n_dom * n_cols
    cur = _butterfly_reduce(cur, axes, n, axis_bits, order[:1], send_dtype)
    cur, carried = lax.optimization_barrier((cur, carried))
    rest = [b for b in axis_bits if b != order[0]]
    return _butterfly_reduce(cur, axes, n, rest, order[1:], send_dtype), carried


def all_gather_blocks(x, axis, n):
    if not _is_pow2(n):
        return jax.tree.map(lambda leaf: lax.all_gather(leaf, axis, axis=0, tiled=False), x)
    me = lax.axis_index(axis)
    k = n.bit_length() - 1
    cur = x
    for b in reversed(range(k)):
        mine = (me >> b) & 1
        got = lax.ppermute(cur, axis, _xor_pairs(n, 1 << b))

        def join(held, came, b=b, mine=mine):
            low = jnp.where(mine == 0, held, came)
            high = jnp.where(mine == 0, came, held)
            return jnp.stack([low, high], axis=k - 1 - b)

        cur = jax.tree.map(join, cur, got)
    return jax.tree.map(lambda leaf, orig: leaf.reshape((n,) + orig.shape), cur, x)


def gather_block_list(x, axis, n):
    held = {0: x}
    for b in reversed(range(n.bit_length() - 1)):
        keys = sorted(held)
        came = lax.ppermute(tuple(held[q] for q in keys), axis, _xor_pairs(n, 1 << b))
        for q, blocks in zip(keys, came):
            held[q | (1 << b)] = blocks
    return [held[q] for q in range(n)]


def local(
    features,
    edge_source,
    edge_target,
    neigh_weight,
    self_weight,
    bias_one,
    upper_weight,
    bias_two,
    upper_neighbours,
    out_cotangent,
):
    n_dom = lax.axis_size("dom")
    n_cols = lax.axis_size("cols")
    capacity = edge_source.shape[2]
    width = features.shape[1]
    hidden = upper_weight.shape[1]
    tgt_loc = upper_neighbours.shape[0]
    tgt_dev = tgt_loc * n_cols
    w_rows = neigh_weight.shape[0]
    up_rows = upper_weight.shape[0]

    neigh_full, self_full, full_upper = all_gather_blocks(
        (neigh_weight, self_weight, upper_weight), "cols", n_cols
    )
    full_upper = full_upper.reshape(n_cols * up_rows, hidden)

    me_dom = lax.axis_index("dom")
    me_col = lax.axis_index("cols")
    own_t = features[:tgt_dev].T
    both_full = jnp.concatenate([neigh_full, self_full], axis=1)

    summed_t = jnp.zeros((width, tgt_dev), jnp.float32)
    counts = jnp.zeros((8, tgt_dev), jnp.float32)
    for shift in range(n_dom):
        dest = (me_dom + shift) % n_dom
        src = (me_dom - shift) % n_dom
        slots = lax.dynamic_index_in_dim(edge_source[0], dest, 0, keepdims=False)
        rows_t = features.at[slots].get(mode="promise_in_bounds").T
        if shift:
            rows_t = lax.ppermute(rows_t, "dom", _shift_pairs(n_dom, shift))
        targets = lax.dynamic_index_in_dim(edge_target[0], src, 0, keepdims=True)
        summed_t, counts = accumulate(targets, rows_t, summed_t, counts)
    mean_t = (summed_t / jnp.maximum(counts[:1], 1.0)).astype(jnp.bfloat16)
    both_t = jnp.concatenate([mean_t, own_t], axis=0)

    pre_one = bias_one
    for shift in range(n_cols):
        dest = (me_col + shift) % n_cols
        src = (me_col - shift) % n_cols
        chunk = lax.dynamic_slice_in_dim(both_t, dest * tgt_loc, tgt_loc, axis=1)
        if shift:
            chunk = lax.ppermute(chunk, "cols", _shift_pairs(n_cols, shift))
        weight = lax.dynamic_index_in_dim(both_full, src, 0, keepdims=False)
        pre_one = pre_one + contract_rows(chunk, weight)
    hidden_one = jax.nn.silu(pre_one).astype(jnp.bfloat16)
    mix_matrix = mixing(upper_neighbours, tgt_loc)
    upper_input = jnp.dot(
        mix_matrix, hidden_one.astype(jnp.float32), precision=lax.Precision.HIGHEST
    ).astype(jnp.bfloat16)
    pre_two = jnp.dot(upper_input, full_upper, preferred_element_type=jnp.float32) + bias_two
    hidden_two = jax.nn.silu(pre_two).astype(jnp.bfloat16)
    slope_two = (out_cotangent.astype(jnp.float32) * swish_slope(pre_two)).astype(jnp.bfloat16)

    local_grad = contract_rows(upper_input, slope_two)
    back_mixed = lax.dot_general(
        slope_two, full_upper, (((1,), (1,)), ((), ())), preferred_element_type=jnp.float32
    )
    back_one = jnp.dot(mix_matrix.T, back_mixed, precision=lax.Precision.HIGHEST)
    slope_one = (back_one * swish_slope(pre_one)).astype(jnp.bfloat16)
    dom_rows = up_rows // n_dom
    upper_part, slope_one = reduce_scatter_grid(
        local_grad.reshape(n_cols, n_dom, dom_rows, hidden),
        n_dom,
        n_cols,
        jnp.bfloat16,
        slope_one,
    )
    if _is_pow2(n_cols):
        slope_blocks = gather_block_list((slope_one,), "cols", n_cols)
        stacked = jnp.zeros((2 * width, hidden), jnp.float32)
        for j, (block,) in enumerate(slope_blocks):
            owner_cols = lax.dynamic_slice_in_dim(
                both_t, (me_col ^ j) * tgt_loc, tgt_loc, axis=1
            )
            stacked = stacked + jnp.dot(owner_cols, block, preferred_element_type=jnp.float32)
    else:
        slab_rows = all_gather_blocks(slope_one, "cols", n_cols).reshape(tgt_dev, hidden)
        stacked = jnp.dot(both_t, slab_rows, preferred_element_type=jnp.float32)
    dom_cols = hidden // n_dom
    grad_upper = all_gather_blocks(upper_part.astype(jnp.bfloat16), "dom", n_dom)
    grad_upper = grad_upper.reshape(up_rows, hidden).astype(jnp.float32)
    grad_layer = reduce_scatter_blocks(
        jnp.swapaxes(stacked.reshape(2 * width, n_dom, dom_cols), 0, 1),
        "dom",
        n_dom,
        jnp.bfloat16,
        high_first=True,
    )
    grad_neigh = grad_layer[:w_rows]
    grad_self = grad_layer[w_rows:]
    return (hidden_two, grad_neigh, grad_self, grad_upper)


def solution(mesh):
    in_specs = (
        P(("groups", "dom"), "cols"),
        P(("groups", "dom"), None, None),
        P(("groups", "dom"), None, None),
        P("cols", None),
        P("cols", None),
        P(),
        P("cols", None),
        P(),
        P(("groups", "dom", "cols"), None),
        P(("groups", "dom", "cols"), None),
    )
    out_specs = (
        P(("groups", "dom", "cols"), None),
        P(("groups", "cols"), "dom"),
        P(("groups", "cols"), "dom"),
        P(("groups", "cols"), None),
    )
    return jax.shard_map(local, mesh=mesh, in_specs=in_specs, out_specs=out_specs, check_vma=False)
```

```python
import jax
import jax.numpy as jnp
from jax import lax
from jax.experimental import pallas as pl
from jax.experimental.pallas import tpu as pltpu
from jax.sharding import PartitionSpec as P


def swish_slope(preact):
    gate_val = jax.nn.sigmoid(preact)
    return gate_val * (1.0 + preact * (1.0 - gate_val))


def mixing(neighbours, block_len):
    positions = jnp.arange(block_len, dtype=jnp.int32)
    neighbour_hits = jnp.sum(
        (neighbours[:, :, None] == positions[None, None, :]).astype(jnp.float32), axis=1
    )
    return (jnp.eye(block_len, dtype=jnp.float32) + neighbour_hits) / (neighbours.shape[1] + 1.0)


def contract_rows(left_mat, right_mat):
    return lax.dot_general(
        left_mat, right_mat, (((0,), (0,)), ((), ())), preferred_element_type=jnp.float32
    )


def _accumulate_kernel(tgt_ref, rec_ref, sum_in, cnt_in, sum_ref, cnt_ref):
    targets = tgt_ref[...]
    n_tgt = sum_ref.shape[1]
    width = sum_ref.shape[0]
    rows = lax.broadcasted_iota(jnp.int32, (n_tgt, targets.shape[1]), 0)
    hot = (rows == targets).astype(jnp.bfloat16)
    ones = jnp.ones((cnt_ref.shape[0], targets.shape[1]), jnp.bfloat16)
    extended = jnp.concatenate([rec_ref[...], ones], axis=0)
    dims = (((1,), (1,)), ((), ()))
    both = lax.dot_general(extended, hot, dims, preferred_element_type=jnp.float32)
    sum_ref[...] = sum_in[...] + both[:width]
    cnt_ref[...] = cnt_in[...] + both[width:]


def accumulate(targets, rec_t, acc_sum, acc_cnt):
    width, cap = rec_t.shape
    n_tgt = acc_sum.shape[1]
    return pl.pallas_call(
        _accumulate_kernel,
        out_shape=[
            jax.ShapeDtypeStruct(acc_sum.shape, jnp.float32),
            jax.ShapeDtypeStruct(acc_cnt.shape, jnp.float32),
        ],
        input_output_aliases={2: 0, 3: 1},
        cost_estimate=pl.CostEstimate(
            flops=2 * n_tgt * cap * (width + acc_cnt.shape[0]),
            transcendentals=0,
            bytes_accessed=cap * (width * 2 + 4) + 2 * n_tgt * (width + acc_cnt.shape[0]) * 4,
        ),
    )(targets, rec_t, acc_sum, acc_cnt)


def _shift_pairs(n, shift):
    return [(i, (i + shift) % n) for i in range(n)]


def _xor_pairs(n, bit):
    return [(i, i ^ bit) for i in range(n)]


def _is_pow2(n):
    return n & (n - 1) == 0


def reduce_scatter_blocks(x, axis, n, send_dtype, high_first=False):
    if not _is_pow2(n):
        got = lax.all_to_all(x.astype(send_dtype), axis, 0, 0, tiled=True)
        return jnp.sum(got.astype(x.dtype), axis=0)
    k = n.bit_length() - 1
    axis_bits = list(reversed(range(k)))
    order = axis_bits[:] if high_first else list(range(k))
    return _butterfly_reduce(
        x.reshape((2,) * k + x.shape[1:]), axis, n, axis_bits, order, send_dtype
    )


def _butterfly_reduce(cur, axis, n, axis_bits, order, send_dtype):
    me = lax.axis_index(axis)
    axis_bits = list(axis_bits)
    for b in order:
        ax = axis_bits.index(b)
        axis_bits.remove(b)
        mine = (me >> b) & 1
        keep = lax.dynamic_index_in_dim(cur, mine, axis=ax, keepdims=False)
        send = lax.dynamic_index_in_dim(cur, 1 - mine, axis=ax, keepdims=False)
        got = lax.ppermute(send.astype(send_dtype), axis, _xor_pairs(n, 1 << b))
        cur = keep + got.astype(keep.dtype)
    return cur


def reduce_scatter_grid(x, n_dom, n_cols, send_dtype, carried):
    if not (_is_pow2(n_dom) and _is_pow2(n_cols)):
        part = reduce_scatter_blocks(x, "cols", n_cols, send_dtype)
        return reduce_scatter_blocks(part, "dom", n_dom, send_dtype), carried
    kc = n_cols.bit_length() - 1
    kd = n_dom.bit_length() - 1
    axis_bits = [kc - 1 - i for i in range(kc)] + [kc + kd - 1 - i for i in range(kd)]
    order = list(range(min(kc, 1))) + list(range(kc, kc + kd)) + list(range(1, kc))
    cur = x.reshape((2,) * (kc + kd) + x.shape[2:])
    axes = ("dom", "cols")
    n = n_dom * n_cols
    cur = _butterfly_reduce(cur, axes, n, axis_bits, order[:1], send_dtype)
    cur, carried = lax.optimization_barrier((cur, carried))
    rest = [b for b in axis_bits if b != order[0]]
    return _butterfly_reduce(cur, axes, n, rest, order[1:], send_dtype), carried


def all_gather_blocks(x, axis, n):
    if not _is_pow2(n):
        return jax.tree.map(lambda leaf: lax.all_gather(leaf, axis, axis=0, tiled=False), x)
    me = lax.axis_index(axis)
    k = n.bit_length() - 1
    cur = x
    for b in reversed(range(k)):
        mine = (me >> b) & 1
        got = lax.ppermute(cur, axis, _xor_pairs(n, 1 << b))

        def join(held, came, b=b, mine=mine):
            low = jnp.where(mine == 0, held, came)
            high = jnp.where(mine == 0, came, held)
            return jnp.stack([low, high], axis=k - 1 - b)

        cur = jax.tree.map(join, cur, got)
    return jax.tree.map(lambda leaf, orig: leaf.reshape((n,) + orig.shape), cur, x)


def gather_block_list(x, axis, n):
    held = {0: x}
    for b in reversed(range(n.bit_length() - 1)):
        keys = sorted(held)
        came = lax.ppermute(tuple(held[q] for q in keys), axis, _xor_pairs(n, 1 << b))
        for q, blocks in zip(keys, came):
            held[q | (1 << b)] = blocks
    return [held[q] for q in range(n)]


def local(
    features,
    edge_source,
    edge_target,
    neigh_weight,
    self_weight,
    bias_one,
    upper_weight,
    bias_two,
    upper_neighbours,
    out_cotangent,
):
    n_dom = lax.axis_size("dom")
    n_cols = lax.axis_size("cols")
    capacity = edge_source.shape[2]
    width = features.shape[1]
    hidden = upper_weight.shape[1]
    tgt_loc = upper_neighbours.shape[0]
    tgt_dev = tgt_loc * n_cols
    w_rows = neigh_weight.shape[0]
    up_rows = upper_weight.shape[0]

    neigh_full, self_full, full_upper = all_gather_blocks(
        (neigh_weight, self_weight, upper_weight), "cols", n_cols
    )
    full_upper = full_upper.reshape(n_cols * up_rows, hidden)

    me_dom = lax.axis_index("dom")
    me_col = lax.axis_index("cols")
    own_t = features[:tgt_dev].T
    both_full = jnp.concatenate([neigh_full, self_full], axis=1)

    summed_t = jnp.zeros((width, tgt_dev), jnp.float32)
    counts = jnp.zeros((8, tgt_dev), jnp.float32)
    for shift in range(n_dom):
        dest = (me_dom + shift) % n_dom
        src = (me_dom - shift) % n_dom
        slots = lax.dynamic_index_in_dim(edge_source[0], dest, 0, keepdims=False)
        rows_t = features.at[slots].get(mode="promise_in_bounds").T
        if shift:
            rows_t = lax.ppermute(rows_t, "dom", _shift_pairs(n_dom, shift))
        targets = lax.dynamic_index_in_dim(edge_target[0], src, 0, keepdims=True)
        summed_t, counts = accumulate(targets, rows_t, summed_t, counts)
    mean_t = (summed_t / jnp.maximum(counts[:1], 1.0)).astype(jnp.bfloat16)
    both_t = jnp.concatenate([mean_t, own_t], axis=0)

    pre_one = bias_one
    for shift in range(n_cols):
        dest = (me_col + shift) % n_cols
        src = (me_col - shift) % n_cols
        chunk = lax.dynamic_slice_in_dim(both_t, dest * tgt_loc, tgt_loc, axis=1)
        if shift:
            chunk = lax.ppermute(chunk, "cols", _shift_pairs(n_cols, shift))
        weight = lax.dynamic_index_in_dim(both_full, src, 0, keepdims=False)
        pre_one = pre_one + contract_rows(chunk, weight)
    hidden_one = jax.nn.silu(pre_one).astype(jnp.bfloat16)
    mix_matrix = mixing(upper_neighbours, tgt_loc)
    upper_input = jnp.dot(
        mix_matrix, hidden_one.astype(jnp.float32), precision=lax.Precision.HIGHEST
    ).astype(jnp.bfloat16)
    pre_two = jnp.dot(upper_input, full_upper, preferred_element_type=jnp.float32) + bias_two
    hidden_two = jax.nn.silu(pre_two).astype(jnp.bfloat16)
    slope_two = (out_cotangent.astype(jnp.float32) * swish_slope(pre_two)).astype(jnp.bfloat16)

    local_grad = contract_rows(upper_input, slope_two)
    back_mixed = lax.dot_general(
        slope_two, full_upper, (((1,), (1,)), ((), ())), preferred_element_type=jnp.float32
    )
    back_one = jnp.dot(mix_matrix.T, back_mixed, precision=lax.Precision.HIGHEST)
    slope_one = (back_one * swish_slope(pre_one)).astype(jnp.bfloat16)
    dom_rows = up_rows // n_dom
    upper_part, slope_one = reduce_scatter_grid(
        local_grad.reshape(n_cols, n_dom, dom_rows, hidden),
        n_dom,
        n_cols,
        jnp.bfloat16,
        slope_one,
    )
    if _is_pow2(n_cols):
        slope_blocks = gather_block_list((slope_one,), "cols", n_cols)
        stacked = jnp.zeros((2 * width, hidden), jnp.float32)
        for j, (block,) in enumerate(slope_blocks):
            owner_cols = lax.dynamic_slice_in_dim(
                both_t, (me_col ^ j) * tgt_loc, tgt_loc, axis=1
            )
            stacked = stacked + jnp.dot(owner_cols, block, preferred_element_type=jnp.float32)
    else:
        slab_rows = all_gather_blocks(slope_one, "cols", n_cols).reshape(tgt_dev, hidden)
        stacked = jnp.dot(both_t, slab_rows, preferred_element_type=jnp.float32)
    dom_cols = hidden // n_dom
    grad_upper = all_gather_blocks(upper_part.astype(jnp.bfloat16), "dom", n_dom)
    grad_upper = grad_upper.reshape(up_rows, hidden).astype(jnp.float32)
    grad_layer = reduce_scatter_blocks(
        jnp.swapaxes(stacked.reshape(2 * width, n_dom, dom_cols), 0, 1),
        "dom",
        n_dom,
        jnp.bfloat16,
    )
    grad_neigh = grad_layer[:w_rows]
    grad_self = grad_layer[w_rows:]
    return (hidden_two, grad_neigh, grad_self, grad_upper)


def solution(mesh):
    in_specs = (
        P(("groups", "dom"), "cols"),
        P(("groups", "dom"), None, None),
        P(("groups", "dom"), None, None),
        P("cols", None),
        P("cols", None),
        P(),
        P("cols", None),
        P(),
        P(("groups", "dom", "cols"), None),
        P(("groups", "dom", "cols"), None),
    )
    out_specs = (
        P(("groups", "dom", "cols"), None),
        P(("groups", "cols"), "dom"),
        P(("groups", "cols"), "dom"),
        P(("groups", "cols"), None),
    )
    return jax.shard_map(local, mesh=mesh, in_specs=in_specs, out_specs=out_specs, check_vma=False)
```
